128 devices in a mesh: section: 8 (over z, core), ctx: 16 (over y, x).
Axes of the slice: x: 4, y: 4, z: 4, core: 2. Of those that a mesh axis runs over, the one named last changes fastest.
Arguments:
- previous: bfloat16 [8, 2048, 8192], P('section', 'ctx'), may hold values from -6 to 6
- fresh: bfloat16 [2048, 8192], P('ctx'), may hold values from -6 to 6
- dt_raw: float32 [8, 2048, 128], P('section', 'ctx'), may hold values from -3 to 4100
- dt_bias: float32 [8, 128], P('section'), may hold values from -0.5 to 0.5
- a_log: float32 [8, 128], P('section'), may hold values from -12 to -2
- b_in: bfloat16 [8, 2048, 1024], P('section', 'ctx'), may hold values from -0.5 to 0.5
- c_in: bfloat16 [8, 2048, 1024], P('section', 'ctx'), may hold values from -6 to 6
- skip_d: float32 [8, 128], P('section'), may hold values from 0.5 to 1.5
- norm_gain: bfloat16 [8, 8192], P('section'), may hold values from 0.099609375 to 1.8984375
- queries: bfloat16 [8, 2048, 8192], P('section', 'ctx'), may hold values from -12 to 12
- keys: bfloat16 [8, 2048, 1024], P('section', 'ctx'), may hold values from -12 to 12
- values: bfloat16 [8, 2048, 1024], P('section', 'ctx'), may hold values from -6 to 6
- doc_ids: int32 [8, 2048], P('section'), may hold values from 0 to 7, never falling along the last dimension, each value on 1 to 512 neighbouring positions
Outputs:
- section_out: bfloat16 [8, 2048, 8192], P('section', 'ctx')
The draws below stay inside these ranges and needn't reach their ends.
Inputs may be any that keep to these rules, and one draw needn't show every extreme that they name: `doc_ids`: each row never falls; every document covers 1 to 512 positions and one covers exactly 512.
All inputs are finite; a program needn't handle non-finite values.
Results may differ from the reference program's by a relative error of at most 0.0085.
Values may be sent and summed in bfloat16 or wider, within the bound.
No kernel may reach another device: no remote copies, remote signals or barrier semaphores. Data moves between devices by JAX's collectives and lax.ppermute only.
A program may use at most 256 MiB of HBM per device.

```python
import math
import jax
import jax.numpy as jnp
import numpy as np
from jax import lax

HEAD_A = 128
Q_HEADS = 64
KV_HEADS = 8
D = 8192
HEADS_M = 128
STATE = 128
GROUPS = 8
TOK_DEV = 128
DOCS = 8
PACKED_LENGTH = 2048
MOST = 512
N_SECTION = 8
N_CTX = 16


def draw_a_log(key, part):
    pick_key, fast_key, slow_key = jax.random.split(jax.random.fold_in(key, 3), 3)
    full_shape = (N_SECTION, HEADS_M)
    share = 0.5
    picked = jax.random.uniform(pick_key, full_shape) < share
    fast_rate = jax.random.uniform(fast_key, full_shape, minval=0.02, maxval=0.05)
    slow_rate = jax.random.uniform(slow_key, full_shape, minval=0.1, maxval=0.3) / PACKED_LENGTH
    return jnp.log(jnp.where(picked, fast_rate, slow_rate)).astype(jnp.float32)


def draw_dt_raw(key, part):
    baseline_key, shift_key, cluster_key = jax.random.split(jax.random.fold_in(key, 4), 3)
    full_shape = (N_SECTION, PACKED_LENGTH, HEADS_M)
    baseline_sample = jnp.clip(0.5 * jax.random.normal(baseline_key, full_shape), -1.5, 1.5)
    position_shift = jax.random.uniform(shift_key, (N_SECTION, N_CTX, 1, HEADS_M), minval=-0.8, maxval=1.2)
    position_shift = jnp.broadcast_to(position_shift, (N_SECTION, N_CTX, TOK_DEV, HEADS_M)).reshape(full_shape)
    marked_rows = jax.random.randint(cluster_key, (N_SECTION, 3), 0, PACKED_LENGTH)
    token_positions = jnp.arange(PACKED_LENGTH)
    cluster_mask = jnp.any(token_positions[None, :, None] == marked_rows[:, None, :], axis=2).astype(jnp.float32)
    return (baseline_sample + position_shift + 2.0 * PACKED_LENGTH * cluster_mask[:, :, None]).astype(jnp.float32)


def draw_queries(key, part):
    full_shape = (N_SECTION, PACKED_LENGTH, D)
    baseline_key = jax.random.fold_in(key, 1)
    baseline_sample = jnp.clip(jax.random.normal(baseline_key, full_shape), -4.0, 4.0)
    return baseline_sample.astype(jnp.bfloat16)


def draw_keys(key, part):
    full_shape = (N_SECTION, PACKED_LENGTH, KV_HEADS * HEAD_A)
    baseline_key = jax.random.fold_in(key, 2)
    baseline_sample = jnp.clip(jax.random.normal(baseline_key, full_shape), -4.0, 4.0)
    return baseline_sample.astype(jnp.bfloat16)


def shard_levels(stream_key, shape, shards, low, high):
    gain = 1.0
    for axis_at, blocks in shards:
        draws = jax.random.uniform(jax.random.fold_in(jax.random.fold_in(stream_key, 6), axis_at), (blocks,), jnp.float32, low / len(shards), high / len(shards))
        gain = gain * jnp.repeat(jnp.exp(draws), shape[axis_at] // blocks).reshape((-1,) + (1,) * (len(shape) - 1 - axis_at))
    return gain


def split_up(count, total, most, lean):
    weights = [(1 << 20) // math.isqrt(grade ** lean) + 1 for grade in range(2, count + 1)]
    surplus, counts = total - most - (count - 1), [1] * (count - 1)
    while surplus > 0:
        free = [i for i in range(count - 1) if counts[i] < most]
        pool, remaining = sum([weights[i] for i in free]), surplus
        for i in free:
            addition = min(most - counts[i], max(1, remaining * weights[i] // pool), surplus)
            counts[i] = counts[i] + addition
            surplus = surplus - addition
    return np.array([most] + counts)


def uneven_parts(rng, number_of, total, most, lean):
    if number_of == 2:
        one = jax.random.randint(rng, (), max(1, total - most), min(most, total - 1) + 1)
        return jnp.stack([one, total - one])
    sizes = jnp.asarray(split_up(number_of, total, most, lean), jnp.int32)
    twos = (number_of - 1) // 2
    giver, taker = sizes[1:1 + 2 * twos:2], sizes[2:2 + 2 * twos:2]
    slack = jnp.minimum(giver - 1, most - taker)
    shifted = jax.random.randint(jax.random.fold_in(rng, 1), (twos,), 0, 1 << 20) % (slack + 1)
    sizes = sizes.at[1:1 + 2 * twos:2].set(giver - shifted).at[2:2 + 2 * twos:2].set(taker + shifted)
    return sizes[jax.random.permutation(jax.random.fold_in(rng, 2), number_of)]


def scatter_about(stream_key, extent, width, most, cuts=(), kind=jnp.bfloat16):
    values = width * jax.random.normal(stream_key, extent, jnp.float32)
    if cuts:
        values = values * shard_levels(stream_key, extent, cuts, -0.22, 0.18)
    return jnp.clip(values, -most, most).astype(kind)


def setup_inputs(seed: int = 0) -> dict:
    arg_keys = jax.random.split(jax.random.key(seed), 14)
    return {
        "previous": scatter_about(arg_keys[0], (N_SECTION, PACKED_LENGTH, D), 1.0, 6.0, ((0, 8), (1, 16))),
        "fresh": scatter_about(arg_keys[1], (PACKED_LENGTH, D), 1.0, 6.0, ((0, 16),)),
        "dt_raw": draw_dt_raw(jax.random.fold_in(arg_keys[13], 71), 0),
        "dt_bias": jnp.clip(jax.random.uniform(arg_keys[3], (N_SECTION, HEADS_M), jnp.float32, -0.5, 0.5) * shard_levels(arg_keys[3], (N_SECTION, HEADS_M), ((0, 8),), -0.4, 0.0), -0.5, 0.5),
        "a_log": draw_a_log(jax.random.fold_in(arg_keys[13], 71), 0),
        "b_in": scatter_about(arg_keys[5], (N_SECTION, PACKED_LENGTH, GROUPS * STATE), STATE ** -0.5, 0.5, ((0, 8), (1, 16))),
        "c_in": scatter_about(arg_keys[6], (N_SECTION, PACKED_LENGTH, GROUPS * STATE), 1.0, 6.0, ((0, 8), (1, 16))),
        "skip_d": jnp.clip(0.5 + 1.0 * jax.random.uniform(arg_keys[7], (N_SECTION, HEADS_M), jnp.float32) ** shard_levels(arg_keys[7], (N_SECTION, HEADS_M), ((0, 8),), -0.2, 0.2), 0.5, 1.5),
        "norm_gain": jnp.clip(1.0 + 0.18 * jax.random.normal(arg_keys[8], (N_SECTION, D), jnp.float32), 0.099609375, 1.8984375).astype(jnp.bfloat16),
        "queries": draw_queries(jax.random.fold_in(arg_keys[13], 71), 0),
        "keys": draw_keys(jax.random.fold_in(arg_keys[13], 71), 0),
        "values": scatter_about(arg_keys[11], (N_SECTION, PACKED_LENGTH, KV_HEADS * HEAD_A), 1.0, 6.0, ((0, 8), (1, 16))),
        "doc_ids": jax.vmap(lambda own: jnp.searchsorted(jnp.cumsum(uneven_parts(own, DOCS, PACKED_LENGTH, MOST, 2)), jnp.arange(PACKED_LENGTH), side="right"))(jax.random.split(arg_keys[12], N_SECTION)).reshape((N_SECTION, PACKED_LENGTH)).astype(jnp.int32),
    }


norm_eps = 1e-05

def block_terms(head_input, step_size, log_cum, b_groups, c_groups, own_ids):
    tok_rows = head_input.shape[0]
    per_group = head_input.shape[1] // GROUPS
    rows_at = jnp.arange(tok_rows)
    same_doc = (own_ids[:, None] == own_ids[None, :]) & (rows_at[:, None] >= rows_at[None, :])
    log_gaps = jnp.where(same_doc[:, :, None], log_cum[:, None, :] - log_cum[None, :, :], 0.0)
    decay_mask = jnp.where(same_doc[:, :, None], jnp.exp(log_gaps), 0.0)
    inner_cb = jnp.einsum('ign,jgn->ijg', c_groups.astype(jnp.float32), b_groups.astype(jnp.float32))
    inner_cb = jnp.repeat(inner_cb, per_group, axis=2)
    intra_w = (decay_mask * inner_cb * step_size[None, :, :]).astype(jnp.bfloat16)
    local_out = jnp.einsum('ijh,jhp->ihp', intra_w.astype(jnp.float32), head_input.astype(jnp.float32))
    last_id = own_ids[-1]
    end_scale = jnp.exp(log_cum[-1][None, :] - log_cum) * step_size * (own_ids == last_id).astype(jnp.float32)[:, None]
    end_w = (end_scale[:, :, None] * jnp.repeat(b_groups, per_group, axis=1).astype(jnp.float32)).astype(jnp.bfloat16)
    block_state = jnp.einsum('thn,thp->hpn', end_w.astype(jnp.float32), head_input.astype(jnp.float32))
    block_gain = jnp.exp(log_cum[-1]) * (own_ids[0] == last_id).astype(jnp.float32)
    return (local_out, block_state, block_gain)

def mixer_section(stream, dt_row, bias_row, alog_row, b_row, c_row, skip_row, gain_row, doc_row):
    mamba_heads = dt_row.shape[1]
    head_dim = D // mamba_heads
    per_group = mamba_heads // GROUPS
    step_size = jax.nn.softplus(dt_row + bias_row[None, :])
    log_rate = -step_size * jnp.exp(alog_row)[None, :]

    def one_block(carry, pieces):
        state_in, prev_last = carry
        head_input, block_step, block_rate, b_block, c_block, own_ids = pieces
        log_cum = jnp.cumsum(block_rate, axis=0)
        local_out, block_state, block_gain = block_terms(head_input, block_step, log_cum, b_block, c_block, own_ids)
        edge_match = (own_ids[0] == prev_last).astype(jnp.float32)
        edge_valid = (own_ids == prev_last).astype(jnp.float32)
        state_bf = state_in.astype(jnp.bfloat16)
        carried_out = jnp.einsum('tgn,gkpn->tgkp', c_block.astype(jnp.float32), state_bf.astype(jnp.float32).reshape(GROUPS, per_group, head_dim, STATE)).reshape(TOK_DEV, mamba_heads, head_dim)
        carried_out = carried_out * (jnp.exp(log_cum) * edge_valid[:, None])[:, :, None]
        mixer_out = local_out + carried_out + skip_row[None, :, None] * head_input.astype(jnp.float32)
        next_state = (block_gain * edge_match)[:, None, None] * state_in + block_state
        return ((next_state, own_ids[-1]), mixer_out)
    pieces = (stream.reshape(N_CTX, TOK_DEV, mamba_heads, head_dim), step_size.reshape(N_CTX, TOK_DEV, mamba_heads), log_rate.reshape(N_CTX, TOK_DEV, mamba_heads), b_row.reshape(N_CTX, TOK_DEV, GROUPS, STATE), c_row.reshape(N_CTX, TOK_DEV, GROUPS, STATE), doc_row.reshape(N_CTX, TOK_DEV))
    initial = (jnp.zeros((mamba_heads, head_dim, STATE), jnp.float32), jnp.array(-1, jnp.int32))
    final_carry, outputs = lax.scan(one_block, initial, pieces)
    flat_out = outputs.reshape(PACKED_LENGTH, D)
    inv_rms = lax.rsqrt(lax.optimization_barrier(jnp.mean(flat_out * flat_out, axis=1, keepdims=True)) + norm_eps)
    return (stream.astype(jnp.float32) + flat_out * inv_rms * gain_row.astype(jnp.float32)[None, :]).astype(jnp.bfloat16)

def attend_section(query_row, key_row, value_row, doc_row):
    group_size = Q_HEADS // KV_HEADS
    inv_sqrt = 1.0 / math.sqrt(HEAD_A)
    rows_at = jnp.arange(PACKED_LENGTH)
    allowed = (doc_row[:, None] == doc_row[None, :]) & (rows_at[:, None] >= rows_at[None, :])
    query_heads = query_row.reshape(PACKED_LENGTH, KV_HEADS, group_size, HEAD_A).transpose(1, 0, 2, 3)
    key_heads = key_row.reshape(PACKED_LENGTH, KV_HEADS, HEAD_A).transpose(1, 0, 2)
    value_heads = value_row.reshape(PACKED_LENGTH, KV_HEADS, HEAD_A).transpose(1, 0, 2)

    def one_head(pieces):
        query_part, key_part, value_part = pieces
        logits = jnp.einsum('igd,jd->igj', query_part.astype(jnp.float32), key_part.astype(jnp.float32)) * inv_sqrt
        logits = jnp.where(allowed[:, None, :], logits, -jnp.inf)
        row_max = lax.optimization_barrier(jnp.max(logits, axis=2, keepdims=True))
        exp_terms = jnp.exp(logits - row_max)
        probs = (exp_terms / lax.optimization_barrier(jnp.sum(exp_terms, axis=2, keepdims=True))).astype(jnp.bfloat16)
        return jnp.einsum('igj,jd->igd', probs.astype(jnp.float32), value_part.astype(jnp.float32))
    head_outs = lax.map(one_head, (query_heads, key_heads, value_heads))
    return head_outs.transpose(1, 0, 2, 3).reshape(PACKED_LENGTH, D).astype(jnp.bfloat16)

def reference(previous, fresh, dt_raw, dt_bias, a_log, b_in, c_in, skip_d, norm_gain, queries, keys, values, doc_ids):
    section_in = jnp.concatenate([fresh[None], previous[:-1]], axis=0)

    def one_section(pieces):
        stream, dt_row, bias_row, alog_row, b_row, c_row, skip_row, gain_row, query_row, key_row, value_row, doc_row = pieces
        mixed = mixer_section(stream, dt_row, bias_row, alog_row, b_row, c_row, skip_row, gain_row, doc_row)
        attended = attend_section(query_row, key_row, value_row, doc_row)
        return (mixed.astype(jnp.float32) + attended.astype(jnp.float32)).astype(jnp.bfloat16)
    return lax.map(one_section, (section_in, dt_raw, dt_bias, a_log, b_in, c_in, skip_d, norm_gain, queries, keys, values, doc_ids))
```

```python
import math

import jax
import jax.numpy as jnp
from jax import lax
from jax.sharding import PartitionSpec as P

HEAD_A = 128
STATE = 128
GROUPS = 8
BLOCK = 128
MOST_DOC = 512
Q_BLOCK = 256


norm_eps = 1e-05


def shifted(value, axis, by):
    peers = lax.axis_size(axis)
    pairs = [(i, i + by) for i in range(peers) if 0 <= i + by < peers]
    return lax.ppermute(value, axis, pairs)


def to_heads(row, chunks):
    tok_rows = row.shape[0]
    width = row.shape[1] // chunks
    moved = lax.all_to_all(row.reshape(tok_rows, chunks, width), "ctx", split_axis=1, concat_axis=0, tiled=True)
    return moved.reshape(tok_rows * chunks, width)


def mixer_heads(x_h, dt_h, bias_h, alog_h, b_g, c_g, skip_h, all_ids):
    total, heads, head_dim = x_h.shape
    nblk = total // BLOCK
    step = jax.nn.softplus(dt_h + bias_h[None, :])
    log_rate = -step * jnp.exp(alog_h)[None, :]
    log_cum = jnp.cumsum(log_rate.reshape(nblk, BLOCK, heads), axis=1)
    lc = log_cum.transpose(0, 2, 1)
    st = step.reshape(nblk, BLOCK, heads).transpose(0, 2, 1)
    ids = all_ids.reshape(nblk, BLOCK)
    xb = x_h.reshape(nblk, BLOCK, heads, head_dim)
    bb = b_g.reshape(nblk, BLOCK, STATE)
    cb_in = c_g.reshape(nblk, BLOCK, STATE)
    rows_at = jnp.arange(BLOCK)
    same_doc = (ids[:, :, None] == ids[:, None, :]) & (rows_at[:, None] >= rows_at[None, :])[None]
    inner_cb = jnp.einsum("bin,bjn->bij", cb_in, bb, preferred_element_type=jnp.float32)
    decay = jnp.where(same_doc[:, None], jnp.exp(lc[:, :, :, None] - lc[:, :, None, :]), 0.0)
    intra_w = (decay * inner_cb[:, None] * st[:, :, None, :]).astype(jnp.bfloat16)
    local_out = jnp.einsum("bhij,bjhp->bihp", intra_w, xb, preferred_element_type=jnp.float32)
    last_id = ids[:, -1]
    end_scale = (
        jnp.exp(lc[:, :, -1:] - lc) * st * (ids == last_id[:, None]).astype(jnp.float32)[:, None, :]
    )
    end_w = (end_scale[:, :, :, None] * bb.astype(jnp.float32)[:, None]).astype(jnp.bfloat16)
    block_state = jnp.einsum("bhjn,bjhp->bhpn", end_w, xb, preferred_element_type=jnp.float32)
    prev_last = jnp.concatenate([jnp.full((1,), -1, ids.dtype), last_id[:-1]])
    edge_match = (ids[:, 0] == prev_last).astype(jnp.float32)
    block_gain = jnp.exp(lc[:, :, -1]) * (ids[:, 0] == last_id).astype(jnp.float32)[:, None]
    block_gain = block_gain * edge_match[:, None]
    carries = [jnp.zeros_like(block_state[0])]
    for b in range(nblk - 1):
        carries.append(block_gain[b][:, None, None] * carries[-1] + block_state[b])
    carry_bf = jnp.stack(carries).astype(jnp.bfloat16)
    carried = jnp.einsum("bin,bhpn->bihp", cb_in, carry_bf, preferred_element_type=jnp.float32)
    edge_valid = (ids == prev_last[:, None]).astype(jnp.float32)
    scale = jnp.exp(log_cum) * edge_valid[:, :, None]
    carried = carried * scale[:, :, :, None]
    mixer_out = local_out + carried + skip_h[None, None, :, None] * xb.astype(jnp.float32)
    return mixer_out.reshape(total, heads * head_dim)


def attend_heads(q_h, k_h, v_h, all_ids):
    total, qpd, _ = q_h.shape
    inv_sqrt = 1.0 / math.sqrt(HEAD_A)
    q_blk = min(Q_BLOCK, total)
    window = min(q_blk + MOST_DOC, total)
    outs = []
    for i in range(total // q_blk):
        q0 = i * q_blk
        k0 = max(0, min(q0 + q_blk - window, total - window))
        qb = q_h[q0:q0 + q_blk]
        kb = k_h[k0:k0 + window]
        vb = v_h[k0:k0 + window]
        q_at = q0 + jnp.arange(q_blk)
        k_at = k0 + jnp.arange(window)
        allowed = (all_ids[q0:q0 + q_blk][:, None] == all_ids[k0:k0 + window][None, :]) & (
            q_at[:, None] >= k_at[None, :]
        )
        logits = jnp.einsum("igd,jd->igj", qb, kb, preferred_element_type=jnp.float32) * inv_sqrt
        logits = jnp.where(allowed[:, None, :], logits, -jnp.inf)
        row_max = jnp.max(logits, axis=2, keepdims=True)
        exp_terms = jnp.exp(logits - row_max)
        probs = (exp_terms / jnp.sum(exp_terms, axis=2, keepdims=True)).astype(jnp.bfloat16)
        outs.append(
            jnp.einsum("igj,jd->igd", probs, vb, preferred_element_type=jnp.float32).astype(jnp.bfloat16)
        )
    return jnp.concatenate(outs, axis=0).reshape(total, qpd * HEAD_A)


def body(
    previous,
    fresh,
    dt_raw,
    dt_bias,
    a_log,
    b_in,
    c_in,
    skip_d,
    norm_gain,
    queries,
    keys,
    values,
    doc_ids,
):
    tok_rows, width = fresh.shape
    nctx = lax.axis_size("ctx")
    me = lax.axis_index("ctx")
    total = tok_rows * nctx
    part = width // nctx
    mamba_heads = dt_raw.shape[2]
    heads_dev = mamba_heads // nctx
    head_dim = width // mamba_heads
    kv_heads = keys.shape[2] // HEAD_A
    qpd = part // HEAD_A

    q_h = to_heads(queries[0], nctx).reshape(total, qpd, HEAD_A)
    kvbc = jnp.stack(
        [
            keys[0].reshape(tok_rows, kv_heads, HEAD_A),
            values[0].reshape(tok_rows, kv_heads, HEAD_A),
            b_in[0].reshape(tok_rows, GROUPS, STATE),
            c_in[0].reshape(tok_rows, GROUPS, STATE),
        ],
        axis=2,
    )
    kvbc = jnp.repeat(kvbc, nctx // kv_heads, axis=1).reshape(tok_rows, nctx * 4 * HEAD_A)
    kvbc_h = to_heads(kvbc, nctx).reshape(total, 4, HEAD_A)
    k_h, v_h, b_g, c_g = kvbc_h[:, 0], kvbc_h[:, 1], kvbc_h[:, 2], kvbc_h[:, 3]
    dt_h = to_heads(dt_raw[0], nctx)

    handed = shifted(previous[0], "section", 1)
    stream = jnp.where(lax.axis_index("section") == 0, fresh, handed)
    x_h = to_heads(stream, nctx)

    all_ids = doc_ids[0]
    bias_h = lax.dynamic_slice_in_dim(dt_bias[0], me * heads_dev, heads_dev)
    alog_h = lax.dynamic_slice_in_dim(a_log[0], me * heads_dev, heads_dev)
    skip_h = lax.dynamic_slice_in_dim(skip_d[0], me * heads_dev, heads_dev)
    gain_h = lax.dynamic_slice_in_dim(norm_gain[0], me * part, part)

    attended = attend_heads(q_h, k_h, v_h, all_ids)

    mixer_out = mixer_heads(
        x_h.reshape(total, heads_dev, head_dim), dt_h, bias_h, alog_h, b_g, c_g, skip_h, all_ids
    )
    sq_part = jnp.sum(mixer_out * mixer_out, axis=1, keepdims=True)
    mean_sq = lax.psum(sq_part, "ctx") / width
    inv_rms = lax.rsqrt(mean_sq + norm_eps)
    mixed = (
        x_h.astype(jnp.float32) + mixer_out * inv_rms * gain_h.astype(jnp.float32)[None, :]
    ).astype(jnp.bfloat16)
    out_h = (mixed.astype(jnp.float32) + attended.astype(jnp.float32)).astype(jnp.bfloat16)
    returned = lax.all_to_all(
        out_h.reshape(total, 1, part), "ctx", split_axis=0, concat_axis=1, tiled=True
    )
    return returned.reshape(tok_rows, width)[None]


def solution(mesh):
    in_specs = (
        P("section", "ctx", None),
        P("ctx", None),
        P("section", "ctx", None),
        P("section", None),
        P("section", None),
        P("section", "ctx", None),
        P("section", "ctx", None),
        P("section", None),
        P("section", None),
        P("section", "ctx", None),
        P("section", "ctx", None),
        P("section", "ctx", None),
        P("section", None),
    )
    out_specs = P("section", "ctx", None)
    return jax.shard_map(body, mesh=mesh, in_specs=in_specs, out_specs=out_specs, check_vma=False)
```

```python
import math

import jax
import jax.numpy as jnp
from jax import lax
from jax.sharding import PartitionSpec as P

HEAD_A = 128
STATE = 128
GROUPS = 8
BLOCK = 128
MOST_DOC = 512
Q_BLOCK = 256


norm_eps = 1e-05


def shifted(value, axis, by):
    peers = lax.axis_size(axis)
    pairs = [(i, i + by) for i in range(peers) if 0 <= i + by < peers]
    return lax.ppermute(value, axis, pairs)


def to_heads(row, chunks):
    tok_rows = row.shape[0]
    width = row.shape[1] // chunks
    lead = row.reshape(tok_rows, chunks, width).transpose(1, 0, 2)
    moved = lax.all_to_all(lead, "ctx", split_axis=0, concat_axis=0, tiled=True)
    return moved.reshape(tok_rows * chunks, width)


def to_rows(block, chunks):
    total, width = block.shape
    tok_rows = total // chunks
    moved = lax.all_to_all(block.reshape(chunks, tok_rows, width), "ctx", split_axis=0, concat_axis=0, tiled=True)
    return moved.transpose(1, 0, 2).reshape(tok_rows, chunks * width)


def mixer_heads(x_h, dt_h, bias_h, alog_h, b_g, c_g, skip_h, all_ids):
    total, heads, head_dim = x_h.shape
    nblk = total // BLOCK
    step = jax.nn.softplus(dt_h + bias_h[None, :])
    log_rate = -step * jnp.exp(alog_h)[None, :]
    log_cum = jnp.cumsum(log_rate.reshape(nblk, BLOCK, heads), axis=1)
    lc = log_cum.transpose(0, 2, 1)
    st = step.reshape(nblk, BLOCK, heads).transpose(0, 2, 1)
    ids = all_ids.reshape(nblk, BLOCK)
    xb = x_h.reshape(nblk, BLOCK, heads, head_dim)
    bb = b_g.reshape(nblk, BLOCK, STATE)
    cb_in = c_g.reshape(nblk, BLOCK, STATE)
    rows_at = jnp.arange(BLOCK)
    same_doc = (ids[:, :, None] == ids[:, None, :]) & (rows_at[:, None] >= rows_at[None, :])[None]
    inner_cb = jnp.einsum("bin,bjn->bij", cb_in, bb, preferred_element_type=jnp.float32)
    decay = jnp.where(same_doc[:, None], jnp.exp(lc[:, :, :, None] - lc[:, :, None, :]), 0.0)
    intra_w = (decay * inner_cb[:, None] * st[:, :, None, :]).astype(jnp.bfloat16)
    local_out = jnp.einsum("bhij,bjhp->bihp", intra_w, xb, preferred_element_type=jnp.float32)
    last_id = ids[:, -1]
    end_scale = (
        jnp.exp(lc[:, :, -1:] - lc) * st * (ids == last_id[:, None]).astype(jnp.float32)[:, None, :]
    )
    end_w = (end_scale[:, :, :, None] * bb.astype(jnp.float32)[:, None]).astype(jnp.bfloat16)
    block_state = jnp.einsum("bhjn,bjhp->bhpn", end_w, xb, preferred_element_type=jnp.float32)
    prev_last = jnp.concatenate([jnp.full((1,), -1, ids.dtype), last_id[:-1]])
    edge_match = (ids[:, 0] == prev_last).astype(jnp.float32)
    block_gain = jnp.exp(lc[:, :, -1]) * (ids[:, 0] == last_id).astype(jnp.float32)[:, None]
    block_gain = block_gain * edge_match[:, None]
    carries = [jnp.zeros_like(block_state[0])]
    for b in range(nblk - 1):
        carries.append(block_gain[b][:, None, None] * carries[-1] + block_state[b])
    carry_bf = jnp.stack(carries).astype(jnp.bfloat16)
    carried = jnp.einsum("bin,bhpn->bihp", cb_in, carry_bf, preferred_element_type=jnp.float32)
    edge_valid = (ids == prev_last[:, None]).astype(jnp.float32)
    scale = jnp.exp(log_cum) * edge_valid[:, :, None]
    carried = carried * scale[:, :, :, None]
    mixer_out = local_out + carried + skip_h[None, None, :, None] * xb.astype(jnp.float32)
    return mixer_out.reshape(total, heads * head_dim)


def attend_heads(q_h, k_h, v_h, all_ids):
    total, qpd, _ = q_h.shape
    inv_sqrt = 1.0 / math.sqrt(HEAD_A)
    q_blk = min(Q_BLOCK, total)
    window = min(q_blk + MOST_DOC, total)
    outs = []
    for i in range(total // q_blk):
        q0 = i * q_blk
        k0 = max(0, min(q0 + q_blk - window, total - window))
        qb = q_h[q0:q0 + q_blk]
        kb = k_h[k0:k0 + window]
        vb = v_h[k0:k0 + window]
        q_at = q0 + jnp.arange(q_blk)
        k_at = k0 + jnp.arange(window)
        allowed = (all_ids[q0:q0 + q_blk][:, None] == all_ids[k0:k0 + window][None, :]) & (
            q_at[:, None] >= k_at[None, :]
        )
        logits = jnp.einsum("igd,jd->igj", qb, kb, preferred_element_type=jnp.float32) * inv_sqrt
        logits = jnp.where(allowed[:, None, :], logits, -jnp.inf)
        row_max = jnp.max(logits, axis=2, keepdims=True)
        exp_terms = jnp.exp(logits - row_max)
        probs = (exp_terms / jnp.sum(exp_terms, axis=2, keepdims=True)).astype(jnp.bfloat16)
        outs.append(
            jnp.einsum("igj,jd->igd", probs, vb, preferred_element_type=jnp.float32).astype(jnp.bfloat16)
        )
    return jnp.concatenate(outs, axis=0).reshape(total, qpd * HEAD_A)


def body(
    previous,
    fresh,
    dt_raw,
    dt_bias,
    a_log,
    b_in,
    c_in,
    skip_d,
    norm_gain,
    queries,
    keys,
    values,
    doc_ids,
):
    tok_rows, width = fresh.shape
    nctx = lax.axis_size("ctx")
    me = lax.axis_index("ctx")
    total = tok_rows * nctx
    part = width // nctx
    mamba_heads = dt_raw.shape[2]
    heads_dev = mamba_heads // nctx
    head_dim = width // mamba_heads
    kv_heads = keys.shape[2] // HEAD_A
    qpd = part // HEAD_A

    q_h = to_heads(queries[0], nctx).reshape(total, qpd, HEAD_A)
    kvbc = jnp.stack(
        [
            keys[0].reshape(tok_rows, kv_heads, HEAD_A),
            values[0].reshape(tok_rows, kv_heads, HEAD_A),
            b_in[0].reshape(tok_rows, GROUPS, STATE),
            c_in[0].reshape(tok_rows, GROUPS, STATE),
        ],
        axis=2,
    )
    kvbc = jnp.repeat(kvbc, nctx // kv_heads, axis=1).reshape(tok_rows, nctx * 4 * HEAD_A)
    kvbc_h = to_heads(kvbc, nctx).reshape(total, 4, HEAD_A)
    k_h, v_h, b_g, c_g = kvbc_h[:, 0], kvbc_h[:, 1], kvbc_h[:, 2], kvbc_h[:, 3]
    dt_h = to_heads(dt_raw[0], nctx)

    handed = shifted(previous[0], "section", 1)
    stream = jnp.where(lax.axis_index("section") == 0, fresh, handed)
    x_h = to_heads(stream, nctx)

    all_ids = doc_ids[0]
    bias_h = lax.dynamic_slice_in_dim(dt_bias[0], me * heads_dev, heads_dev)
    alog_h = lax.dynamic_slice_in_dim(a_log[0], me * heads_dev, heads_dev)
    skip_h = lax.dynamic_slice_in_dim(skip_d[0], me * heads_dev, heads_dev)
    gain_h = lax.dynamic_slice_in_dim(norm_gain[0], me * part, part)

    attended = attend_heads(q_h, k_h, v_h, all_ids)

    mixer_out = mixer_heads(
        x_h.reshape(total, heads_dev, head_dim), dt_h, bias_h, alog_h, b_g, c_g, skip_h, all_ids
    )
    sq_part = jnp.sum(mixer_out * mixer_out, axis=1)
    sq_all = lax.all_to_all(
        jnp.broadcast_to(sq_part[None], (nctx, total)), "ctx", split_axis=0, concat_axis=0, tiled=True
    )
    mean_sq = (jnp.sum(sq_all, axis=0) / width)[:, None]
    inv_rms = lax.rsqrt(mean_sq + norm_eps)
    mixed = (
        x_h.astype(jnp.float32) + mixer_out * inv_rms * gain_h.astype(jnp.float32)[None, :]
    ).astype(jnp.bfloat16)
    out_h = (mixed.astype(jnp.float32) + attended.astype(jnp.float32)).astype(jnp.bfloat16)
    return to_rows(out_h, nctx)[None]


def solution(mesh):
    in_specs = (
        P("section", "ctx", None),
        P("ctx", None),
        P("section", "ctx", None),
        P("section", None),
        P("section", None),
        P("section", "ctx", None),
        P("section", "ctx", None),
        P("section", None),
        P("section", None),
        P("section", "ctx", None),
        P("section", "ctx", None),
        P("section", "ctx", None),
        P("section", None),
    )
    out_specs = P("section", "ctx", None)
    return jax.shard_map(body, mesh=mesh, in_specs=in_specs, out_specs=out_specs, check_vma=False)
```

```python
import math

import jax
import jax.numpy as jnp
from jax import lax
from jax.experimental import pallas as pl
from jax.sharding import PartitionSpec as P

HEAD_A = 128
STATE = 128
GROUPS = 8
BLOCK = 128
MOST_DOC = 512
Q_BLOCK = 256


norm_eps = 1e-05


def shifted(value, axis, by):
    peers = lax.axis_size(axis)
    pairs = [(i, i + by) for i in range(peers) if 0 <= i + by < peers]
    return lax.ppermute(value, axis, pairs)


def to_heads(row, chunks):
    tok_rows = row.shape[0]
    width = row.shape[1] // chunks
    lead = row.reshape(tok_rows, chunks, width).transpose(1, 0, 2)
    moved = lax.all_to_all(lead, "ctx", split_axis=0, concat_axis=0, tiled=True)
    return moved.reshape(tok_rows * chunks, width)


def to_rows(block, chunks):
    total, width = block.shape
    tok_rows = total // chunks
    moved = lax.all_to_all(block.reshape(chunks, tok_rows, width), "ctx", split_axis=0, concat_axis=0, tiled=True)
    return moved.transpose(1, 0, 2).reshape(tok_rows, chunks * width)


def mixer_heads(x_h, dt_h, bias_h, alog_h, b_g, c_g, skip_h, all_ids):
    total, heads, head_dim = x_h.shape
    nblk = total // BLOCK
    step = jax.nn.softplus(dt_h + bias_h[None, :])
    log_rate = -step * jnp.exp(alog_h)[None, :]
    log_cum = jnp.cumsum(log_rate.reshape(nblk, BLOCK, heads), axis=1)
    lc = log_cum.transpose(0, 2, 1)
    st = step.reshape(nblk, BLOCK, heads).transpose(0, 2, 1)
    ids = all_ids.reshape(nblk, BLOCK)
    xb = x_h.reshape(nblk, BLOCK, heads, head_dim)
    bb = b_g.reshape(nblk, BLOCK, STATE)
    cb_in = c_g.reshape(nblk, BLOCK, STATE)
    rows_at = jnp.arange(BLOCK)
    same_doc = (ids[:, :, None] == ids[:, None, :]) & (rows_at[:, None] >= rows_at[None, :])[None]
    inner_cb = jnp.einsum("bin,bjn->bij", cb_in, bb, preferred_element_type=jnp.float32)
    decay = jnp.where(same_doc[:, None], jnp.exp(lc[:, :, :, None] - lc[:, :, None, :]), 0.0)
    intra_w = (decay * inner_cb[:, None] * st[:, :, None, :]).astype(jnp.bfloat16)
    local_out = jnp.einsum("bhij,bjhp->bihp", intra_w, xb, preferred_element_type=jnp.float32)
    last_id = ids[:, -1]
    end_scale = (
        jnp.exp(lc[:, :, -1:] - lc) * st * (ids == last_id[:, None]).astype(jnp.float32)[:, None, :]
    )
    end_w = (end_scale[:, :, :, None] * bb.astype(jnp.float32)[:, None]).astype(jnp.bfloat16)
    block_state = jnp.einsum("bhjn,bjhp->bhpn", end_w, xb, preferred_element_type=jnp.float32)
    prev_last = jnp.concatenate([jnp.full((1,), -1, ids.dtype), last_id[:-1]])
    edge_match = (ids[:, 0] == prev_last).astype(jnp.float32)
    block_gain = jnp.exp(lc[:, :, -1]) * (ids[:, 0] == last_id).astype(jnp.float32)[:, None]
    block_gain = block_gain * edge_match[:, None]
    carries = [jnp.zeros_like(block_state[0])]
    for b in range(nblk - 1):
        carries.append(block_gain[b][:, None, None] * carries[-1] + block_state[b])
    carry_bf = jnp.stack(carries).astype(jnp.bfloat16)
    carried = jnp.einsum("bin,bhpn->bihp", cb_in, carry_bf, preferred_element_type=jnp.float32)
    edge_valid = (ids == prev_last[:, None]).astype(jnp.float32)
    scale = jnp.exp(log_cum) * edge_valid[:, :, None]
    carried = carried * scale[:, :, :, None]
    mixer_out = local_out + carried + skip_h[None, None, :, None] * xb.astype(jnp.float32)
    return mixer_out.reshape(total, heads * head_dim)


def attend_heads(q_h, k_h, v_h, all_ids, interpret=False):
    total, q_width = q_h.shape
    groups = q_width // HEAD_A
    q_blk = min(Q_BLOCK, total)
    window = min(q_blk + MOST_DOC, total)
    inv_sqrt = 1.0 / math.sqrt(HEAD_A)

    def kernel(q_ref, k_ref, v_ref, ic_ref, ir_ref, o_ref):
        q0 = pl.multiple_of(pl.program_id(0) * q_blk, q_blk)
        k0 = pl.multiple_of(jnp.clip(q0 + q_blk - window, 0, total - window), q_blk)
        kb = k_ref[pl.ds(k0, window), :]
        vb = v_ref[pl.ds(k0, window), :]
        qid = ic_ref[pl.ds(q0, q_blk), :]
        kid = ir_ref[:, pl.ds(k0, window)]
        q_at = q0 + lax.broadcasted_iota(jnp.int32, (q_blk, window), 0)
        k_at = k0 + lax.broadcasted_iota(jnp.int32, (q_blk, window), 1)
        allowed = (qid == kid) & (q_at >= k_at)
        for g in range(groups):
            cols = slice(g * HEAD_A, (g + 1) * HEAD_A)
            logits = lax.dot_general(
                q_ref[:, cols], kb, (((1,), (1,)), ((), ())), preferred_element_type=jnp.float32
            ) * inv_sqrt
            logits = jnp.where(allowed, logits, -jnp.inf)
            row_max = jnp.max(logits, axis=1, keepdims=True)
            exp_terms = jnp.exp(logits - row_max)
            probs = (exp_terms / jnp.sum(exp_terms, axis=1, keepdims=True)).astype(jnp.bfloat16)
            o_ref[:, cols] = jnp.dot(probs, vb, preferred_element_type=jnp.float32).astype(o_ref.dtype)

    return pl.pallas_call(
        kernel,
        grid=(total // q_blk,),
        in_specs=[
            pl.BlockSpec((q_blk, q_width), lambda i: (i, 0)),
            pl.BlockSpec((total, HEAD_A), lambda i: (0, 0)),
            pl.BlockSpec((total, HEAD_A), lambda i: (0, 0)),
            pl.BlockSpec((total, 1), lambda i: (0, 0)),
            pl.BlockSpec((1, total), lambda i: (0, 0)),
        ],
        out_specs=pl.BlockSpec((q_blk, q_width), lambda i: (i, 0)),
        out_shape=jax.ShapeDtypeStruct((total, q_width), jnp.bfloat16),
        interpret=interpret,
    )(q_h, k_h, v_h, all_ids.reshape(total, 1), all_ids.reshape(1, total))


def body(
    previous,
    fresh,
    dt_raw,
    dt_bias,
    a_log,
    b_in,
    c_in,
    skip_d,
    norm_gain,
    queries,
    keys,
    values,
    doc_ids,
):
    tok_rows, width = fresh.shape
    nctx = lax.axis_size("ctx")
    me = lax.axis_index("ctx")
    total = tok_rows * nctx
    part = width // nctx
    mamba_heads = dt_raw.shape[2]
    heads_dev = mamba_heads // nctx
    head_dim = width // mamba_heads
    kv_heads = keys.shape[2] // HEAD_A
    qpd = part // HEAD_A

    q_h = to_heads(queries[0], nctx)
    kvbc = jnp.stack(
        [
            keys[0].reshape(tok_rows, kv_heads, HEAD_A),
            values[0].reshape(tok_rows, kv_heads, HEAD_A),
            b_in[0].reshape(tok_rows, GROUPS, STATE),
            c_in[0].reshape(tok_rows, GROUPS, STATE),
        ],
        axis=2,
    )
    kvbc = jnp.repeat(kvbc, nctx // kv_heads, axis=1).reshape(tok_rows, nctx * 4 * HEAD_A)
    kvbc_h = to_heads(kvbc, nctx).reshape(total, 4, HEAD_A)
    k_h, v_h, b_g, c_g = kvbc_h[:, 0], kvbc_h[:, 1], kvbc_h[:, 2], kvbc_h[:, 3]
    dt_h = to_heads(dt_raw[0], nctx)

    handed = shifted(previous[0], "section", 1)
    stream = jnp.where(lax.axis_index("section") == 0, fresh, handed)
    x_h = to_heads(stream, nctx)

    all_ids = doc_ids[0]
    bias_h = lax.dynamic_slice_in_dim(dt_bias[0], me * heads_dev, heads_dev)
    alog_h = lax.dynamic_slice_in_dim(a_log[0], me * heads_dev, heads_dev)
    skip_h = lax.dynamic_slice_in_dim(skip_d[0], me * heads_dev, heads_dev)
    gain_h = lax.dynamic_slice_in_dim(norm_gain[0], me * part, part)

    attended = attend_heads(q_h, k_h, v_h, all_ids)

    mixer_out = mixer_heads(
        x_h.reshape(total, heads_dev, head_dim), dt_h, bias_h, alog_h, b_g, c_g, skip_h, all_ids
    )
    sq_part = jnp.sum(mixer_out * mixer_out, axis=1)
    sq_all = lax.all_to_all(
        jnp.broadcast_to(sq_part[None], (nctx, total)), "ctx", split_axis=0, concat_axis=0, tiled=True
    )
    mean_sq = (jnp.sum(sq_all, axis=0) / width)[:, None]
    inv_rms = lax.rsqrt(mean_sq + norm_eps)
    mixed = (
        x_h.astype(jnp.float32) + mixer_out * inv_rms * gain_h.astype(jnp.float32)[None, :]
    ).astype(jnp.bfloat16)
    out_h = (mixed.astype(jnp.float32) + attended.astype(jnp.float32)).astype(jnp.bfloat16)
    return to_rows(out_h, nctx)[None]


def solution(mesh):
    in_specs = (
        P("section", "ctx", None),
        P("ctx", None),
        P("section", "ctx", None),
        P("section", None),
        P("section", None),
        P("section", "ctx", None),
        P("section", "ctx", None),
        P("section", None),
        P("section", None),
        P("section", "ctx", None),
        P("section", "ctx", None),
        P("section", "ctx", None),
        P("section", None),
    )
    out_specs = P("section", "ctx", None)
    return jax.shard_map(body, mesh=mesh, in_specs=in_specs, out_specs=out_specs, check_vma=False)
```

```python
import math

import jax
import jax.numpy as jnp
from jax import lax
from jax.experimental import pallas as pl
from jax.experimental.pallas import tpu as pltpu
from jax.sharding import PartitionSpec as P

HEAD_A = 128
STATE = 128
GROUPS = 8
BLOCK = 128
MOST_DOC = 512
Q_BLOCK = 256


norm_eps = 1e-05


def shifted(value, axis, by):
    peers = lax.axis_size(axis)
    pairs = [(i, i + by) for i in range(peers) if 0 <= i + by < peers]
    return lax.ppermute(value, axis, pairs)


def to_heads(row, chunks):
    tok_rows = row.shape[0]
    width = row.shape[1] // chunks
    lead = row.reshape(tok_rows, chunks, width).transpose(1, 0, 2)
    moved = lax.all_to_all(lead, "ctx", split_axis=0, concat_axis=0, tiled=True)
    return moved.reshape(tok_rows * chunks, width)


def to_rows(block, chunks):
    total, width = block.shape
    tok_rows = total // chunks
    moved = lax.all_to_all(block.reshape(chunks, tok_rows, width), "ctx", split_axis=0, concat_axis=0, tiled=True)
    return moved.transpose(1, 0, 2).reshape(tok_rows, chunks * width)


def mixer_heads(x_h, dt_h, bias_h, alog_h, b_g, c_g, skip_h, all_ids, interpret=False):
    total, x_width = x_h.shape
    heads = dt_h.shape[1]
    head_dim = x_width // heads
    nblk = total // BLOCK
    step = jax.nn.softplus(dt_h + bias_h[None, :])
    log_rate = -step * jnp.exp(alog_h)[None, :]
    log_cum = jnp.cumsum(log_rate.reshape(nblk, BLOCK, heads), axis=1)
    st = step.reshape(nblk, BLOCK, heads)
    ids = all_ids.reshape(nblk, BLOCK)
    last_id = ids[:, -1]
    prev_last = jnp.concatenate([jnp.full((1,), -1, ids.dtype), last_id[:-1]])
    edge_valid = (ids == prev_last[:, None]).astype(jnp.float32)
    carry_scale = jnp.exp(log_cum) * edge_valid[:, :, None]
    end_scale = (
        jnp.exp(log_cum[:, -1:, :] - log_cum) * st * (ids == last_id[:, None]).astype(jnp.float32)[:, :, None]
    )
    edge_match = (ids[:, 0] == prev_last).astype(jnp.float32)
    block_gain = jnp.exp(log_cum[:, -1, :]) * (ids[:, 0] == last_id).astype(jnp.float32)[:, None]
    block_gain = block_gain * edge_match[:, None]
    gain_rows = jnp.broadcast_to(block_gain[:, :, None], (nblk, heads, STATE))
    lc_rows = log_cum.transpose(0, 2, 1)
    st_rows = st.transpose(0, 2, 1)
    x_t = x_h.T

    def kernel(x_ref, xt_ref, b_ref, c_ref, lcc_ref, lcr_ref, str_ref, csc_ref, esc_ref, gain_ref,
               idc_ref, idr_ref, skip_ref, o_ref, sq_ref, carry_ref):
        @pl.when(pl.program_id(0) == 0)
        def _():
            carry_ref[...] = jnp.zeros(carry_ref.shape, carry_ref.dtype)

        b_blk = b_ref[...]
        c_blk = c_ref[...]
        inner_cb = lax.dot_general(c_blk, b_blk, (((1,), (1,)), ((), ())), preferred_element_type=jnp.float32)
        rows_at = lax.broadcasted_iota(jnp.int32, (BLOCK, BLOCK), 0)
        cols_at = lax.broadcasted_iota(jnp.int32, (BLOCK, BLOCK), 1)
        same_doc = (idc_ref[...] == idr_ref[0]) & (rows_at >= cols_at)
        b_f32 = b_blk.astype(jnp.float32)
        sq = jnp.zeros((BLOCK, 1), jnp.float32)
        for h in range(heads):
            cols = slice(h * head_dim, (h + 1) * head_dim)
            lc_c = lcc_ref[0, :, h:h + 1]
            lc_r = lcr_ref[0, h:h + 1, :]
            decay = jnp.where(same_doc, jnp.exp(lc_c - lc_r), 0.0)
            intra_w = (decay * inner_cb * str_ref[0, h:h + 1, :]).astype(jnp.bfloat16)
            xh = x_ref[:, cols]
            local = jnp.dot(intra_w, xh, preferred_element_type=jnp.float32)
            state_bf = carry_ref[h].astype(jnp.bfloat16)
            carried = lax.dot_general(
                c_blk, state_bf, (((1,), (1,)), ((), ())), preferred_element_type=jnp.float32
            )
            carried = carried * csc_ref[0, :, h:h + 1]
            out = local + carried + skip_ref[h] * xh.astype(jnp.float32)
            o_ref[:, cols] = out
            sq = sq + jnp.sum(out * out, axis=1, keepdims=True)
            end_w = (esc_ref[0, :, h:h + 1] * b_f32).astype(jnp.bfloat16)
            block_state = jnp.dot(xt_ref[cols, :], end_w, preferred_element_type=jnp.float32)
            carry_ref[h] = gain_ref[0, h:h + 1, :] * carry_ref[h] + block_state
        sq_ref[...] = sq

    per_block = lambda shape: pl.BlockSpec((1,) + shape, lambda i: (i, 0, 0))
    return pl.pallas_call(
        kernel,
        grid=(nblk,),
        in_specs=[
            pl.BlockSpec((BLOCK, x_width), lambda i: (i, 0)),
            pl.BlockSpec((x_width, BLOCK), lambda i: (0, i)),
            pl.BlockSpec((BLOCK, STATE), lambda i: (i, 0)),
            pl.BlockSpec((BLOCK, STATE), lambda i: (i, 0)),
            per_block((BLOCK, heads)),
            per_block((heads, BLOCK)),
            per_block((heads, BLOCK)),
            per_block((BLOCK, heads)),
            per_block((BLOCK, heads)),
            per_block((heads, STATE)),
            pl.BlockSpec((BLOCK, 1), lambda i: (i, 0)),
            per_block((1, BLOCK)),
            pl.BlockSpec(memory_space=pltpu.SMEM),
        ],
        out_specs=[
            pl.BlockSpec((BLOCK, x_width), lambda i: (i, 0)),
            pl.BlockSpec((BLOCK, 1), lambda i: (i, 0)),
        ],
        out_shape=[
            jax.ShapeDtypeStruct((total, x_width), jnp.float32),
            jax.ShapeDtypeStruct((total, 1), jnp.float32),
        ],
        scratch_shapes=[pltpu.VMEM((heads, head_dim, STATE), jnp.float32)],
        compiler_params=pltpu.CompilerParams(dimension_semantics=("arbitrary",)),
        interpret=interpret,
    )(
        x_h, x_t, b_g, c_g, log_cum, lc_rows, st_rows, carry_scale, end_scale, gain_rows,
        all_ids.reshape(total, 1), ids.reshape(nblk, 1, BLOCK), skip_h,
    )


def attend_heads(q_h, k_h, v_h, all_ids, interpret=False):
    total, q_width = q_h.shape
    groups = q_width // HEAD_A
    q_blk = min(Q_BLOCK, total)
    window = min(q_blk + MOST_DOC, total)
    inv_sqrt = 1.0 / math.sqrt(HEAD_A)

    def kernel(q_ref, k_ref, v_ref, ic_ref, ir_ref, o_ref):
        q0 = pl.multiple_of(pl.program_id(0) * q_blk, q_blk)
        k0 = pl.multiple_of(jnp.clip(q0 + q_blk - window, 0, total - window), q_blk)
        kb = k_ref[pl.ds(k0, window), :]
        vb = v_ref[pl.ds(k0, window), :]
        qid = ic_ref[pl.ds(q0, q_blk), :]
        kid = ir_ref[:, pl.ds(k0, window)]
        q_at = q0 + lax.broadcasted_iota(jnp.int32, (q_blk, window), 0)
        k_at = k0 + lax.broadcasted_iota(jnp.int32, (q_blk, window), 1)
        allowed = (qid == kid) & (q_at >= k_at)
        for g in range(groups):
            cols = slice(g * HEAD_A, (g + 1) * HEAD_A)
            logits = lax.dot_general(
                q_ref[:, cols], kb, (((1,), (1,)), ((), ())), preferred_element_type=jnp.float32
            ) * inv_sqrt
            logits = jnp.where(allowed, logits, -jnp.inf)
            row_max = jnp.max(logits, axis=1, keepdims=True)
            exp_terms = jnp.exp(logits - row_max)
            probs = (exp_terms / jnp.sum(exp_terms, axis=1, keepdims=True)).astype(jnp.bfloat16)
            o_ref[:, cols] = jnp.dot(probs, vb, preferred_element_type=jnp.float32).astype(o_ref.dtype)

    return pl.pallas_call(
        kernel,
        grid=(total // q_blk,),
        in_specs=[
            pl.BlockSpec((q_blk, q_width), lambda i: (i, 0)),
            pl.BlockSpec((total, HEAD_A), lambda i: (0, 0)),
            pl.BlockSpec((total, HEAD_A), lambda i: (0, 0)),
            pl.BlockSpec((total, 1), lambda i: (0, 0)),
            pl.BlockSpec((1, total), lambda i: (0, 0)),
        ],
        out_specs=pl.BlockSpec((q_blk, q_width), lambda i: (i, 0)),
        out_shape=jax.ShapeDtypeStruct((total, q_width), jnp.bfloat16),
        interpret=interpret,
    )(q_h, k_h, v_h, all_ids.reshape(total, 1), all_ids.reshape(1, total))


def body(
    previous,
    fresh,
    dt_raw,
    dt_bias,
    a_log,
    b_in,
    c_in,
    skip_d,
    norm_gain,
    queries,
    keys,
    values,
    doc_ids,
):
    tok_rows, width = fresh.shape
    nctx = lax.axis_size("ctx")
    me = lax.axis_index("ctx")
    total = tok_rows * nctx
    part = width // nctx
    mamba_heads = dt_raw.shape[2]
    heads_dev = mamba_heads // nctx
    head_dim = width // mamba_heads
    kv_heads = keys.shape[2] // HEAD_A
    qpd = part // HEAD_A

    q_h = to_heads(queries[0], nctx)
    kvbc = jnp.stack(
        [
            keys[0].reshape(tok_rows, kv_heads, HEAD_A),
            values[0].reshape(tok_rows, kv_heads, HEAD_A),
            b_in[0].reshape(tok_rows, GROUPS, STATE),
            c_in[0].reshape(tok_rows, GROUPS, STATE),
        ],
        axis=2,
    )
    kvbc = jnp.repeat(kvbc, nctx // kv_heads, axis=1).reshape(tok_rows, nctx * 4 * HEAD_A)
    kvbc_h = to_heads(kvbc, nctx).reshape(total, 4, HEAD_A)
    k_h, v_h, b_g, c_g = kvbc_h[:, 0], kvbc_h[:, 1], kvbc_h[:, 2], kvbc_h[:, 3]
    dt_h = to_heads(dt_raw[0], nctx)

    handed = shifted(previous[0], "section", 1)
    stream = jnp.where(lax.axis_index("section") == 0, fresh, handed)
    x_h = to_heads(stream, nctx)

    all_ids = doc_ids[0]
    bias_h = lax.dynamic_slice_in_dim(dt_bias[0], me * heads_dev, heads_dev)
    alog_h = lax.dynamic_slice_in_dim(a_log[0], me * heads_dev, heads_dev)
    skip_h = lax.dynamic_slice_in_dim(skip_d[0], me * heads_dev, heads_dev)
    gain_h = lax.dynamic_slice_in_dim(norm_gain[0], me * part, part)

    attended = attend_heads(q_h, k_h, v_h, all_ids)

    mixer_out, sq_part = mixer_heads(x_h, dt_h, bias_h, alog_h, b_g, c_g, skip_h, all_ids)
    sq_part = sq_part[:, 0]
    sq_all = lax.all_to_all(
        jnp.broadcast_to(sq_part[None], (nctx, total)), "ctx", split_axis=0, concat_axis=0, tiled=True
    )
    mean_sq = (jnp.sum(sq_all, axis=0) / width)[:, None]
    inv_rms = lax.rsqrt(mean_sq + norm_eps)
    mixed = (
        x_h.astype(jnp.float32) + mixer_out * inv_rms * gain_h.astype(jnp.float32)[None, :]
    ).astype(jnp.bfloat16)
    out_h = (mixed.astype(jnp.float32) + attended.astype(jnp.float32)).astype(jnp.bfloat16)
    return to_rows(out_h, nctx)[None]


def solution(mesh):
    in_specs = (
        P("section", "ctx", None),
        P("ctx", None),
        P("section", "ctx", None),
        P("section", None),
        P("section", None),
        P("section", "ctx", None),
        P("section", "ctx", None),
        P("section", None),
        P("section", None),
        P("section", "ctx", None),
        P("section", "ctx", None),
        P("section", "ctx", None),
        P("section", None),
    )
    out_specs = P("section", "ctx", None)
    return jax.shard_map(body, mesh=mesh, in_specs=in_specs, out_specs=out_specs, check_vma=False)
```

```python
import math

import jax
import jax.numpy as jnp
from jax import lax
from jax.experimental import pallas as pl
from jax.experimental.pallas import tpu as pltpu
from jax.sharding import PartitionSpec as P

HEAD_A = 128
STATE = 128
GROUPS = 8
BLOCK = 128
MOST_DOC = 512
Q_BLOCK = 256


norm_eps = 1e-05


def shifted(value, axis, by):
    peers = lax.axis_size(axis)
    pairs = [(i, i + by) for i in range(peers) if 0 <= i + by < peers]
    return lax.ppermute(value, axis, pairs)


def to_heads(row, chunks):
    tok_rows = row.shape[0]
    width = row.shape[1] // chunks
    lead = row.reshape(tok_rows, chunks, width).transpose(1, 0, 2)
    moved = lax.all_to_all(lead, "ctx", split_axis=0, concat_axis=0, tiled=True)
    return moved.reshape(tok_rows * chunks, width)


def to_rows(block, chunks):
    total, width = block.shape
    tok_rows = total // chunks
    moved = lax.all_to_all(block.reshape(chunks, tok_rows, width), "ctx", split_axis=0, concat_axis=0, tiled=True)
    return moved.transpose(1, 0, 2).reshape(tok_rows, chunks * width)


def mixer_heads(x_h, dt_h, bias_h, alog_h, b_g, c_g, skip_h, all_ids, interpret=False):
    total, x_width = x_h.shape
    heads = dt_h.shape[1]
    head_dim = x_width // heads
    nblk = total // BLOCK
    step = jax.nn.softplus(dt_h + bias_h[None, :])
    log_rate = -step * jnp.exp(alog_h)[None, :]
    log_cum = jnp.cumsum(log_rate.reshape(nblk, BLOCK, heads), axis=1)
    st = step.reshape(nblk, BLOCK, heads)
    ids = all_ids.reshape(nblk, BLOCK)
    last_id = ids[:, -1]
    prev_last = jnp.concatenate([jnp.full((1,), -1, ids.dtype), last_id[:-1]])
    edge_valid = (ids == prev_last[:, None]).astype(jnp.float32)
    carry_scale = jnp.exp(log_cum) * edge_valid[:, :, None]
    end_scale = (
        jnp.exp(log_cum[:, -1:, :] - log_cum) * st * (ids == last_id[:, None]).astype(jnp.float32)[:, :, None]
    )
    edge_match = (ids[:, 0] == prev_last).astype(jnp.float32)
    block_gain = jnp.exp(log_cum[:, -1, :]) * (ids[:, 0] == last_id).astype(jnp.float32)[:, None]
    block_gain = block_gain * edge_match[:, None]
    gain_rows = jnp.broadcast_to(block_gain[:, :, None], (nblk, heads, STATE))
    lc_rows = log_cum.transpose(0, 2, 1)
    st_rows = st.transpose(0, 2, 1)
    x_t = x_h.T

    def kernel(x_ref, xt_ref, b_ref, c_ref, lcc_ref, lcr_ref, str_ref, csc_ref, esc_ref, gain_ref,
               idc_ref, idr_ref, skip_ref, o_ref, sq_ref, carry_ref):
        @pl.when(pl.program_id(0) == 0)
        def _():
            carry_ref[...] = jnp.zeros(carry_ref.shape, carry_ref.dtype)

        b_blk = b_ref[...]
        c_blk = c_ref[...]
        inner_cb = lax.dot_general(c_blk, b_blk, (((1,), (1,)), ((), ())), preferred_element_type=jnp.float32)
        rows_at = lax.broadcasted_iota(jnp.int32, (BLOCK, BLOCK), 0)
        cols_at = lax.broadcasted_iota(jnp.int32, (BLOCK, BLOCK), 1)
        same_doc = (idc_ref[...] == idr_ref[0]) & (rows_at >= cols_at)
        b_f32 = b_blk.astype(jnp.float32)
        sq = jnp.zeros((BLOCK, 1), jnp.float32)
        for h in range(heads):
            cols = slice(h * head_dim, (h + 1) * head_dim)
            lc_c = lcc_ref[0, :, h:h + 1]
            lc_r = lcr_ref[0, h:h + 1, :]
            decay = jnp.where(same_doc, jnp.exp(lc_c - lc_r), 0.0)
            intra_w = (decay * inner_cb * str_ref[0, h:h + 1, :]).astype(jnp.bfloat16)
            xh = x_ref[:, cols]
            local = jnp.dot(intra_w, xh, preferred_element_type=jnp.float32)
            state_bf = carry_ref[h].astype(jnp.bfloat16)
            carried = lax.dot_general(
                c_blk, state_bf, (((1,), (1,)), ((), ())), preferred_element_type=jnp.float32
            )
            carried = carried * csc_ref[0, :, h:h + 1]
            out = local + carried + skip_ref[h] * xh.astype(jnp.float32)
            o_ref[:, cols] = out
            sq = sq + jnp.sum(out * out, axis=1, keepdims=True)
            end_w = (esc_ref[0, :, h:h + 1] * b_f32).astype(jnp.bfloat16)
            block_state = jnp.dot(xt_ref[cols, :], end_w, preferred_element_type=jnp.float32)
            carry_ref[h] = gain_ref[0, h:h + 1, :] * carry_ref[h] + block_state
        sq_ref[...] = sq

    per_block = lambda shape: pl.BlockSpec((1,) + shape, lambda i: (i, 0, 0))
    return pl.pallas_call(
        kernel,
        grid=(nblk,),
        in_specs=[
            pl.BlockSpec((BLOCK, x_width), lambda i: (i, 0)),
            pl.BlockSpec((x_width, BLOCK), lambda i: (0, i)),
            pl.BlockSpec((BLOCK, STATE), lambda i: (i, 0)),
            pl.BlockSpec((BLOCK, STATE), lambda i: (i, 0)),
            per_block((BLOCK, heads)),
            per_block((heads, BLOCK)),
            per_block((heads, BLOCK)),
            per_block((BLOCK, heads)),
            per_block((BLOCK, heads)),
            per_block((heads, STATE)),
            pl.BlockSpec((BLOCK, 1), lambda i: (i, 0)),
            per_block((1, BLOCK)),
            pl.BlockSpec(memory_space=pltpu.SMEM),
        ],
        out_specs=[
            pl.BlockSpec((BLOCK, x_width), lambda i: (i, 0)),
            pl.BlockSpec((BLOCK, 1), lambda i: (i, 0)),
        ],
        out_shape=[
            jax.ShapeDtypeStruct((total, x_width), jnp.float32),
            jax.ShapeDtypeStruct((total, 1), jnp.float32),
        ],
        scratch_shapes=[pltpu.VMEM((heads, head_dim, STATE), jnp.float32)],
        compiler_params=pltpu.CompilerParams(dimension_semantics=("arbitrary",)),
        interpret=interpret,
    )(
        x_h, x_t, b_g, c_g, log_cum, lc_rows, st_rows, carry_scale, end_scale, gain_rows,
        all_ids.reshape(total, 1), ids.reshape(nblk, 1, BLOCK), skip_h,
    )


def attend_rows(q_row, kv_win, ids_q, ids_k, interpret=False):
    tok_rows, q_width = q_row.shape
    window = kv_win.shape[0]
    kv_heads = kv_win.shape[1] // (2 * HEAD_A)
    group = q_width // HEAD_A // kv_heads
    lead = window - tok_rows
    inv_sqrt = 1.0 / math.sqrt(HEAD_A)

    def kernel(q_ref, k_ref, v_ref, iq_ref, ik_ref, o_ref):
        q_at = lead + lax.broadcasted_iota(jnp.int32, (tok_rows, window), 0)
        k_at = lax.broadcasted_iota(jnp.int32, (tok_rows, window), 1)
        allowed = (iq_ref[...] == ik_ref[...]) & (q_at >= k_at)
        kb = k_ref[...]
        vb = v_ref[...]
        for g in range(group):
            cols = slice(g * HEAD_A, (g + 1) * HEAD_A)
            logits = lax.dot_general(
                q_ref[:, cols], kb, (((1,), (1,)), ((), ())), preferred_element_type=jnp.float32
            ) * inv_sqrt
            logits = jnp.where(allowed, logits, -jnp.inf)
            row_max = jnp.max(logits, axis=1, keepdims=True)
            exp_terms = jnp.exp(logits - row_max)
            probs = (exp_terms / jnp.sum(exp_terms, axis=1, keepdims=True)).astype(jnp.bfloat16)
            o_ref[:, cols] = jnp.dot(probs, vb, preferred_element_type=jnp.float32).astype(o_ref.dtype)

    return pl.pallas_call(
        kernel,
        grid=(kv_heads,),
        in_specs=[
            pl.BlockSpec((tok_rows, group * HEAD_A), lambda i: (0, i)),
            pl.BlockSpec((window, HEAD_A), lambda i: (0, i)),
            pl.BlockSpec((window, HEAD_A), lambda i: (0, kv_heads + i)),
            pl.BlockSpec((tok_rows, 1), lambda i: (0, 0)),
            pl.BlockSpec((1, window), lambda i: (0, 0)),
        ],
        out_specs=pl.BlockSpec((tok_rows, group * HEAD_A), lambda i: (0, i)),
        out_shape=jax.ShapeDtypeStruct((tok_rows, q_width), jnp.bfloat16),
        interpret=interpret,
    )(q_row, kv_win, kv_win, ids_q, ids_k)


def body(
    previous,
    fresh,
    dt_raw,
    dt_bias,
    a_log,
    b_in,
    c_in,
    skip_d,
    norm_gain,
    queries,
    keys,
    values,
    doc_ids,
):
    tok_rows, width = fresh.shape
    nctx = lax.axis_size("ctx")
    me = lax.axis_index("ctx")
    total = tok_rows * nctx
    part = width // nctx
    mamba_heads = dt_raw.shape[2]
    heads_dev = mamba_heads // nctx
    head_dim = width // mamba_heads
    kv_heads = keys.shape[2] // HEAD_A
    qpd = part // HEAD_A

    rep = nctx // kv_heads
    bc = jnp.stack(
        [b_in[0].reshape(tok_rows, GROUPS, STATE), c_in[0].reshape(tok_rows, GROUPS, STATE)], axis=2
    )
    bc_h = to_heads(jnp.repeat(bc, rep, axis=1).reshape(tok_rows, nctx * 2 * STATE), nctx)
    b_g, c_g = bc_h[:, :STATE], bc_h[:, STATE:]
    dt_h = to_heads(dt_raw[0], nctx)

    handed = shifted(previous[0], "section", 1)
    stream = jnp.where(lax.axis_index("section") == 0, fresh, handed)
    x_h = to_heads(stream, nctx)

    halo = -(-MOST_DOC // tok_rows)
    kv_row = jnp.concatenate([keys[0], values[0]], axis=1)
    kv_win = jnp.concatenate([shifted(kv_row, "ctx", by) for by in range(halo, 0, -1)] + [kv_row], axis=0)
    all_ids = doc_ids[0]
    lead = halo * tok_rows
    padded_ids = jnp.concatenate([jnp.full((lead,), -1, all_ids.dtype), all_ids])
    ids_k = lax.dynamic_slice_in_dim(padded_ids, me * tok_rows, lead + tok_rows)
    ids_q = lax.dynamic_slice_in_dim(all_ids, me * tok_rows, tok_rows)
    attended = attend_rows(queries[0], kv_win, ids_q.reshape(tok_rows, 1), ids_k.reshape(1, lead + tok_rows))

    bias_h = lax.dynamic_slice_in_dim(dt_bias[0], me * heads_dev, heads_dev)
    alog_h = lax.dynamic_slice_in_dim(a_log[0], me * heads_dev, heads_dev)
    skip_h = lax.dynamic_slice_in_dim(skip_d[0], me * heads_dev, heads_dev)
    gain_h = lax.dynamic_slice_in_dim(norm_gain[0], me * part, part)

    mixer_out, sq_part = mixer_heads(x_h, dt_h, bias_h, alog_h, b_g, c_g, skip_h, all_ids)
    sq_all = lax.all_to_all(
        jnp.broadcast_to(sq_part[:, 0][None], (nctx, total)), "ctx", split_axis=0, concat_axis=0, tiled=True
    )
    mean_sq = (jnp.sum(sq_all, axis=0) / width)[:, None]
    inv_rms = lax.rsqrt(mean_sq + norm_eps)
    mixed = (
        x_h.astype(jnp.float32) + mixer_out * inv_rms * gain_h.astype(jnp.float32)[None, :]
    ).astype(jnp.bfloat16)
    mixed_rows = to_rows(mixed, nctx)
    return (mixed_rows.astype(jnp.float32) + attended.astype(jnp.float32)).astype(jnp.bfloat16)[None]


def solution(mesh):
    in_specs = (
        P("section", "ctx", None),
        P("ctx", None),
        P("section", "ctx", None),
        P("section", None),
        P("section", None),
        P("section", "ctx", None),
        P("section", "ctx", None),
        P("section", None),
        P("section", None),
        P("section", "ctx", None),
        P("section", "ctx", None),
        P("section", "ctx", None),
        P("section", None),
    )
    out_specs = P("section", "ctx", None)
    return jax.shard_map(body, mesh=mesh, in_specs=in_specs, out_specs=out_specs, check_vma=False)
```

```python
import math

import jax
import jax.numpy as jnp
from jax import lax
from jax.experimental import pallas as pl
from jax.experimental.pallas import tpu as pltpu
from jax.sharding import PartitionSpec as P

HEAD_A = 128
STATE = 128
GROUPS = 8
BLOCK = 128
MOST_DOC = 512
Q_BLOCK = 256


norm_eps = 1e-05


def shifted(value, axis, by):
    peers = lax.axis_size(axis)
    pairs = [(i, i + by) for i in range(peers) if 0 <= i + by < peers]
    return lax.ppermute(value, axis, pairs)


def to_heads(row, chunks):
    tok_rows = row.shape[0]
    width = row.shape[1] // chunks
    lead = row.reshape(tok_rows, chunks, width).transpose(1, 0, 2)
    moved = lax.all_to_all(lead, "ctx", split_axis=0, concat_axis=0, tiled=True)
    return moved.reshape(tok_rows * chunks, width)


def to_rows(block, chunks):
    total, width = block.shape
    tok_rows = total // chunks
    moved = lax.all_to_all(block.reshape(chunks, tok_rows, width), "ctx", split_axis=0, concat_axis=0, tiled=True)
    return moved.transpose(1, 0, 2).reshape(tok_rows, chunks * width)


def mixer_heads(x_h, dt_h, bias_h, alog_h, b_g, c_g, skip_h, all_ids, interpret=False):
    total, x_width = x_h.shape
    heads = dt_h.shape[1]
    head_dim = x_width // heads
    nblk = total // BLOCK
    step = jax.nn.softplus(dt_h + bias_h[None, :])
    log_rate = -step * jnp.exp(alog_h)[None, :]
    log_cum = jnp.cumsum(log_rate.reshape(nblk, BLOCK, heads), axis=1)
    st = step.reshape(nblk, BLOCK, heads)
    ids = all_ids.reshape(nblk, BLOCK)
    last_id = ids[:, -1]
    prev_last = jnp.concatenate([jnp.full((1,), -1, ids.dtype), last_id[:-1]])
    edge_valid = (ids == prev_last[:, None]).astype(jnp.float32)
    carry_scale = jnp.exp(log_cum) * edge_valid[:, :, None]
    end_scale = (
        jnp.exp(log_cum[:, -1:, :] - log_cum) * st * (ids == last_id[:, None]).astype(jnp.float32)[:, :, None]
    )
    edge_match = (ids[:, 0] == prev_last).astype(jnp.float32)
    block_gain = jnp.exp(log_cum[:, -1, :]) * (ids[:, 0] == last_id).astype(jnp.float32)[:, None]
    block_gain = block_gain * edge_match[:, None]
    gain_rows = jnp.broadcast_to(block_gain[:, :, None], (nblk, heads, STATE))
    lc_rows = log_cum.transpose(0, 2, 1)
    st_rows = st.transpose(0, 2, 1)
    x_t = x_h.T

    def kernel(x_ref, xt_ref, b_ref, c_ref, lcc_ref, lcr_ref, str_ref, csc_ref, esc_ref, gain_ref,
               idc_ref, idr_ref, skip_ref, o_ref, sq_ref, carry_ref):
        @pl.when(pl.program_id(0) == 0)
        def _():
            carry_ref[...] = jnp.zeros(carry_ref.shape, carry_ref.dtype)

        b_blk = b_ref[...]
        c_blk = c_ref[...]
        inner_cb = lax.dot_general(c_blk, b_blk, (((1,), (1,)), ((), ())), preferred_element_type=jnp.float32)
        rows_at = lax.broadcasted_iota(jnp.int32, (BLOCK, BLOCK), 0)
        cols_at = lax.broadcasted_iota(jnp.int32, (BLOCK, BLOCK), 1)
        same_doc = (idc_ref[...] == idr_ref[0]) & (rows_at >= cols_at)
        b_f32 = b_blk.astype(jnp.float32)
        sq = jnp.zeros((BLOCK, 1), jnp.float32)
        for h in range(heads):
            cols = slice(h * head_dim, (h + 1) * head_dim)
            lc_c = lcc_ref[0, :, h:h + 1]
            lc_r = lcr_ref[0, h:h + 1, :]
            decay = jnp.where(same_doc, jnp.exp(lc_c - lc_r), 0.0)
            intra_w = (decay * inner_cb * str_ref[0, h:h + 1, :]).astype(jnp.bfloat16)
            xh = x_ref[:, cols]
            local = jnp.dot(intra_w, xh, preferred_element_type=jnp.float32)
            state_bf = carry_ref[h].astype(jnp.bfloat16)
            carried = lax.dot_general(
                c_blk, state_bf, (((1,), (1,)), ((), ())), preferred_element_type=jnp.float32
            )
            carried = carried * csc_ref[0, :, h:h + 1]
            out = local + carried + skip_ref[h] * xh.astype(jnp.float32)
            o_ref[:, cols] = out
            sq = sq + jnp.sum(out * out, axis=1, keepdims=True)
            end_w = (esc_ref[0, :, h:h + 1] * b_f32).astype(jnp.bfloat16)
            block_state = jnp.dot(xt_ref[cols, :], end_w, preferred_element_type=jnp.float32)
            carry_ref[h] = gain_ref[0, h:h + 1, :] * carry_ref[h] + block_state
        sq_ref[...] = sq

    per_block = lambda shape: pl.BlockSpec((1,) + shape, lambda i: (i, 0, 0))
    return pl.pallas_call(
        kernel,
        grid=(nblk,),
        in_specs=[
            pl.BlockSpec((BLOCK, x_width), lambda i: (i, 0)),
            pl.BlockSpec((x_width, BLOCK), lambda i: (0, i)),
            pl.BlockSpec((BLOCK, STATE), lambda i: (i, 0)),
            pl.BlockSpec((BLOCK, STATE), lambda i: (i, 0)),
            per_block((BLOCK, heads)),
            per_block((heads, BLOCK)),
            per_block((heads, BLOCK)),
            per_block((BLOCK, heads)),
            per_block((BLOCK, heads)),
            per_block((heads, STATE)),
            pl.BlockSpec((BLOCK, 1), lambda i: (i, 0)),
            per_block((1, BLOCK)),
            pl.BlockSpec(memory_space=pltpu.SMEM),
        ],
        out_specs=[
            pl.BlockSpec((BLOCK, x_width), lambda i: (i, 0)),
            pl.BlockSpec((BLOCK, 1), lambda i: (i, 0)),
        ],
        out_shape=[
            jax.ShapeDtypeStruct((total, x_width), jnp.float32),
            jax.ShapeDtypeStruct((total, 1), jnp.float32),
        ],
        scratch_shapes=[pltpu.VMEM((heads, head_dim, STATE), jnp.float32)],
        compiler_params=pltpu.CompilerParams(dimension_semantics=("arbitrary",)),
        interpret=interpret,
    )(
        x_h, x_t, b_g, c_g, log_cum, lc_rows, st_rows, carry_scale, end_scale, gain_rows,
        all_ids.reshape(total, 1), ids.reshape(nblk, 1, BLOCK), skip_h,
    )


def attend_rows(q_row, kv_win, ids_q, ids_k, interpret=False):
    tok_rows, q_width = q_row.shape
    window = kv_win.shape[0]
    kv_heads = kv_win.shape[1] // (2 * HEAD_A)
    group = q_width // HEAD_A // kv_heads
    lead = window - tok_rows
    inv_sqrt = 1.0 / math.sqrt(HEAD_A)

    def kernel(q_ref, k_ref, v_ref, iq_ref, ik_ref, o_ref):
        q_at = lead + lax.broadcasted_iota(jnp.int32, (tok_rows, window), 0)
        k_at = lax.broadcasted_iota(jnp.int32, (tok_rows, window), 1)
        allowed = (iq_ref[...] == ik_ref[...]) & (q_at >= k_at)
        kb = k_ref[...]
        vb = v_ref[...]
        for g in range(group):
            cols = slice(g * HEAD_A, (g + 1) * HEAD_A)
            logits = lax.dot_general(
                q_ref[:, cols], kb, (((1,), (1,)), ((), ())), preferred_element_type=jnp.float32
            ) * inv_sqrt
            logits = jnp.where(allowed, logits, -jnp.inf)
            row_max = jnp.max(logits, axis=1, keepdims=True)
            exp_terms = jnp.exp(logits - row_max)
            probs = (exp_terms / jnp.sum(exp_terms, axis=1, keepdims=True)).astype(jnp.bfloat16)
            o_ref[:, cols] = jnp.dot(probs, vb, preferred_element_type=jnp.float32).astype(o_ref.dtype)

    return pl.pallas_call(
        kernel,
        grid=(kv_heads,),
        in_specs=[
            pl.BlockSpec((tok_rows, group * HEAD_A), lambda i: (0, i)),
            pl.BlockSpec((window, HEAD_A), lambda i: (0, i)),
            pl.BlockSpec((window, HEAD_A), lambda i: (0, kv_heads + i)),
            pl.BlockSpec((tok_rows, 1), lambda i: (0, 0)),
            pl.BlockSpec((1, window), lambda i: (0, 0)),
        ],
        out_specs=pl.BlockSpec((tok_rows, group * HEAD_A), lambda i: (0, i)),
        out_shape=jax.ShapeDtypeStruct((tok_rows, q_width), jnp.bfloat16),
        interpret=interpret,
    )(q_row, kv_win, kv_win, ids_q, ids_k)


def body(
    previous,
    fresh,
    dt_raw,
    dt_bias,
    a_log,
    b_in,
    c_in,
    skip_d,
    norm_gain,
    queries,
    keys,
    values,
    doc_ids,
):
    tok_rows, width = fresh.shape
    nctx = lax.axis_size("ctx")
    me = lax.axis_index("ctx")
    total = tok_rows * nctx
    part = width // nctx
    mamba_heads = dt_raw.shape[2]
    heads_dev = mamba_heads // nctx
    head_dim = width // mamba_heads
    kv_heads = keys.shape[2] // HEAD_A
    qpd = part // HEAD_A

    rep = nctx // kv_heads
    bc = jnp.stack(
        [b_in[0].reshape(tok_rows, GROUPS, STATE), c_in[0].reshape(tok_rows, GROUPS, STATE)], axis=2
    )
    bc_h = to_heads(jnp.repeat(bc, rep, axis=1).reshape(tok_rows, nctx * 2 * STATE), nctx)
    b_g, c_g = bc_h[:, :STATE], bc_h[:, STATE:]
    dt_h = to_heads(dt_raw[0], nctx)

    handed = shifted(previous[0], "section", 1)
    stream = jnp.where(lax.axis_index("section") == 0, fresh, handed)
    x_h = to_heads(stream, nctx)

    halo = -(-MOST_DOC // tok_rows)
    kv_row = jnp.concatenate([keys[0], values[0]], axis=1)
    kv_win = jnp.concatenate([shifted(kv_row, "ctx", by) for by in range(halo, 0, -1)] + [kv_row], axis=0)
    kv_win, x_h = lax.optimization_barrier((kv_win, x_h))
    all_ids = doc_ids[0]
    lead = halo * tok_rows
    padded_ids = jnp.concatenate([jnp.full((lead,), -1, all_ids.dtype), all_ids])
    ids_k = lax.dynamic_slice_in_dim(padded_ids, me * tok_rows, lead + tok_rows)
    ids_q = lax.dynamic_slice_in_dim(all_ids, me * tok_rows, tok_rows)
    attended = attend_rows(queries[0], kv_win, ids_q.reshape(tok_rows, 1), ids_k.reshape(1, lead + tok_rows))

    bias_h = lax.dynamic_slice_in_dim(dt_bias[0], me * heads_dev, heads_dev)
    alog_h = lax.dynamic_slice_in_dim(a_log[0], me * heads_dev, heads_dev)
    skip_h = lax.dynamic_slice_in_dim(skip_d[0], me * heads_dev, heads_dev)
    gain_h = lax.dynamic_slice_in_dim(norm_gain[0], me * part, part)

    mixer_out, sq_part = mixer_heads(x_h, dt_h, bias_h, alog_h, b_g, c_g, skip_h, all_ids)
    sq_all = lax.all_to_all(
        jnp.broadcast_to(sq_part[:, 0][None], (nctx, total)), "ctx", split_axis=0, concat_axis=0, tiled=True
    )
    mean_sq = (jnp.sum(sq_all, axis=0) / width)[:, None]
    inv_rms = lax.rsqrt(mean_sq + norm_eps)
    mixed = (
        x_h.astype(jnp.float32) + mixer_out * inv_rms * gain_h.astype(jnp.float32)[None, :]
    ).astype(jnp.bfloat16)
    mixed_rows = to_rows(mixed, nctx)
    return (mixed_rows.astype(jnp.float32) + attended.astype(jnp.float32)).astype(jnp.bfloat16)[None]


def solution(mesh):
    in_specs = (
        P("section", "ctx", None),
        P("ctx", None),
        P("section", "ctx", None),
        P("section", None),
        P("section", None),
        P("section", "ctx", None),
        P("section", "ctx", None),
        P("section", None),
        P("section", None),
        P("section", "ctx", None),
        P("section", "ctx", None),
        P("section", "ctx", None),
        P("section", None),
    )
    out_specs = P("section", "ctx", None)
    return jax.shard_map(body, mesh=mesh, in_specs=in_specs, out_specs=out_specs, check_vma=False)
```

```python
import math

import jax
import jax.numpy as jnp
from jax import lax
from jax.experimental import pallas as pl
from jax.experimental.pallas import tpu as pltpu
from jax.sharding import PartitionSpec as P

HEAD_A = 128
STATE = 128
GROUPS = 8
BLOCK = 128
MOST_DOC = 512
Q_BLOCK = 256


norm_eps = 1e-05


def shifted(value, axis, by):
    peers = lax.axis_size(axis)
    pairs = [(i, i + by) for i in range(peers) if 0 <= i + by < peers]
    return lax.ppermute(value, axis, pairs)


def to_heads(row, chunks):
    tok_rows = row.shape[0]
    width = row.shape[1] // chunks
    lead = row.reshape(tok_rows, chunks, width).transpose(1, 0, 2)
    moved = lax.all_to_all(lead, "ctx", split_axis=0, concat_axis=0, tiled=True)
    return moved.reshape(tok_rows * chunks, width)


def to_rows(block, chunks):
    total, width = block.shape
    tok_rows = total // chunks
    moved = lax.all_to_all(block.reshape(chunks, tok_rows, width), "ctx", split_axis=0, concat_axis=0, tiled=True)
    return moved.transpose(1, 0, 2).reshape(tok_rows, chunks * width)


def mixer_heads(x_h, dt_h, bias_h, alog_h, b_g, c_g, skip_h, all_ids, interpret=False):
    total, x_width = x_h.shape
    heads = dt_h.shape[1]
    head_dim = x_width // heads
    nblk = total // BLOCK
    step = jax.nn.softplus(dt_h + bias_h[None, :])
    log_rate = -step * jnp.exp(alog_h)[None, :]
    log_cum = jnp.cumsum(log_rate.reshape(nblk, BLOCK, heads), axis=1)
    st = step.reshape(nblk, BLOCK, heads)
    ids = all_ids.reshape(nblk, BLOCK)
    last_id = ids[:, -1]
    prev_last = jnp.concatenate([jnp.full((1,), -1, ids.dtype), last_id[:-1]])
    edge_valid = (ids == prev_last[:, None]).astype(jnp.float32)
    carry_scale = jnp.exp(log_cum) * edge_valid[:, :, None]
    end_scale = (
        jnp.exp(log_cum[:, -1:, :] - log_cum) * st * (ids == last_id[:, None]).astype(jnp.float32)[:, :, None]
    )
    edge_match = (ids[:, 0] == prev_last).astype(jnp.float32)
    block_gain = jnp.exp(log_cum[:, -1, :]) * (ids[:, 0] == last_id).astype(jnp.float32)[:, None]
    block_gain = block_gain * edge_match[:, None]
    gain_rows = jnp.broadcast_to(block_gain[:, :, None], (nblk, heads, STATE))
    lc_rows = log_cum.transpose(0, 2, 1)
    st_rows = st.transpose(0, 2, 1)
    x_t = x_h.T

    def kernel(x_ref, xt_ref, b_ref, c_ref, lcc_ref, lcr_ref, str_ref, csc_ref, esc_ref, gain_ref,
               idc_ref, idr_ref, skip_ref, o_ref, sq_ref, carry_ref):
        @pl.when(pl.program_id(0) == 0)
        def _():
            carry_ref[...] = jnp.zeros(carry_ref.shape, carry_ref.dtype)

        b_blk = b_ref[...]
        c_blk = c_ref[...]
        inner_cb = lax.dot_general(c_blk, b_blk, (((1,), (1,)), ((), ())), preferred_element_type=jnp.float32)
        rows_at = lax.broadcasted_iota(jnp.int32, (BLOCK, BLOCK), 0)
        cols_at = lax.broadcasted_iota(jnp.int32, (BLOCK, BLOCK), 1)
        same_doc = (idc_ref[...] == idr_ref[0]) & (rows_at >= cols_at)
        b_f32 = b_blk.astype(jnp.float32)
        sq = jnp.zeros((BLOCK, 1), jnp.float32)
        for h in range(heads):
            cols = slice(h * head_dim, (h + 1) * head_dim)
            lc_c = lcc_ref[0, :, h:h + 1]
            lc_r = lcr_ref[0, h:h + 1, :]
            decay = jnp.where(same_doc, jnp.exp(lc_c - lc_r), 0.0)
            intra_w = (decay * inner_cb * str_ref[0, h:h + 1, :]).astype(jnp.bfloat16)
            xh = x_ref[:, cols]
            local = jnp.dot(intra_w, xh, preferred_element_type=jnp.float32)
            state_bf = carry_ref[h].astype(jnp.bfloat16)
            carried = lax.dot_general(
                c_blk, state_bf, (((1,), (1,)), ((), ())), preferred_element_type=jnp.float32
            )
            carried = carried * csc_ref[0, :, h:h + 1]
            out = local + carried + skip_ref[h] * xh.astype(jnp.float32)
            o_ref[:, cols] = out
            sq = sq + jnp.sum(out * out, axis=1, keepdims=True)
            end_w = (esc_ref[0, :, h:h + 1] * b_f32).astype(jnp.bfloat16)
            block_state = jnp.dot(xt_ref[cols, :], end_w, preferred_element_type=jnp.float32)
            carry_ref[h] = gain_ref[0, h:h + 1, :] * carry_ref[h] + block_state
        sq_ref[...] = sq

    per_block = lambda shape: pl.BlockSpec((1,) + shape, lambda i: (i, 0, 0))
    return pl.pallas_call(
        kernel,
        grid=(nblk,),
        in_specs=[
            pl.BlockSpec((BLOCK, x_width), lambda i: (i, 0)),
            pl.BlockSpec((x_width, BLOCK), lambda i: (0, i)),
            pl.BlockSpec((BLOCK, STATE), lambda i: (i, 0)),
            pl.BlockSpec((BLOCK, STATE), lambda i: (i, 0)),
            per_block((BLOCK, heads)),
            per_block((heads, BLOCK)),
            per_block((heads, BLOCK)),
            per_block((BLOCK, heads)),
            per_block((BLOCK, heads)),
            per_block((heads, STATE)),
            pl.BlockSpec((BLOCK, 1), lambda i: (i, 0)),
            per_block((1, BLOCK)),
            pl.BlockSpec(memory_space=pltpu.SMEM),
        ],
        out_specs=[
            pl.BlockSpec((BLOCK, x_width), lambda i: (i, 0)),
            pl.BlockSpec((BLOCK, 1), lambda i: (i, 0)),
        ],
        out_shape=[
            jax.ShapeDtypeStruct((total, x_width), jnp.float32),
            jax.ShapeDtypeStruct((total, 1), jnp.float32),
        ],
        scratch_shapes=[pltpu.VMEM((heads, head_dim, STATE), jnp.float32)],
        compiler_params=pltpu.CompilerParams(dimension_semantics=("arbitrary",)),
        interpret=interpret,
    )(
        x_h, x_t, b_g, c_g, log_cum, lc_rows, st_rows, carry_scale, end_scale, gain_rows,
        all_ids.reshape(total, 1), ids.reshape(nblk, 1, BLOCK), skip_h,
    )


def attend_rows(q_row, kv_win, ids_q, ids_k, interpret=False):
    tok_rows, q_width = q_row.shape
    window = kv_win.shape[0]
    kv_heads = kv_win.shape[1] // (2 * HEAD_A)
    group = q_width // HEAD_A // kv_heads
    lead = window - tok_rows
    inv_sqrt = 1.0 / math.sqrt(HEAD_A)

    def kernel(q_ref, k_ref, v_ref, iq_ref, ik_ref, o_ref):
        q_at = lead + lax.broadcasted_iota(jnp.int32, (tok_rows, window), 0)
        k_at = lax.broadcasted_iota(jnp.int32, (tok_rows, window), 1)
        allowed = (iq_ref[...] == ik_ref[...]) & (q_at >= k_at)
        kb = k_ref[...]
        vb = v_ref[...]
        for g in range(group):
            cols = slice(g * HEAD_A, (g + 1) * HEAD_A)
            logits = lax.dot_general(
                q_ref[:, cols], kb, (((1,), (1,)), ((), ())), preferred_element_type=jnp.float32
            ) * inv_sqrt
            logits = jnp.where(allowed, logits, -jnp.inf)
            row_max = jnp.max(logits, axis=1, keepdims=True)
            exp_terms = jnp.exp(logits - row_max)
            probs = (exp_terms / jnp.sum(exp_terms, axis=1, keepdims=True)).astype(jnp.bfloat16)
            o_ref[:, cols] = jnp.dot(probs, vb, preferred_element_type=jnp.float32).astype(o_ref.dtype)

    return pl.pallas_call(
        kernel,
        grid=(kv_heads,),
        in_specs=[
            pl.BlockSpec((tok_rows, group * HEAD_A), lambda i: (0, i)),
            pl.BlockSpec((window, HEAD_A), lambda i: (0, i)),
            pl.BlockSpec((window, HEAD_A), lambda i: (0, kv_heads + i)),
            pl.BlockSpec((tok_rows, 1), lambda i: (0, 0)),
            pl.BlockSpec((1, window), lambda i: (0, 0)),
        ],
        out_specs=pl.BlockSpec((tok_rows, group * HEAD_A), lambda i: (0, i)),
        out_shape=jax.ShapeDtypeStruct((tok_rows, q_width), jnp.bfloat16),
        interpret=interpret,
    )(q_row, kv_win, kv_win, ids_q, ids_k)


def body(
    previous,
    fresh,
    dt_raw,
    dt_bias,
    a_log,
    b_in,
    c_in,
    skip_d,
    norm_gain,
    queries,
    keys,
    values,
    doc_ids,
):
    tok_rows, width = fresh.shape
    nctx = lax.axis_size("ctx")
    me = lax.axis_index("ctx")
    total = tok_rows * nctx
    part = width // nctx
    mamba_heads = dt_raw.shape[2]
    heads_dev = mamba_heads // nctx
    head_dim = width // mamba_heads
    kv_heads = keys.shape[2] // HEAD_A
    qpd = part // HEAD_A

    rep = nctx // kv_heads
    bc = jnp.stack(
        [b_in[0].reshape(tok_rows, GROUPS, STATE), c_in[0].reshape(tok_rows, GROUPS, STATE)], axis=2
    )
    bc_h = to_heads(jnp.repeat(bc, rep, axis=1).reshape(tok_rows, nctx * 2 * STATE), nctx)
    b_g, c_g = bc_h[:, :STATE], bc_h[:, STATE:]
    dt_h = to_heads(dt_raw[0], nctx)

    handed = shifted(previous[0], "section", 1)
    stream = jnp.where(lax.axis_index("section") == 0, fresh, handed)
    x_h = to_heads(stream, nctx)

    halo = -(-MOST_DOC // tok_rows)
    kv_row = jnp.concatenate([keys[0], values[0]], axis=1)
    kv_row, x_h = lax.optimization_barrier((kv_row, x_h))
    kv_win = jnp.concatenate([shifted(kv_row, "ctx", by) for by in range(halo, 0, -1)] + [kv_row], axis=0)
    all_ids = doc_ids[0]
    lead = halo * tok_rows
    padded_ids = jnp.concatenate([jnp.full((lead,), -1, all_ids.dtype), all_ids])
    ids_k = lax.dynamic_slice_in_dim(padded_ids, me * tok_rows, lead + tok_rows)
    ids_q = lax.dynamic_slice_in_dim(all_ids, me * tok_rows, tok_rows)

    bias_h = lax.dynamic_slice_in_dim(dt_bias[0], me * heads_dev, heads_dev)
    alog_h = lax.dynamic_slice_in_dim(a_log[0], me * heads_dev, heads_dev)
    skip_h = lax.dynamic_slice_in_dim(skip_d[0], me * heads_dev, heads_dev)
    gain_h = lax.dynamic_slice_in_dim(norm_gain[0], me * part, part)

    mixer_out, sq_part = mixer_heads(x_h, dt_h, bias_h, alog_h, b_g, c_g, skip_h, all_ids)
    kv_win, mixer_out, sq_part = lax.optimization_barrier((kv_win, mixer_out, sq_part))
    attended = attend_rows(queries[0], kv_win, ids_q.reshape(tok_rows, 1), ids_k.reshape(1, lead + tok_rows))
    sq_all = lax.all_to_all(
        jnp.broadcast_to(sq_part[:, 0][None], (nctx, total)), "ctx", split_axis=0, concat_axis=0, tiled=True
    )
    mean_sq = (jnp.sum(sq_all, axis=0) / width)[:, None]
    inv_rms = lax.rsqrt(mean_sq + norm_eps)
    mixed = (
        x_h.astype(jnp.float32) + mixer_out * inv_rms * gain_h.astype(jnp.float32)[None, :]
    ).astype(jnp.bfloat16)
    mixed_rows = to_rows(mixed, nctx)
    return (mixed_rows.astype(jnp.float32) + attended.astype(jnp.float32)).astype(jnp.bfloat16)[None]


def solution(mesh):
    in_specs = (
        P("section", "ctx", None),
        P("ctx", None),
        P("section", "ctx", None),
        P("section", None),
        P("section", None),
        P("section", "ctx", None),
        P("section", "ctx", None),
        P("section", None),
        P("section", None),
        P("section", "ctx", None),
        P("section", "ctx", None),
        P("section", "ctx", None),
        P("section", None),
    )
    out_specs = P("section", "ctx", None)
    return jax.shard_map(body, mesh=mesh, in_specs=in_specs, out_specs=out_specs, check_vma=False)
```

```python
import math

import jax
import jax.numpy as jnp
from jax import lax
from jax.experimental import pallas as pl
from jax.experimental.pallas import tpu as pltpu
from jax.sharding import PartitionSpec as P

HEAD_A = 128
STATE = 128
GROUPS = 8
BLOCK = 128
MOST_DOC = 512
Q_BLOCK = 256


norm_eps = 1e-05


def shifted(value, axis, by):
    peers = lax.axis_size(axis)
    pairs = [(i, i + by) for i in range(peers) if 0 <= i + by < peers]
    return lax.ppermute(value, axis, pairs)


def to_heads(row, chunks):
    tok_rows = row.shape[0]
    width = row.shape[1] // chunks
    lead = row.reshape(tok_rows, chunks, width).transpose(1, 0, 2)
    moved = lax.all_to_all(lead, "ctx", split_axis=0, concat_axis=0, tiled=True)
    return moved.reshape(tok_rows * chunks, width)


def to_rows(block, chunks):
    total, width = block.shape
    tok_rows = total // chunks
    moved = lax.all_to_all(block.reshape(chunks, tok_rows, width), "ctx", split_axis=0, concat_axis=0, tiled=True)
    return moved.transpose(1, 0, 2).reshape(tok_rows, chunks * width)


def mixer_heads(x_h, dt_h, bias_h, alog_h, b_g, c_g, skip_h, all_ids, interpret=False):
    total, x_width = x_h.shape
    heads = dt_h.shape[1]
    head_dim = x_width // heads
    nblk = total // BLOCK
    step = jax.nn.softplus(dt_h + bias_h[None, :])
    log_rate = -step * jnp.exp(alog_h)[None, :]
    log_cum = jnp.cumsum(log_rate.reshape(nblk, BLOCK, heads), axis=1)
    st = step.reshape(nblk, BLOCK, heads)
    ids = all_ids.reshape(nblk, BLOCK)
    last_id = ids[:, -1]
    prev_last = jnp.concatenate([jnp.full((1,), -1, ids.dtype), last_id[:-1]])
    edge_valid = (ids == prev_last[:, None]).astype(jnp.float32)
    carry_scale = jnp.exp(log_cum) * edge_valid[:, :, None]
    end_scale = (
        jnp.exp(log_cum[:, -1:, :] - log_cum) * st * (ids == last_id[:, None]).astype(jnp.float32)[:, :, None]
    )
    edge_match = (ids[:, 0] == prev_last).astype(jnp.float32)
    block_gain = jnp.exp(log_cum[:, -1, :]) * (ids[:, 0] == last_id).astype(jnp.float32)[:, None]
    block_gain = block_gain * edge_match[:, None]
    gain_rows = jnp.broadcast_to(block_gain[:, :, None], (nblk, heads, head_dim))
    lc_rows = log_cum.transpose(0, 2, 1)
    st_rows = st.transpose(0, 2, 1)

    def kernel(x_ref, b_ref, c_ref, lcc_ref, lcr_ref, str_ref, csc_ref, esc_ref, gain_ref,
               idc_ref, idr_ref, skip_ref, o_ref, sq_ref, carry_ref):
        @pl.when(pl.program_id(0) == 0)
        def _():
            carry_ref[...] = jnp.zeros(carry_ref.shape, carry_ref.dtype)

        b_blk = b_ref[...]
        c_blk = c_ref[...]
        inner_cb = lax.dot_general(c_blk, b_blk, (((1,), (1,)), ((), ())), preferred_element_type=jnp.float32)
        rows_at = lax.broadcasted_iota(jnp.int32, (BLOCK, BLOCK), 0)
        cols_at = lax.broadcasted_iota(jnp.int32, (BLOCK, BLOCK), 1)
        same_doc = (idc_ref[...] == idr_ref[0]) & (rows_at >= cols_at)
        b_f32 = b_blk.astype(jnp.float32)
        sq = jnp.zeros((BLOCK, 1), jnp.float32)
        for h in range(heads):
            cols = slice(h * head_dim, (h + 1) * head_dim)
            lc_c = lcc_ref[0, :, h:h + 1]
            lc_r = lcr_ref[0, h:h + 1, :]
            decay = jnp.where(same_doc, jnp.exp(lc_c - lc_r), 0.0)
            intra_w = (decay * inner_cb * str_ref[0, h:h + 1, :]).astype(jnp.bfloat16)
            xh = x_ref[:, cols]
            local = jnp.dot(intra_w, xh, preferred_element_type=jnp.float32)
            state_bf = carry_ref[h].astype(jnp.bfloat16)
            carried = jnp.dot(c_blk, state_bf, preferred_element_type=jnp.float32)
            carried = carried * csc_ref[0, :, h:h + 1]
            out = local + carried + skip_ref[h] * xh.astype(jnp.float32)
            o_ref[:, cols] = out
            sq = sq + jnp.sum(out * out, axis=1, keepdims=True)
            end_w_t = (esc_ref[0, :, h:h + 1] * b_f32).T.astype(jnp.bfloat16)
            block_state = jnp.dot(end_w_t, xh, preferred_element_type=jnp.float32)
            carry_ref[h] = gain_ref[0, h:h + 1, :] * carry_ref[h] + block_state
        sq_ref[...] = sq

    per_block = lambda shape: pl.BlockSpec((1,) + shape, lambda i: (i, 0, 0))
    return pl.pallas_call(
        kernel,
        grid=(nblk,),
        in_specs=[
            pl.BlockSpec((BLOCK, x_width), lambda i: (i, 0)),
            pl.BlockSpec((BLOCK, STATE), lambda i: (i, 0)),
            pl.BlockSpec((BLOCK, STATE), lambda i: (i, 0)),
            per_block((BLOCK, heads)),
            per_block((heads, BLOCK)),
            per_block((heads, BLOCK)),
            per_block((BLOCK, heads)),
            per_block((BLOCK, heads)),
            per_block((heads, head_dim)),
            pl.BlockSpec((BLOCK, 1), lambda i: (i, 0)),
            per_block((1, BLOCK)),
            pl.BlockSpec(memory_space=pltpu.SMEM),
        ],
        out_specs=[
            pl.BlockSpec((BLOCK, x_width), lambda i: (i, 0)),
            pl.BlockSpec((BLOCK, 1), lambda i: (i, 0)),
        ],
        out_shape=[
            jax.ShapeDtypeStruct((total, x_width), jnp.float32),
            jax.ShapeDtypeStruct((total, 1), jnp.float32),
        ],
        scratch_shapes=[pltpu.VMEM((heads, STATE, head_dim), jnp.float32)],
        compiler_params=pltpu.CompilerParams(dimension_semantics=("arbitrary",)),
        interpret=interpret,
    )(
        x_h, b_g, c_g, log_cum, lc_rows, st_rows, carry_scale, end_scale, gain_rows,
        all_ids.reshape(total, 1), ids.reshape(nblk, 1, BLOCK), skip_h,
    )


def attend_rows(q_row, kv_win, ids_q, ids_k, interpret=False):
    tok_rows, q_width = q_row.shape
    window = kv_win.shape[0]
    kv_heads = kv_win.shape[1] // (2 * HEAD_A)
    group = q_width // HEAD_A // kv_heads
    lead = window - tok_rows
    inv_sqrt = 1.0 / math.sqrt(HEAD_A)

    def kernel(q_ref, k_ref, v_ref, iq_ref, ik_ref, o_ref):
        q_at = lead + lax.broadcasted_iota(jnp.int32, (tok_rows, window), 0)
        k_at = lax.broadcasted_iota(jnp.int32, (tok_rows, window), 1)
        allowed = (iq_ref[...] == ik_ref[...]) & (q_at >= k_at)
        kb = k_ref[...]
        vb = v_ref[...]
        for g in range(group):
            cols = slice(g * HEAD_A, (g + 1) * HEAD_A)
            logits = lax.dot_general(
                q_ref[:, cols], kb, (((1,), (1,)), ((), ())), preferred_element_type=jnp.float32
            ) * inv_sqrt
            logits = jnp.where(allowed, logits, -jnp.inf)
            row_max = jnp.max(logits, axis=1, keepdims=True)
            exp_terms = jnp.exp(logits - row_max)
            probs = (exp_terms / jnp.sum(exp_terms, axis=1, keepdims=True)).astype(jnp.bfloat16)
            o_ref[:, cols] = jnp.dot(probs, vb, preferred_element_type=jnp.float32).astype(o_ref.dtype)

    return pl.pallas_call(
        kernel,
        grid=(kv_heads,),
        in_specs=[
            pl.BlockSpec((tok_rows, group * HEAD_A), lambda i: (0, i)),
            pl.BlockSpec((window, HEAD_A), lambda i: (0, i)),
            pl.BlockSpec((window, HEAD_A), lambda i: (0, kv_heads + i)),
            pl.BlockSpec((tok_rows, 1), lambda i: (0, 0)),
            pl.BlockSpec((1, window), lambda i: (0, 0)),
        ],
        out_specs=pl.BlockSpec((tok_rows, group * HEAD_A), lambda i: (0, i)),
        out_shape=jax.ShapeDtypeStruct((tok_rows, q_width), jnp.bfloat16),
        interpret=interpret,
    )(q_row, kv_win, kv_win, ids_q, ids_k)


def body(
    previous,
    fresh,
    dt_raw,
    dt_bias,
    a_log,
    b_in,
    c_in,
    skip_d,
    norm_gain,
    queries,
    keys,
    values,
    doc_ids,
):
    tok_rows, width = fresh.shape
    nctx = lax.axis_size("ctx")
    me = lax.axis_index("ctx")
    total = tok_rows * nctx
    part = width // nctx
    mamba_heads = dt_raw.shape[2]
    heads_dev = mamba_heads // nctx
    head_dim = width // mamba_heads
    kv_heads = keys.shape[2] // HEAD_A
    qpd = part // HEAD_A

    rep = nctx // kv_heads
    bc = jnp.stack(
        [b_in[0].reshape(tok_rows, GROUPS, STATE), c_in[0].reshape(tok_rows, GROUPS, STATE)], axis=2
    )
    bc_h = to_heads(jnp.repeat(bc, rep, axis=1).reshape(tok_rows, nctx * 2 * STATE), nctx)
    b_g, c_g = bc_h[:, :STATE], bc_h[:, STATE:]
    dt_h = to_heads(dt_raw[0], nctx)

    handed = shifted(previous[0], "section", 1)
    stream = jnp.where(lax.axis_index("section") == 0, fresh, handed)
    x_h = to_heads(stream, nctx)

    halo = -(-MOST_DOC // tok_rows)
    kv_row = jnp.concatenate([keys[0], values[0]], axis=1)
    kv_row, x_h = lax.optimization_barrier((kv_row, x_h))
    kv_win = jnp.concatenate([shifted(kv_row, "ctx", by) for by in range(halo, 0, -1)] + [kv_row], axis=0)
    all_ids = doc_ids[0]
    lead = halo * tok_rows
    padded_ids = jnp.concatenate([jnp.full((lead,), -1, all_ids.dtype), all_ids])
    ids_k = lax.dynamic_slice_in_dim(padded_ids, me * tok_rows, lead + tok_rows)
    ids_q = lax.dynamic_slice_in_dim(all_ids, me * tok_rows, tok_rows)

    bias_h = lax.dynamic_slice_in_dim(dt_bias[0], me * heads_dev, heads_dev)
    alog_h = lax.dynamic_slice_in_dim(a_log[0], me * heads_dev, heads_dev)
    skip_h = lax.dynamic_slice_in_dim(skip_d[0], me * heads_dev, heads_dev)
    gain_h = lax.dynamic_slice_in_dim(norm_gain[0], me * part, part)

    mixer_out, sq_part = mixer_heads(x_h, dt_h, bias_h, alog_h, b_g, c_g, skip_h, all_ids)
    kv_win, mixer_out, sq_part = lax.optimization_barrier((kv_win, mixer_out, sq_part))
    attended = attend_rows(queries[0], kv_win, ids_q.reshape(tok_rows, 1), ids_k.reshape(1, lead + tok_rows))
    sq_all = lax.all_to_all(
        jnp.broadcast_to(sq_part[:, 0][None], (nctx, total)), "ctx", split_axis=0, concat_axis=0, tiled=True
    )
    mean_sq = (jnp.sum(sq_all, axis=0) / width)[:, None]
    inv_rms = lax.rsqrt(mean_sq + norm_eps)
    mixed = (
        x_h.astype(jnp.float32) + mixer_out * inv_rms * gain_h.astype(jnp.float32)[None, :]
    ).astype(jnp.bfloat16)
    mixed_rows = to_rows(mixed, nctx)
    return (mixed_rows.astype(jnp.float32) + attended.astype(jnp.float32)).astype(jnp.bfloat16)[None]


def solution(mesh):
    in_specs = (
        P("section", "ctx", None),
        P("ctx", None),
        P("section", "ctx", None),
        P("section", None),
        P("section", None),
        P("section", "ctx", None),
        P("section", "ctx", None),
        P("section", None),
        P("section", None),
        P("section", "ctx", None),
        P("section", "ctx", None),
        P("section", "ctx", None),
        P("section", None),
    )
    out_specs = P("section", "ctx", None)
    return jax.shard_map(body, mesh=mesh, in_specs=in_specs, out_specs=out_specs, check_vma=False)
```

```python
import math

import jax
import jax.numpy as jnp
from jax import lax
from jax.experimental import pallas as pl
from jax.experimental.pallas import tpu as pltpu
from jax.sharding import PartitionSpec as P

HEAD_A = 128
STATE = 128
GROUPS = 8
BLOCK = 128
MOST_DOC = 512
Q_BLOCK = 256


norm_eps = 1e-05


def shifted(value, axis, by):
    peers = lax.axis_size(axis)
    pairs = [(i, i + by) for i in range(peers) if 0 <= i + by < peers]
    return lax.ppermute(value, axis, pairs)


def to_heads(row, chunks):
    tok_rows = row.shape[0]
    width = row.shape[1] // chunks
    lead = row.reshape(tok_rows, chunks, width).transpose(1, 0, 2)
    moved = lax.all_to_all(lead, "ctx", split_axis=0, concat_axis=0, tiled=True)
    return moved.reshape(tok_rows * chunks, width)


def to_rows(block, chunks):
    total, width = block.shape
    tok_rows = total // chunks
    moved = lax.all_to_all(block.reshape(chunks, tok_rows, width), "ctx", split_axis=0, concat_axis=0, tiled=True)
    return moved.transpose(1, 0, 2).reshape(tok_rows, chunks * width)


def mixer_heads(x_h, dt_h, bias_h, alog_h, b_g, c_g, skip_h, all_ids, interpret=False):
    total, x_width = x_h.shape
    heads = dt_h.shape[1]
    head_dim = x_width // heads
    nblk = total // BLOCK
    step = jax.nn.softplus(dt_h + bias_h[None, :])
    log_rate = -step * jnp.exp(alog_h)[None, :]
    log_cum = jnp.cumsum(log_rate.reshape(nblk, BLOCK, heads), axis=1)
    st = step.reshape(nblk, BLOCK, heads)
    ids = all_ids.reshape(nblk, BLOCK)
    last_id = ids[:, -1]
    prev_last = jnp.concatenate([jnp.full((1,), -1, ids.dtype), last_id[:-1]])
    edge_valid = (ids == prev_last[:, None]).astype(jnp.float32)
    carry_scale = jnp.exp(log_cum) * edge_valid[:, :, None]
    end_scale = (
        jnp.exp(log_cum[:, -1:, :] - log_cum) * st * (ids == last_id[:, None]).astype(jnp.float32)[:, :, None]
    )
    edge_match = (ids[:, 0] == prev_last).astype(jnp.float32)
    block_gain = jnp.exp(log_cum[:, -1, :]) * (ids[:, 0] == last_id).astype(jnp.float32)[:, None]
    block_gain = block_gain * edge_match[:, None]
    gain_rows = jnp.broadcast_to(block_gain[:, :, None], (nblk, heads, head_dim))
    lc_rows = log_cum.transpose(0, 2, 1)
    end_rows = end_scale.transpose(0, 2, 1)
    b_t = b_g.T
    st_rows = st.transpose(0, 2, 1)

    def kernel(x_ref, b_ref, c_ref, lcc_ref, lcr_ref, str_ref, csc_ref, esc_ref, gain_ref,
               idc_ref, idr_ref, skip_ref, o_ref, sq_ref, carry_ref):
        @pl.when(pl.program_id(0) == 0)
        def _():
            carry_ref[...] = jnp.zeros(carry_ref.shape, carry_ref.dtype)

        b_t_blk = b_ref[...]
        c_blk = c_ref[...]
        inner_cb = jnp.dot(c_blk, b_t_blk, preferred_element_type=jnp.float32)
        rows_at = lax.broadcasted_iota(jnp.int32, (BLOCK, BLOCK), 0)
        cols_at = lax.broadcasted_iota(jnp.int32, (BLOCK, BLOCK), 1)
        same_doc = (idc_ref[...] == idr_ref[0]) & (rows_at >= cols_at)
        b_t_f32 = b_t_blk.astype(jnp.float32)
        sq = jnp.zeros((BLOCK, 1), jnp.float32)
        for h in range(heads):
            cols = slice(h * head_dim, (h + 1) * head_dim)
            lc_c = lcc_ref[0, :, h:h + 1]
            lc_r = lcr_ref[0, h:h + 1, :]
            decay = jnp.where(same_doc, jnp.exp(lc_c - lc_r), 0.0)
            intra_w = (decay * inner_cb * str_ref[0, h:h + 1, :]).astype(jnp.bfloat16)
            xh = x_ref[:, cols]
            local = jnp.dot(intra_w, xh, preferred_element_type=jnp.float32)
            state_bf = carry_ref[h].astype(jnp.bfloat16)
            carried = jnp.dot(c_blk, state_bf, preferred_element_type=jnp.float32)
            carried = carried * csc_ref[0, :, h:h + 1]
            out = local + carried + skip_ref[h] * xh.astype(jnp.float32)
            o_ref[:, cols] = out
            sq = sq + jnp.sum(out * out, axis=1, keepdims=True)
            end_w_t = (esc_ref[0, h:h + 1, :] * b_t_f32).astype(jnp.bfloat16)
            block_state = jnp.dot(end_w_t, xh, preferred_element_type=jnp.float32)
            carry_ref[h] = gain_ref[0, h:h + 1, :] * carry_ref[h] + block_state
        sq_ref[...] = sq

    per_block = lambda shape: pl.BlockSpec((1,) + shape, lambda i: (i, 0, 0))
    return pl.pallas_call(
        kernel,
        grid=(nblk,),
        in_specs=[
            pl.BlockSpec((BLOCK, x_width), lambda i: (i, 0)),
            pl.BlockSpec((STATE, BLOCK), lambda i: (0, i)),
            pl.BlockSpec((BLOCK, STATE), lambda i: (i, 0)),
            per_block((BLOCK, heads)),
            per_block((heads, BLOCK)),
            per_block((heads, BLOCK)),
            per_block((BLOCK, heads)),
            per_block((heads, BLOCK)),
            per_block((heads, head_dim)),
            pl.BlockSpec((BLOCK, 1), lambda i: (i, 0)),
            per_block((1, BLOCK)),
            pl.BlockSpec(memory_space=pltpu.SMEM),
        ],
        out_specs=[
            pl.BlockSpec((BLOCK, x_width), lambda i: (i, 0)),
            pl.BlockSpec((BLOCK, 1), lambda i: (i, 0)),
        ],
        out_shape=[
            jax.ShapeDtypeStruct((total, x_width), jnp.float32),
            jax.ShapeDtypeStruct((total, 1), jnp.float32),
        ],
        scratch_shapes=[pltpu.VMEM((heads, STATE, head_dim), jnp.float32)],
        compiler_params=pltpu.CompilerParams(dimension_semantics=("arbitrary",)),
        interpret=interpret,
    )(
        x_h, b_t, c_g, log_cum, lc_rows, st_rows, carry_scale, end_rows, gain_rows,
        all_ids.reshape(total, 1), ids.reshape(nblk, 1, BLOCK), skip_h,
    )


def attend_rows(q_row, kv_win, ids_q, ids_k, interpret=False):
    tok_rows, q_width = q_row.shape
    window = kv_win.shape[0]
    kv_heads = kv_win.shape[1] // (2 * HEAD_A)
    group = q_width // HEAD_A // kv_heads
    lead = window - tok_rows
    inv_sqrt = 1.0 / math.sqrt(HEAD_A)

    def kernel(q_ref, k_ref, v_ref, iq_ref, ik_ref, o_ref):
        q_at = lead + lax.broadcasted_iota(jnp.int32, (tok_rows, window), 0)
        k_at = lax.broadcasted_iota(jnp.int32, (tok_rows, window), 1)
        allowed = (iq_ref[...] == ik_ref[...]) & (q_at >= k_at)
        kb = k_ref[...]
        vb = v_ref[...]
        for g in range(group):
            cols = slice(g * HEAD_A, (g + 1) * HEAD_A)
            logits = lax.dot_general(
                q_ref[:, cols], kb, (((1,), (1,)), ((), ())), preferred_element_type=jnp.float32
            ) * inv_sqrt
            logits = jnp.where(allowed, logits, -jnp.inf)
            row_max = jnp.max(logits, axis=1, keepdims=True)
            exp_terms = jnp.exp(logits - row_max)
            probs = (exp_terms / jnp.sum(exp_terms, axis=1, keepdims=True)).astype(jnp.bfloat16)
            o_ref[:, cols] = jnp.dot(probs, vb, preferred_element_type=jnp.float32).astype(o_ref.dtype)

    return pl.pallas_call(
        kernel,
        grid=(kv_heads,),
        in_specs=[
            pl.BlockSpec((tok_rows, group * HEAD_A), lambda i: (0, i)),
            pl.BlockSpec((window, HEAD_A), lambda i: (0, i)),
            pl.BlockSpec((window, HEAD_A), lambda i: (0, kv_heads + i)),
            pl.BlockSpec((tok_rows, 1), lambda i: (0, 0)),
            pl.BlockSpec((1, window), lambda i: (0, 0)),
        ],
        out_specs=pl.BlockSpec((tok_rows, group * HEAD_A), lambda i: (0, i)),
        out_shape=jax.ShapeDtypeStruct((tok_rows, q_width), jnp.bfloat16),
        interpret=interpret,
    )(q_row, kv_win, kv_win, ids_q, ids_k)


def body(
    previous,
    fresh,
    dt_raw,
    dt_bias,
    a_log,
    b_in,
    c_in,
    skip_d,
    norm_gain,
    queries,
    keys,
    values,
    doc_ids,
):
    tok_rows, width = fresh.shape
    nctx = lax.axis_size("ctx")
    me = lax.axis_index("ctx")
    total = tok_rows * nctx
    part = width // nctx
    mamba_heads = dt_raw.shape[2]
    heads_dev = mamba_heads // nctx
    head_dim = width // mamba_heads
    kv_heads = keys.shape[2] // HEAD_A
    qpd = part // HEAD_A

    rep = nctx // kv_heads
    bc = jnp.stack(
        [b_in[0].reshape(tok_rows, GROUPS, STATE), c_in[0].reshape(tok_rows, GROUPS, STATE)], axis=2
    )
    bc_h = to_heads(jnp.repeat(bc, rep, axis=1).reshape(tok_rows, nctx * 2 * STATE), nctx)
    b_g, c_g = bc_h[:, :STATE], bc_h[:, STATE:]
    dt_h = to_heads(dt_raw[0], nctx)

    handed = shifted(previous[0], "section", 1)
    stream = jnp.where(lax.axis_index("section") == 0, fresh, handed)
    x_h = to_heads(stream, nctx)

    halo = -(-MOST_DOC // tok_rows)
    kv_row = jnp.concatenate([keys[0], values[0]], axis=1)
    kv_row, x_h = lax.optimization_barrier((kv_row, x_h))
    kv_win = jnp.concatenate([shifted(kv_row, "ctx", by) for by in range(halo, 0, -1)] + [kv_row], axis=0)
    all_ids = doc_ids[0]
    lead = halo * tok_rows
    padded_ids = jnp.concatenate([jnp.full((lead,), -1, all_ids.dtype), all_ids])
    ids_k = lax.dynamic_slice_in_dim(padded_ids, me * tok_rows, lead + tok_rows)
    ids_q = lax.dynamic_slice_in_dim(all_ids, me * tok_rows, tok_rows)

    bias_h = lax.dynamic_slice_in_dim(dt_bias[0], me * heads_dev, heads_dev)
    alog_h = lax.dynamic_slice_in_dim(a_log[0], me * heads_dev, heads_dev)
    skip_h = lax.dynamic_slice_in_dim(skip_d[0], me * heads_dev, heads_dev)
    gain_h = lax.dynamic_slice_in_dim(norm_gain[0], me * part, part)

    mixer_out, sq_part = mixer_heads(x_h, dt_h, bias_h, alog_h, b_g, c_g, skip_h, all_ids)
    kv_win, mixer_out, sq_part = lax.optimization_barrier((kv_win, mixer_out, sq_part))
    attended = attend_rows(queries[0], kv_win, ids_q.reshape(tok_rows, 1), ids_k.reshape(1, lead + tok_rows))
    sq_all = lax.all_to_all(
        jnp.broadcast_to(sq_part[:, 0][None], (nctx, total)), "ctx", split_axis=0, concat_axis=0, tiled=True
    )
    mean_sq = (jnp.sum(sq_all, axis=0) / width)[:, None]
    inv_rms = lax.rsqrt(mean_sq + norm_eps)
    mixed = (
        x_h.astype(jnp.float32) + mixer_out * inv_rms * gain_h.astype(jnp.float32)[None, :]
    ).astype(jnp.bfloat16)
    mixed_rows = to_rows(mixed, nctx)
    return (mixed_rows.astype(jnp.float32) + attended.astype(jnp.float32)).astype(jnp.bfloat16)[None]


def solution(mesh):
    in_specs = (
        P("section", "ctx", None),
        P("ctx", None),
        P("section", "ctx", None),
        P("section", None),
        P("section", None),
        P("section", "ctx", None),
        P("section", "ctx", None),
        P("section", None),
        P("section", None),
        P("section", "ctx", None),
        P("section", "ctx", None),
        P("section", "ctx", None),
        P("section", None),
    )
    out_specs = P("section", "ctx", None)
    return jax.shard_map(body, mesh=mesh, in_specs=in_specs, out_specs=out_specs, check_vma=False)
```

```python
import math

import jax
import jax.numpy as jnp
from jax import lax
from jax.experimental import pallas as pl
from jax.experimental.pallas import tpu as pltpu
from jax.sharding import PartitionSpec as P

HEAD_A = 128
STATE = 128
GROUPS = 8
BLOCK = 128
MOST_DOC = 512
Q_BLOCK = 256


norm_eps = 1e-05


def shifted(value, axis, by):
    peers = lax.axis_size(axis)
    pairs = [(i, i + by) for i in range(peers) if 0 <= i + by < peers]
    return lax.ppermute(value, axis, pairs)


def to_heads(row, chunks):
    tok_rows = row.shape[0]
    width = row.shape[1] // chunks
    lead = row.reshape(tok_rows, chunks, width).transpose(1, 0, 2)
    moved = lax.all_to_all(lead, "ctx", split_axis=0, concat_axis=0, tiled=True)
    return moved.reshape(tok_rows * chunks, width)


def to_rows(block, chunks):
    total, width = block.shape
    tok_rows = total // chunks
    moved = lax.all_to_all(block.reshape(chunks, tok_rows, width), "ctx", split_axis=0, concat_axis=0, tiled=True)
    return moved.transpose(1, 0, 2).reshape(tok_rows, chunks * width)


def mixer_heads(x_h, dt_h, bias_h, alog_h, b_g, c_g, skip_h, all_ids, interpret=False):
    total, x_width = x_h.shape
    heads = dt_h.shape[1]
    head_dim = x_width // heads
    nblk = total // BLOCK
    step = jax.nn.softplus(dt_h + bias_h[None, :])
    log_rate = -step * jnp.exp(alog_h)[None, :]
    log_cum = jnp.cumsum(log_rate.reshape(nblk, BLOCK, heads), axis=1)
    st = step.reshape(nblk, BLOCK, heads)
    ids = all_ids.reshape(nblk, BLOCK)
    last_id = ids[:, -1]
    prev_last = jnp.concatenate([jnp.full((1,), -1, ids.dtype), last_id[:-1]])
    edge_valid = (ids == prev_last[:, None]).astype(jnp.float32)
    carry_scale = jnp.exp(log_cum) * edge_valid[:, :, None]
    end_scale = (
        jnp.exp(log_cum[:, -1:, :] - log_cum) * st * (ids == last_id[:, None]).astype(jnp.float32)[:, :, None]
    )
    edge_match = (ids[:, 0] == prev_last).astype(jnp.float32)
    block_gain = jnp.exp(log_cum[:, -1, :]) * (ids[:, 0] == last_id).astype(jnp.float32)[:, None]
    block_gain = block_gain * edge_match[:, None]
    gain_rows = jnp.broadcast_to(block_gain[:, :, None], (nblk, heads, head_dim))
    lc_rows = log_cum.transpose(0, 2, 1)
    end_rows = end_scale.transpose(0, 2, 1)
    b_t = b_g.T
    st_rows = st.transpose(0, 2, 1)

    def kernel(x_ref, b_ref, c_ref, lcc_ref, lcr_ref, str_ref, csc_ref, esc_ref, gain_ref,
               idc_ref, idr_ref, skip_ref, o_ref, sq_ref, carry_ref):
        @pl.when(pl.program_id(0) == 0)
        def _():
            carry_ref[...] = jnp.zeros(carry_ref.shape, carry_ref.dtype)

        b_t_blk = b_ref[...]
        c_blk = c_ref[...]
        inner_cb = jnp.dot(c_blk, b_t_blk, preferred_element_type=jnp.float32)
        rows_at = lax.broadcasted_iota(jnp.int32, (BLOCK, BLOCK), 0)
        cols_at = lax.broadcasted_iota(jnp.int32, (BLOCK, BLOCK), 1)
        same_doc = (idc_ref[...] == idr_ref[0]) & (rows_at >= cols_at)
        b_t_f32 = b_t_blk.astype(jnp.float32)
        sq = jnp.zeros((BLOCK, 1), jnp.float32)
        for h in range(heads):
            cols = slice(h * head_dim, (h + 1) * head_dim)
            lc_c = lcc_ref[0, :, h:h + 1]
            lc_r = lcr_ref[0, h:h + 1, :]
            decay = jnp.where(same_doc, jnp.exp(lc_c - lc_r), 0.0)
            intra_w = (decay * inner_cb * str_ref[0, h:h + 1, :]).astype(jnp.bfloat16)
            xh = x_ref[:, cols]
            local = jnp.dot(intra_w, xh, preferred_element_type=jnp.float32)
            state_bf = carry_ref[h].astype(jnp.bfloat16)
            carried = jnp.dot(c_blk, state_bf, preferred_element_type=jnp.float32)
            carried = carried * csc_ref[0, :, h:h + 1]
            out = local + carried + skip_ref[h] * xh.astype(jnp.float32)
            o_ref[:, cols] = out
            sq = sq + jnp.sum(out * out, axis=1, keepdims=True)
            end_w_t = (esc_ref[0, h:h + 1, :] * b_t_f32).astype(jnp.bfloat16)
            block_state = jnp.dot(end_w_t, xh, preferred_element_type=jnp.float32)
            carry_ref[h] = gain_ref[0, h:h + 1, :] * carry_ref[h] + block_state
        sq_ref[...] = sq

    per_block = lambda shape: pl.BlockSpec((1,) + shape, lambda i: (i, 0, 0))
    return pl.pallas_call(
        kernel,
        grid=(nblk,),
        in_specs=[
            pl.BlockSpec((BLOCK, x_width), lambda i: (i, 0)),
            pl.BlockSpec((STATE, BLOCK), lambda i: (0, i)),
            pl.BlockSpec((BLOCK, STATE), lambda i: (i, 0)),
            per_block((BLOCK, heads)),
            per_block((heads, BLOCK)),
            per_block((heads, BLOCK)),
            per_block((BLOCK, heads)),
            per_block((heads, BLOCK)),
            per_block((heads, head_dim)),
            pl.BlockSpec((BLOCK, 1), lambda i: (i, 0)),
            per_block((1, BLOCK)),
            pl.BlockSpec(memory_space=pltpu.SMEM),
        ],
        out_specs=[
            pl.BlockSpec((BLOCK, x_width), lambda i: (i, 0)),
            pl.BlockSpec((BLOCK, 1), lambda i: (i, 0)),
        ],
        out_shape=[
            jax.ShapeDtypeStruct((total, x_width), jnp.float32),
            jax.ShapeDtypeStruct((total, 1), jnp.float32),
        ],
        scratch_shapes=[pltpu.VMEM((heads, STATE, head_dim), jnp.float32)],
        compiler_params=pltpu.CompilerParams(dimension_semantics=("arbitrary",)),
        interpret=interpret,
    )(
        x_h, b_t, c_g, log_cum, lc_rows, st_rows, carry_scale, end_rows, gain_rows,
        all_ids.reshape(total, 1), ids.reshape(nblk, 1, BLOCK), skip_h,
    )


def attend_rows(q_row, kv_win, ids_q, ids_k, interpret=False):
    tok_rows, q_width = q_row.shape
    window = kv_win.shape[0]
    kv_heads = kv_win.shape[1] // (2 * HEAD_A)
    group = q_width // HEAD_A // kv_heads
    lead = window - tok_rows
    inv_sqrt = 1.0 / math.sqrt(HEAD_A)

    def kernel(q_ref, k_ref, v_ref, iq_ref, ik_ref, o_ref):
        q_at = lead + lax.broadcasted_iota(jnp.int32, (tok_rows, window), 0)
        k_at = lax.broadcasted_iota(jnp.int32, (tok_rows, window), 1)
        allowed = (iq_ref[...] == ik_ref[...]) & (q_at >= k_at)
        kb = k_ref[...]
        vb = v_ref[...]
        for g in range(group):
            cols = slice(g * HEAD_A, (g + 1) * HEAD_A)
            logits = lax.dot_general(
                q_ref[:, cols], kb, (((1,), (1,)), ((), ())), preferred_element_type=jnp.float32
            ) * inv_sqrt
            logits = jnp.where(allowed, logits, -jnp.inf)
            row_max = jnp.max(logits, axis=1, keepdims=True)
            exp_terms = jnp.exp(logits - row_max)
            probs = (exp_terms / jnp.sum(exp_terms, axis=1, keepdims=True)).astype(jnp.bfloat16)
            o_ref[:, cols] = jnp.dot(probs, vb, preferred_element_type=jnp.float32).astype(o_ref.dtype)

    return pl.pallas_call(
        kernel,
        grid=(kv_heads,),
        in_specs=[
            pl.BlockSpec((tok_rows, group * HEAD_A), lambda i: (0, i)),
            pl.BlockSpec((window, HEAD_A), lambda i: (0, i)),
            pl.BlockSpec((window, HEAD_A), lambda i: (0, kv_heads + i)),
            pl.BlockSpec((tok_rows, 1), lambda i: (0, 0)),
            pl.BlockSpec((1, window), lambda i: (0, 0)),
        ],
        out_specs=pl.BlockSpec((tok_rows, group * HEAD_A), lambda i: (0, i)),
        out_shape=jax.ShapeDtypeStruct((tok_rows, q_width), jnp.bfloat16),
        interpret=interpret,
    )(q_row, kv_win, kv_win, ids_q, ids_k)


def body(
    previous,
    fresh,
    dt_raw,
    dt_bias,
    a_log,
    b_in,
    c_in,
    skip_d,
    norm_gain,
    queries,
    keys,
    values,
    doc_ids,
):
    tok_rows, width = fresh.shape
    nctx = lax.axis_size("ctx")
    me = lax.axis_index("ctx")
    total = tok_rows * nctx
    part = width // nctx
    mamba_heads = dt_raw.shape[2]
    heads_dev = mamba_heads // nctx
    head_dim = width // mamba_heads
    kv_heads = keys.shape[2] // HEAD_A
    qpd = part // HEAD_A

    rep = nctx // kv_heads
    bc = jnp.stack(
        [b_in[0].reshape(tok_rows, GROUPS, STATE), c_in[0].reshape(tok_rows, GROUPS, STATE)], axis=2
    )
    bc_h = to_heads(jnp.repeat(bc, rep, axis=1).reshape(tok_rows, nctx * 2 * STATE), nctx)
    b_g, c_g = bc_h[:, :STATE], bc_h[:, STATE:]
    dt_h = to_heads(dt_raw[0], nctx)

    handed = shifted(previous[0], "section", 1)
    stream = jnp.where(lax.axis_index("section") == 0, fresh, handed)
    x_h = to_heads(stream, nctx)

    halo = -(-MOST_DOC // tok_rows)
    kv_row = jnp.concatenate([keys[0], values[0]], axis=1)
    kv_win = jnp.concatenate([shifted(kv_row, "ctx", by) for by in range(halo, 0, -1)] + [kv_row], axis=0)
    kv_win, x_h = lax.optimization_barrier((kv_win, x_h))
    all_ids = doc_ids[0]
    lead = halo * tok_rows
    padded_ids = jnp.concatenate([jnp.full((lead,), -1, all_ids.dtype), all_ids])
    ids_k = lax.dynamic_slice_in_dim(padded_ids, me * tok_rows, lead + tok_rows)
    ids_q = lax.dynamic_slice_in_dim(all_ids, me * tok_rows, tok_rows)

    bias_h = lax.dynamic_slice_in_dim(dt_bias[0], me * heads_dev, heads_dev)
    alog_h = lax.dynamic_slice_in_dim(a_log[0], me * heads_dev, heads_dev)
    skip_h = lax.dynamic_slice_in_dim(skip_d[0], me * heads_dev, heads_dev)
    gain_h = lax.dynamic_slice_in_dim(norm_gain[0], me * part, part)

    mixer_out, sq_part = mixer_heads(x_h, dt_h, bias_h, alog_h, b_g, c_g, skip_h, all_ids)
    attended = attend_rows(queries[0], kv_win, ids_q.reshape(tok_rows, 1), ids_k.reshape(1, lead + tok_rows))
    sq_all = lax.all_to_all(
        jnp.broadcast_to(sq_part[:, 0][None], (nctx, total)), "ctx", split_axis=0, concat_axis=0, tiled=True
    )
    mean_sq = (jnp.sum(sq_all, axis=0) / width)[:, None]
    inv_rms = lax.rsqrt(mean_sq + norm_eps)
    mixed = (
        x_h.astype(jnp.float32) + mixer_out * inv_rms * gain_h.astype(jnp.float32)[None, :]
    ).astype(jnp.bfloat16)
    mixed_rows = to_rows(mixed, nctx)
    return (mixed_rows.astype(jnp.float32) + attended.astype(jnp.float32)).astype(jnp.bfloat16)[None]


def solution(mesh):
    in_specs = (
        P("section", "ctx", None),
        P("ctx", None),
        P("section", "ctx", None),
        P("section", None),
        P("section", None),
        P("section", "ctx", None),
        P("section", "ctx", None),
        P("section", None),
        P("section", None),
        P("section", "ctx", None),
        P("section", "ctx", None),
        P("section", "ctx", None),
        P("section", None),
    )
    out_specs = P("section", "ctx", None)
    return jax.shard_map(body, mesh=mesh, in_specs=in_specs, out_specs=out_specs, check_vma=False)
```

```python
import math

import jax
import jax.numpy as jnp
from jax import lax
from jax.experimental import pallas as pl
from jax.experimental.pallas import tpu as pltpu
from jax.sharding import PartitionSpec as P

HEAD_A = 128
STATE = 128
GROUPS = 8
BLOCK = 128
MOST_DOC = 512
Q_BLOCK = 256


norm_eps = 1e-05


def shifted(value, axis, by):
    peers = lax.axis_size(axis)
    pairs = [(i, i + by) for i in range(peers) if 0 <= i + by < peers]
    return lax.ppermute(value, axis, pairs)


def to_heads(row, chunks):
    tok_rows = row.shape[0]
    width = row.shape[1] // chunks
    lead = row.reshape(tok_rows, chunks, width).transpose(1, 0, 2)
    moved = lax.all_to_all(lead, "ctx", split_axis=0, concat_axis=0, tiled=True)
    return moved.reshape(tok_rows * chunks, width)


def to_rows(block, chunks):
    total, width = block.shape
    tok_rows = total // chunks
    moved = lax.all_to_all(block.reshape(chunks, tok_rows, width), "ctx", split_axis=0, concat_axis=0, tiled=True)
    return moved.transpose(1, 0, 2).reshape(tok_rows, chunks * width)


def mixer_heads(x_h, dt_h, bias_h, alog_h, b_g, c_g, skip_h, all_ids, interpret=False):
    total, x_width = x_h.shape
    heads = dt_h.shape[1]
    head_dim = x_width // heads
    nblk = total // BLOCK
    step = jax.nn.softplus(dt_h + bias_h[None, :])
    log_rate = -step * jnp.exp(alog_h)[None, :]
    log_cum = log_rate.reshape(nblk, BLOCK, heads)
    reach = 1
    while reach < BLOCK:
        log_cum = log_cum + jnp.pad(log_cum[:, :-reach], ((0, 0), (reach, 0), (0, 0)))
        reach *= 2
    st = step.reshape(nblk, BLOCK, heads)
    ids = all_ids.reshape(nblk, BLOCK)
    last_id = ids[:, -1]
    prev_last = jnp.concatenate([jnp.full((1,), -1, ids.dtype), last_id[:-1]])
    edge_valid = (ids == prev_last[:, None]).astype(jnp.float32)
    carry_scale = jnp.exp(log_cum) * edge_valid[:, :, None]
    end_scale = (
        jnp.exp(log_cum[:, -1:, :] - log_cum) * st * (ids == last_id[:, None]).astype(jnp.float32)[:, :, None]
    )
    edge_match = (ids[:, 0] == prev_last).astype(jnp.float32)
    block_gain = jnp.exp(log_cum[:, -1, :]) * (ids[:, 0] == last_id).astype(jnp.float32)[:, None]
    block_gain = block_gain * edge_match[:, None]
    gain_rows = jnp.broadcast_to(block_gain[:, :, None], (nblk, heads, head_dim))
    lc_rows = log_cum.transpose(0, 2, 1)
    end_rows = end_scale.transpose(0, 2, 1)
    b_t = b_g.T
    st_rows = st.transpose(0, 2, 1)

    def kernel(x_ref, b_ref, c_ref, lcc_ref, lcr_ref, str_ref, csc_ref, esc_ref, gain_ref,
               idc_ref, idr_ref, skip_ref, o_ref, sq_ref, carry_ref):
        @pl.when(pl.program_id(0) == 0)
        def _():
            carry_ref[...] = jnp.zeros(carry_ref.shape, carry_ref.dtype)

        b_t_blk = b_ref[...]
        c_blk = c_ref[...]
        inner_cb = jnp.dot(c_blk, b_t_blk, preferred_element_type=jnp.float32)
        rows_at = lax.broadcasted_iota(jnp.int32, (BLOCK, BLOCK), 0)
        cols_at = lax.broadcasted_iota(jnp.int32, (BLOCK, BLOCK), 1)
        same_doc = (idc_ref[...] == idr_ref[0]) & (rows_at >= cols_at)
        b_t_f32 = b_t_blk.astype(jnp.float32)
        sq = jnp.zeros((BLOCK, 1), jnp.float32)
        for h in range(heads):
            cols = slice(h * head_dim, (h + 1) * head_dim)
            lc_c = lcc_ref[0, :, h:h + 1]
            lc_r = lcr_ref[0, h:h + 1, :]
            decay = jnp.where(same_doc, jnp.exp(lc_c - lc_r), 0.0)
            intra_w = (decay * inner_cb * str_ref[0, h:h + 1, :]).astype(jnp.bfloat16)
            xh = x_ref[:, cols]
            local = jnp.dot(intra_w, xh, preferred_element_type=jnp.float32)
            state_bf = carry_ref[h].astype(jnp.bfloat16)
            carried = jnp.dot(c_blk, state_bf, preferred_element_type=jnp.float32)
            carried = carried * csc_ref[0, :, h:h + 1]
            out = local + carried + skip_ref[h] * xh.astype(jnp.float32)
            o_ref[:, cols] = out
            sq = sq + jnp.sum(out * out, axis=1, keepdims=True)
            end_w_t = (esc_ref[0, h:h + 1, :] * b_t_f32).astype(jnp.bfloat16)
            block_state = jnp.dot(end_w_t, xh, preferred_element_type=jnp.float32)
            carry_ref[h] = gain_ref[0, h:h + 1, :] * carry_ref[h] + block_state
        sq_ref[...] = sq

    per_block = lambda shape: pl.BlockSpec((1,) + shape, lambda i: (i, 0, 0))
    return pl.pallas_call(
        kernel,
        grid=(nblk,),
        in_specs=[
            pl.BlockSpec((BLOCK, x_width), lambda i: (i, 0)),
            pl.BlockSpec((STATE, BLOCK), lambda i: (0, i)),
            pl.BlockSpec((BLOCK, STATE), lambda i: (i, 0)),
            per_block((BLOCK, heads)),
            per_block((heads, BLOCK)),
            per_block((heads, BLOCK)),
            per_block((BLOCK, heads)),
            per_block((heads, BLOCK)),
            per_block((heads, head_dim)),
            pl.BlockSpec((BLOCK, 1), lambda i: (i, 0)),
            per_block((1, BLOCK)),
            pl.BlockSpec(memory_space=pltpu.SMEM),
        ],
        out_specs=[
            pl.BlockSpec((BLOCK, x_width), lambda i: (i, 0)),
            pl.BlockSpec((BLOCK, 1), lambda i: (i, 0)),
        ],
        out_shape=[
            jax.ShapeDtypeStruct((total, x_width), jnp.float32),
            jax.ShapeDtypeStruct((total, 1), jnp.float32),
        ],
        scratch_shapes=[pltpu.VMEM((heads, STATE, head_dim), jnp.float32)],
        compiler_params=pltpu.CompilerParams(dimension_semantics=("arbitrary",)),
        interpret=interpret,
    )(
        x_h, b_t, c_g, log_cum, lc_rows, st_rows, carry_scale, end_rows, gain_rows,
        all_ids.reshape(total, 1), ids.reshape(nblk, 1, BLOCK), skip_h,
    )


def attend_rows(q_row, kv_win, ids_q, ids_k, interpret=False):
    tok_rows, q_width = q_row.shape
    window = kv_win.shape[0]
    kv_heads = kv_win.shape[1] // (2 * HEAD_A)
    group = q_width // HEAD_A // kv_heads
    lead = window - tok_rows
    inv_sqrt = 1.0 / math.sqrt(HEAD_A)

    def kernel(q_ref, k_ref, v_ref, iq_ref, ik_ref, o_ref):
        q_at = lead + lax.broadcasted_iota(jnp.int32, (tok_rows, window), 0)
        k_at = lax.broadcasted_iota(jnp.int32, (tok_rows, window), 1)
        allowed = (iq_ref[...] == ik_ref[...]) & (q_at >= k_at)
        kb = k_ref[...]
        vb = v_ref[...]
        for g in range(group):
            cols = slice(g * HEAD_A, (g + 1) * HEAD_A)
            logits = lax.dot_general(
                q_ref[:, cols], kb, (((1,), (1,)), ((), ())), preferred_element_type=jnp.float32
            ) * inv_sqrt
            logits = jnp.where(allowed, logits, -jnp.inf)
            row_max = jnp.max(logits, axis=1, keepdims=True)
            exp_terms = jnp.exp(logits - row_max)
            probs = (exp_terms / jnp.sum(exp_terms, axis=1, keepdims=True)).astype(jnp.bfloat16)
            o_ref[:, cols] = jnp.dot(probs, vb, preferred_element_type=jnp.float32).astype(o_ref.dtype)

    return pl.pallas_call(
        kernel,
        grid=(kv_heads,),
        in_specs=[
            pl.BlockSpec((tok_rows, group * HEAD_A), lambda i: (0, i)),
            pl.BlockSpec((window, HEAD_A), lambda i: (0, i)),
            pl.BlockSpec((window, HEAD_A), lambda i: (0, kv_heads + i)),
            pl.BlockSpec((tok_rows, 1), lambda i: (0, 0)),
            pl.BlockSpec((1, window), lambda i: (0, 0)),
        ],
        out_specs=pl.BlockSpec((tok_rows, group * HEAD_A), lambda i: (0, i)),
        out_shape=jax.ShapeDtypeStruct((tok_rows, q_width), jnp.bfloat16),
        interpret=interpret,
    )(q_row, kv_win, kv_win, ids_q, ids_k)


def body(
    previous,
    fresh,
    dt_raw,
    dt_bias,
    a_log,
    b_in,
    c_in,
    skip_d,
    norm_gain,
    queries,
    keys,
    values,
    doc_ids,
):
    tok_rows, width = fresh.shape
    nctx = lax.axis_size("ctx")
    me = lax.axis_index("ctx")
    total = tok_rows * nctx
    part = width // nctx
    mamba_heads = dt_raw.shape[2]
    heads_dev = mamba_heads // nctx
    head_dim = width // mamba_heads
    kv_heads = keys.shape[2] // HEAD_A
    qpd = part // HEAD_A

    rep = nctx // kv_heads
    bc = jnp.stack(
        [b_in[0].reshape(tok_rows, GROUPS, STATE), c_in[0].reshape(tok_rows, GROUPS, STATE)], axis=2
    )
    bc_h = to_heads(jnp.repeat(bc, rep, axis=1).reshape(tok_rows, nctx * 2 * STATE), nctx)
    b_g, c_g = bc_h[:, :STATE], bc_h[:, STATE:]
    dt_h = to_heads(dt_raw[0], nctx)

    handed = shifted(previous[0], "section", 1)
    stream = jnp.where(lax.axis_index("section") == 0, fresh, handed)
    x_h = to_heads(stream, nctx)

    halo = -(-MOST_DOC // tok_rows)
    kv_row = jnp.concatenate([keys[0], values[0]], axis=1)
    kv_win = jnp.concatenate([shifted(kv_row, "ctx", by) for by in range(halo, 0, -1)] + [kv_row], axis=0)
    kv_win, x_h = lax.optimization_barrier((kv_win, x_h))
    all_ids = doc_ids[0]
    lead = halo * tok_rows
    padded_ids = jnp.concatenate([jnp.full((lead,), -1, all_ids.dtype), all_ids])
    ids_k = lax.dynamic_slice_in_dim(padded_ids, me * tok_rows, lead + tok_rows)
    ids_q = lax.dynamic_slice_in_dim(all_ids, me * tok_rows, tok_rows)

    bias_h = lax.dynamic_slice_in_dim(dt_bias[0], me * heads_dev, heads_dev)
    alog_h = lax.dynamic_slice_in_dim(a_log[0], me * heads_dev, heads_dev)
    skip_h = lax.dynamic_slice_in_dim(skip_d[0], me * heads_dev, heads_dev)
    gain_h = lax.dynamic_slice_in_dim(norm_gain[0], me * part, part)

    mixer_out, sq_part = mixer_heads(x_h, dt_h, bias_h, alog_h, b_g, c_g, skip_h, all_ids)
    attended = attend_rows(queries[0], kv_win, ids_q.reshape(tok_rows, 1), ids_k.reshape(1, lead + tok_rows))
    sq_all = lax.all_to_all(
        jnp.broadcast_to(sq_part[:, 0][None], (nctx, total)), "ctx", split_axis=0, concat_axis=0, tiled=True
    )
    mean_sq = (jnp.sum(sq_all, axis=0) / width)[:, None]
    inv_rms = lax.rsqrt(mean_sq + norm_eps)
    mixed = (
        x_h.astype(jnp.float32) + mixer_out * inv_rms * gain_h.astype(jnp.float32)[None, :]
    ).astype(jnp.bfloat16)
    mixed_rows = to_rows(mixed, nctx)
    return (mixed_rows.astype(jnp.float32) + attended.astype(jnp.float32)).astype(jnp.bfloat16)[None]


def solution(mesh):
    in_specs = (
        P("section", "ctx", None),
        P("ctx", None),
        P("section", "ctx", None),
        P("section", None),
        P("section", None),
        P("section", "ctx", None),
        P("section", "ctx", None),
        P("section", None),
        P("section", None),
        P("section", "ctx", None),
        P("section", "ctx", None),
        P("section", "ctx", None),
        P("section", None),
    )
    out_specs = P("section", "ctx", None)
    return jax.shard_map(body, mesh=mesh, in_specs=in_specs, out_specs=out_specs, check_vma=False)
```

```python
import math

import jax
import jax.numpy as jnp
from jax import lax
from jax.experimental import pallas as pl
from jax.experimental.pallas import tpu as pltpu
from jax.sharding import PartitionSpec as P

HEAD_A = 128
STATE = 128
GROUPS = 8
BLOCK = 128
MOST_DOC = 512
Q_BLOCK = 256


norm_eps = 1e-05


def shifted(value, axis, by):
    peers = lax.axis_size(axis)
    pairs = [(i, i + by) for i in range(peers) if 0 <= i + by < peers]
    return lax.ppermute(value, axis, pairs)


def to_heads(row, chunks):
    tok_rows = row.shape[0]
    width = row.shape[1] // chunks
    lead = row.reshape(tok_rows, chunks, width).transpose(1, 0, 2)
    moved = lax.all_to_all(lead, "ctx", split_axis=0, concat_axis=0, tiled=True)
    return moved.reshape(tok_rows * chunks, width)


def to_rows(block, chunks):
    total, width = block.shape
    tok_rows = total // chunks
    moved = lax.all_to_all(block.reshape(chunks, tok_rows, width), "ctx", split_axis=0, concat_axis=0, tiled=True)
    return moved.transpose(1, 0, 2).reshape(tok_rows, chunks * width)


def mixer_heads(x_h, dt_h, bias_h, alog_h, b_g, c_g, skip_h, all_ids, interpret=False):
    total, x_width = x_h.shape
    heads = dt_h.shape[1]
    head_dim = x_width // heads
    nblk = total // BLOCK
    step = jax.nn.softplus(dt_h + bias_h[None, :])
    log_rate = -step * jnp.exp(alog_h)[None, :]
    log_cum = log_rate.reshape(nblk, BLOCK, heads)
    reach = 1
    while reach < BLOCK:
        log_cum = log_cum + jnp.pad(log_cum[:, :-reach], ((0, 0), (reach, 0), (0, 0)))
        reach *= 2
    st = step.reshape(nblk, BLOCK, heads)
    ids = all_ids.reshape(nblk, BLOCK)
    last_id = ids[:, -1]
    prev_last = jnp.concatenate([jnp.full((1,), -1, ids.dtype), last_id[:-1]])
    edge_valid = (ids == prev_last[:, None]).astype(jnp.float32)
    carry_scale = jnp.exp(log_cum) * edge_valid[:, :, None]
    end_scale = (
        jnp.exp(log_cum[:, -1:, :] - log_cum) * st * (ids == last_id[:, None]).astype(jnp.float32)[:, :, None]
    )
    edge_match = (ids[:, 0] == prev_last).astype(jnp.float32)
    block_gain = jnp.exp(log_cum[:, -1, :]) * (ids[:, 0] == last_id).astype(jnp.float32)[:, None]
    block_gain = block_gain * edge_match[:, None]
    gain_rows = jnp.broadcast_to(block_gain[:, :, None], (nblk, heads, head_dim))
    lc_rows = log_cum.transpose(0, 2, 1)
    end_rows = end_scale.transpose(0, 2, 1)
    b_t = b_g.T
    st_rows = st.transpose(0, 2, 1)

    def kernel(x_ref, b_ref, c_ref, lcc_ref, lcr_ref, str_ref, csc_ref, esc_ref, gain_ref,
               idc_ref, idr_ref, skip_ref, o_ref, sq_ref, carry_ref):
        @pl.when(pl.program_id(0) == 0)
        def _():
            carry_ref[...] = jnp.zeros(carry_ref.shape, carry_ref.dtype)

        b_t_blk = b_ref[...]
        c_blk = c_ref[...]
        inner_cb = jnp.dot(c_blk, b_t_blk, preferred_element_type=jnp.float32)
        rows_at = lax.broadcasted_iota(jnp.int32, (BLOCK, BLOCK), 0)
        cols_at = lax.broadcasted_iota(jnp.int32, (BLOCK, BLOCK), 1)
        same_doc = (idc_ref[...] == idr_ref[0]) & (rows_at >= cols_at)
        b_t_f32 = b_t_blk.astype(jnp.float32)
        sq = jnp.zeros((BLOCK, 1), jnp.float32)
        for h in range(heads):
            cols = slice(h * head_dim, (h + 1) * head_dim)
            lc_c = lcc_ref[0, :, h:h + 1]
            lc_r = lcr_ref[0, h:h + 1, :]
            decay = jnp.where(same_doc, jnp.exp(lc_c - lc_r), 0.0)
            intra_w = (decay * inner_cb * str_ref[0, h:h + 1, :]).astype(jnp.bfloat16)
            xh = x_ref[:, cols]
            local = jnp.dot(intra_w, xh, preferred_element_type=jnp.float32)
            state_bf = carry_ref[h].astype(jnp.bfloat16)
            carried = jnp.dot(c_blk, state_bf, preferred_element_type=jnp.float32)
            carried = carried * csc_ref[0, :, h:h + 1]
            out = local + carried + skip_ref[h] * xh.astype(jnp.float32)
            o_ref[:, cols] = out
            sq = sq + jnp.sum(out * out, axis=1, keepdims=True)
            end_w_t = (esc_ref[0, h:h + 1, :] * b_t_f32).astype(jnp.bfloat16)
            block_state = jnp.dot(end_w_t, xh, preferred_element_type=jnp.float32)
            carry_ref[h] = gain_ref[0, h:h + 1, :] * carry_ref[h] + block_state
        sq_ref[...] = sq

    per_block = lambda shape: pl.BlockSpec((1,) + shape, lambda i: (i, 0, 0))
    return pl.pallas_call(
        kernel,
        grid=(nblk,),
        in_specs=[
            pl.BlockSpec((BLOCK, x_width), lambda i: (i, 0)),
            pl.BlockSpec((STATE, BLOCK), lambda i: (0, i)),
            pl.BlockSpec((BLOCK, STATE), lambda i: (i, 0)),
            per_block((BLOCK, heads)),
            per_block((heads, BLOCK)),
            per_block((heads, BLOCK)),
            per_block((BLOCK, heads)),
            per_block((heads, BLOCK)),
            per_block((heads, head_dim)),
            pl.BlockSpec((BLOCK, 1), lambda i: (i, 0)),
            per_block((1, BLOCK)),
            pl.BlockSpec(memory_space=pltpu.SMEM),
        ],
        out_specs=[
            pl.BlockSpec((BLOCK, x_width), lambda i: (i, 0)),
            pl.BlockSpec((BLOCK, 1), lambda i: (i, 0)),
        ],
        out_shape=[
            jax.ShapeDtypeStruct((total, x_width), jnp.float32),
            jax.ShapeDtypeStruct((total, 1), jnp.float32),
        ],
        scratch_shapes=[pltpu.VMEM((heads, STATE, head_dim), jnp.float32)],
        compiler_params=pltpu.CompilerParams(dimension_semantics=("arbitrary",)),
        interpret=interpret,
    )(
        x_h, b_t, c_g, log_cum, lc_rows, st_rows, carry_scale, end_rows, gain_rows,
        all_ids.reshape(total, 1), ids.reshape(nblk, 1, BLOCK), skip_h,
    )


def attend_rows(q_row, kv_win, ids_q, ids_k, interpret=False):
    tok_rows, q_width = q_row.shape
    window = kv_win.shape[0]
    kv_heads = kv_win.shape[1] // (2 * HEAD_A)
    group = q_width // HEAD_A // kv_heads
    lead = window - tok_rows
    inv_sqrt = 1.0 / math.sqrt(HEAD_A)

    def kernel(q_ref, k_ref, v_ref, iq_ref, ik_ref, o_ref):
        q_at = lead + lax.broadcasted_iota(jnp.int32, (tok_rows, window), 0)
        k_at = lax.broadcasted_iota(jnp.int32, (tok_rows, window), 1)
        allowed = (iq_ref[...] == ik_ref[...]) & (q_at >= k_at)
        kb = k_ref[...]
        vb = v_ref[...]
        for g in range(group):
            cols = slice(g * HEAD_A, (g + 1) * HEAD_A)
            logits = lax.dot_general(
                q_ref[:, cols], kb, (((1,), (1,)), ((), ())), preferred_element_type=jnp.float32
            ) * inv_sqrt
            logits = jnp.where(allowed, logits, -jnp.inf)
            row_max = jnp.max(logits, axis=1, keepdims=True)
            exp_terms = jnp.exp(logits - row_max)
            probs = (exp_terms / jnp.sum(exp_terms, axis=1, keepdims=True)).astype(jnp.bfloat16)
            o_ref[:, cols] = jnp.dot(probs, vb, preferred_element_type=jnp.float32).astype(o_ref.dtype)

    return pl.pallas_call(
        kernel,
        grid=(kv_heads,),
        in_specs=[
            pl.BlockSpec((tok_rows, group * HEAD_A), lambda i: (0, i)),
            pl.BlockSpec((window, HEAD_A), lambda i: (0, i)),
            pl.BlockSpec((window, HEAD_A), lambda i: (0, kv_heads + i)),
            pl.BlockSpec((tok_rows, 1), lambda i: (0, 0)),
            pl.BlockSpec((1, window), lambda i: (0, 0)),
        ],
        out_specs=pl.BlockSpec((tok_rows, group * HEAD_A), lambda i: (0, i)),
        out_shape=jax.ShapeDtypeStruct((tok_rows, q_width), jnp.bfloat16),
        interpret=interpret,
    )(q_row, kv_win, kv_win, ids_q, ids_k)


def body(
    previous,
    fresh,
    dt_raw,
    dt_bias,
    a_log,
    b_in,
    c_in,
    skip_d,
    norm_gain,
    queries,
    keys,
    values,
    doc_ids,
):
    tok_rows, width = fresh.shape
    nctx = lax.axis_size("ctx")
    me = lax.axis_index("ctx")
    total = tok_rows * nctx
    part = width // nctx
    mamba_heads = dt_raw.shape[2]
    heads_dev = mamba_heads // nctx
    head_dim = width // mamba_heads
    kv_heads = keys.shape[2] // HEAD_A
    qpd = part // HEAD_A

    rep = nctx // kv_heads
    bc = jnp.stack(
        [b_in[0].reshape(tok_rows, GROUPS, STATE), c_in[0].reshape(tok_rows, GROUPS, STATE)], axis=2
    )
    bc_rows = jnp.repeat(bc, rep, axis=1).reshape(tok_rows, nctx, 2 * STATE)
    dt_h = to_heads(dt_raw[0], nctx)

    handed = shifted(previous[0], "section", 1)
    stream = jnp.where(lax.axis_index("section") == 0, fresh, handed)
    joined = jnp.concatenate([stream.reshape(tok_rows, nctx, part), bc_rows], axis=2)
    moved = to_heads(joined.reshape(tok_rows, nctx * (part + 2 * STATE)), nctx)
    x_h = moved[:, :part]
    b_g, c_g = moved[:, part:part + STATE], moved[:, part + STATE:]

    halo = -(-MOST_DOC // tok_rows)
    kv_row = jnp.concatenate([keys[0], values[0]], axis=1)
    kv_win = jnp.concatenate([shifted(kv_row, "ctx", by) for by in range(halo, 0, -1)] + [kv_row], axis=0)
    kv_win, x_h = lax.optimization_barrier((kv_win, x_h))
    all_ids = doc_ids[0]
    lead = halo * tok_rows
    padded_ids = jnp.concatenate([jnp.full((lead,), -1, all_ids.dtype), all_ids])
    ids_k = lax.dynamic_slice_in_dim(padded_ids, me * tok_rows, lead + tok_rows)
    ids_q = lax.dynamic_slice_in_dim(all_ids, me * tok_rows, tok_rows)

    bias_h = lax.dynamic_slice_in_dim(dt_bias[0], me * heads_dev, heads_dev)
    alog_h = lax.dynamic_slice_in_dim(a_log[0], me * heads_dev, heads_dev)
    skip_h = lax.dynamic_slice_in_dim(skip_d[0], me * heads_dev, heads_dev)
    gain_h = lax.dynamic_slice_in_dim(norm_gain[0], me * part, part)

    mixer_out, sq_part = mixer_heads(x_h, dt_h, bias_h, alog_h, b_g, c_g, skip_h, all_ids)
    attended = attend_rows(queries[0], kv_win, ids_q.reshape(tok_rows, 1), ids_k.reshape(1, lead + tok_rows))
    sq_all = lax.all_to_all(
        jnp.broadcast_to(sq_part[:, 0][None], (nctx, total)), "ctx", split_axis=0, concat_axis=0, tiled=True
    )
    mean_sq = (jnp.sum(sq_all, axis=0) / width)[:, None]
    inv_rms = lax.rsqrt(mean_sq + norm_eps)
    mixed = (
        x_h.astype(jnp.float32) + mixer_out * inv_rms * gain_h.astype(jnp.float32)[None, :]
    ).astype(jnp.bfloat16)
    mixed_rows = to_rows(mixed, nctx)
    return (mixed_rows.astype(jnp.float32) + attended.astype(jnp.float32)).astype(jnp.bfloat16)[None]


def solution(mesh):
    in_specs = (
        P("section", "ctx", None),
        P("ctx", None),
        P("section", "ctx", None),
        P("section", None),
        P("section", None),
        P("section", "ctx", None),
        P("section", "ctx", None),
        P("section", None),
        P("section", None),
        P("section", "ctx", None),
        P("section", "ctx", None),
        P("section", "ctx", None),
        P("section", None),
    )
    out_specs = P("section", "ctx", None)
    return jax.shard_map(body, mesh=mesh, in_specs=in_specs, out_specs=out_specs, check_vma=False)
```

```python
import math

import jax
import jax.numpy as jnp
from jax import lax
from jax.experimental import pallas as pl
from jax.experimental.pallas import tpu as pltpu
from jax.sharding import PartitionSpec as P

HEAD_A = 128
STATE = 128
GROUPS = 8
BLOCK = 128
MOST_DOC = 512
Q_BLOCK = 256


norm_eps = 1e-05


def shifted(value, axis, by):
    peers = lax.axis_size(axis)
    pairs = [(i, i + by) for i in range(peers) if 0 <= i + by < peers]
    return lax.ppermute(value, axis, pairs)


def to_heads(row, chunks):
    tok_rows = row.shape[0]
    width = row.shape[1] // chunks
    lead = row.reshape(tok_rows, chunks, width).transpose(1, 0, 2)
    moved = lax.all_to_all(lead, "ctx", split_axis=0, concat_axis=0, tiled=True)
    return moved.reshape(tok_rows * chunks, width)


def to_rows(block, chunks):
    total, width = block.shape
    tok_rows = total // chunks
    moved = lax.all_to_all(block.reshape(chunks, tok_rows, width), "ctx", split_axis=0, concat_axis=0, tiled=True)
    return moved.transpose(1, 0, 2).reshape(tok_rows, chunks * width)


def mixer_heads(x_h, dt_h, bias_h, alog_h, b_g, c_g, skip_h, all_ids, interpret=False):
    total, x_width = x_h.shape
    heads = dt_h.shape[1]
    head_dim = x_width // heads
    nblk = total // BLOCK
    step = jax.nn.softplus(dt_h + bias_h[None, :])
    log_rate = -step * jnp.exp(alog_h)[None, :]
    log_cum = log_rate.reshape(nblk, BLOCK, heads)
    reach = 1
    while reach < BLOCK:
        log_cum = log_cum + jnp.pad(log_cum[:, :-reach], ((0, 0), (reach, 0), (0, 0)))
        reach *= 2
    st = step.reshape(nblk, BLOCK, heads)
    ids = all_ids.reshape(nblk, BLOCK)
    last_id = ids[:, -1]
    prev_last = jnp.concatenate([jnp.full((1,), -1, ids.dtype), last_id[:-1]])
    edge_valid = (ids == prev_last[:, None]).astype(jnp.float32)
    carry_scale = jnp.exp(log_cum) * edge_valid[:, :, None]
    end_scale = (
        jnp.exp(log_cum[:, -1:, :] - log_cum) * st * (ids == last_id[:, None]).astype(jnp.float32)[:, :, None]
    )
    edge_match = (ids[:, 0] == prev_last).astype(jnp.float32)
    block_gain = jnp.exp(log_cum[:, -1, :]) * (ids[:, 0] == last_id).astype(jnp.float32)[:, None]
    block_gain = block_gain * edge_match[:, None]
    gain_rows = jnp.broadcast_to(block_gain[:, :, None], (nblk, heads, head_dim))
    lc_rows = log_cum.transpose(0, 2, 1)
    end_rows = end_scale.transpose(0, 2, 1)
    b_t = b_g.T
    st_rows = st.transpose(0, 2, 1)

    def kernel(x_ref, b_ref, c_ref, lcc_ref, lcr_ref, str_ref, csc_ref, esc_ref, gain_ref,
               idc_ref, idr_ref, skip_ref, o_ref, sq_ref, carry_ref):
        @pl.when(pl.program_id(0) == 0)
        def _():
            carry_ref[...] = jnp.zeros(carry_ref.shape, carry_ref.dtype)

        b_t_blk = b_ref[...]
        c_blk = c_ref[...]
        inner_cb = jnp.dot(c_blk, b_t_blk, preferred_element_type=jnp.float32)
        rows_at = lax.broadcasted_iota(jnp.int32, (BLOCK, BLOCK), 0)
        cols_at = lax.broadcasted_iota(jnp.int32, (BLOCK, BLOCK), 1)
        same_doc = (idc_ref[...] == idr_ref[0]) & (rows_at >= cols_at)
        b_t_f32 = b_t_blk.astype(jnp.float32)
        sq = jnp.zeros((BLOCK, 1), jnp.float32)
        for h in range(heads):
            cols = slice(h * head_dim, (h + 1) * head_dim)
            lc_c = lcc_ref[0, :, h:h + 1]
            lc_r = lcr_ref[0, h:h + 1, :]
            decay = jnp.where(same_doc, jnp.exp(lc_c - lc_r), 0.0)
            intra_w = (decay * inner_cb * str_ref[0, h:h + 1, :]).astype(jnp.bfloat16)
            xh = x_ref[:, cols]
            local = jnp.dot(intra_w, xh, preferred_element_type=jnp.float32)
            state_bf = carry_ref[h].astype(jnp.bfloat16)
            carried = jnp.dot(c_blk, state_bf, preferred_element_type=jnp.float32)
            carried = carried * csc_ref[0, :, h:h + 1]
            out = local + carried + skip_ref[h] * xh.astype(jnp.float32)
            o_ref[:, cols] = out
            sq = sq + jnp.sum(out * out, axis=1, keepdims=True)
            end_w_t = (esc_ref[0, h:h + 1, :] * b_t_f32).astype(jnp.bfloat16)
            block_state = jnp.dot(end_w_t, xh, preferred_element_type=jnp.float32)
            carry_ref[h] = gain_ref[0, h:h + 1, :] * carry_ref[h] + block_state
        sq_ref[...] = sq

    per_block = lambda shape: pl.BlockSpec((1,) + shape, lambda i: (i, 0, 0))
    return pl.pallas_call(
        kernel,
        grid=(nblk,),
        in_specs=[
            pl.BlockSpec((BLOCK, x_width), lambda i: (i, 0)),
            pl.BlockSpec((STATE, BLOCK), lambda i: (0, i)),
            pl.BlockSpec((BLOCK, STATE), lambda i: (i, 0)),
            per_block((BLOCK, heads)),
            per_block((heads, BLOCK)),
            per_block((heads, BLOCK)),
            per_block((BLOCK, heads)),
            per_block((heads, BLOCK)),
            per_block((heads, head_dim)),
            pl.BlockSpec((BLOCK, 1), lambda i: (i, 0)),
            per_block((1, BLOCK)),
            pl.BlockSpec(memory_space=pltpu.SMEM),
        ],
        out_specs=[
            pl.BlockSpec((BLOCK, x_width), lambda i: (i, 0)),
            pl.BlockSpec((BLOCK, 1), lambda i: (i, 0)),
        ],
        out_shape=[
            jax.ShapeDtypeStruct((total, x_width), jnp.float32),
            jax.ShapeDtypeStruct((total, 1), jnp.float32),
        ],
        scratch_shapes=[pltpu.VMEM((heads, STATE, head_dim), jnp.float32)],
        compiler_params=pltpu.CompilerParams(dimension_semantics=("arbitrary",)),
        interpret=interpret,
    )(
        x_h, b_t, c_g, log_cum, lc_rows, st_rows, carry_scale, end_rows, gain_rows,
        all_ids.reshape(total, 1), ids.reshape(nblk, 1, BLOCK), skip_h,
    )


def attend_rows(q_row, kv_win, ids_q, ids_k, interpret=False):
    tok_rows, q_width = q_row.shape
    window = kv_win.shape[0]
    kv_heads = kv_win.shape[1] // (2 * HEAD_A)
    group = q_width // HEAD_A // kv_heads
    lead = window - tok_rows
    inv_sqrt = 1.0 / math.sqrt(HEAD_A)

    def kernel(q_ref, k_ref, v_ref, iq_ref, ik_ref, o_ref):
        q_at = lead + lax.broadcasted_iota(jnp.int32, (tok_rows, window), 0)
        k_at = lax.broadcasted_iota(jnp.int32, (tok_rows, window), 1)
        allowed = (iq_ref[...] == ik_ref[...]) & (q_at >= k_at)
        kb = k_ref[...]
        vb = v_ref[...]
        for g in range(group):
            cols = slice(g * HEAD_A, (g + 1) * HEAD_A)
            logits = lax.dot_general(
                q_ref[:, cols], kb, (((1,), (1,)), ((), ())), preferred_element_type=jnp.float32
            ) * inv_sqrt
            logits = jnp.where(allowed, logits, -jnp.inf)
            row_max = jnp.max(logits, axis=1, keepdims=True)
            exp_terms = jnp.exp(logits - row_max)
            inv_sum = 1.0 / jnp.sum(exp_terms, axis=1, keepdims=True)
            probs = (exp_terms * inv_sum).astype(jnp.bfloat16)
            o_ref[:, cols] = jnp.dot(probs, vb, preferred_element_type=jnp.float32).astype(o_ref.dtype)

    return pl.pallas_call(
        kernel,
        grid=(kv_heads,),
        in_specs=[
            pl.BlockSpec((tok_rows, group * HEAD_A), lambda i: (0, i)),
            pl.BlockSpec((window, HEAD_A), lambda i: (0, i)),
            pl.BlockSpec((window, HEAD_A), lambda i: (0, kv_heads + i)),
            pl.BlockSpec((tok_rows, 1), lambda i: (0, 0)),
            pl.BlockSpec((1, window), lambda i: (0, 0)),
        ],
        out_specs=pl.BlockSpec((tok_rows, group * HEAD_A), lambda i: (0, i)),
        out_shape=jax.ShapeDtypeStruct((tok_rows, q_width), jnp.bfloat16),
        interpret=interpret,
    )(q_row, kv_win, kv_win, ids_q, ids_k)


def body(
    previous,
    fresh,
    dt_raw,
    dt_bias,
    a_log,
    b_in,
    c_in,
    skip_d,
    norm_gain,
    queries,
    keys,
    values,
    doc_ids,
):
    tok_rows, width = fresh.shape
    nctx = lax.axis_size("ctx")
    me = lax.axis_index("ctx")
    total = tok_rows * nctx
    part = width // nctx
    mamba_heads = dt_raw.shape[2]
    heads_dev = mamba_heads // nctx
    head_dim = width // mamba_heads
    kv_heads = keys.shape[2] // HEAD_A
    qpd = part // HEAD_A

    rep = nctx // kv_heads
    bc = jnp.stack(
        [b_in[0].reshape(tok_rows, GROUPS, STATE), c_in[0].reshape(tok_rows, GROUPS, STATE)], axis=2
    )
    bc_h = to_heads(jnp.repeat(bc, rep, axis=1).reshape(tok_rows, nctx * 2 * STATE), nctx)
    b_g, c_g = bc_h[:, :STATE], bc_h[:, STATE:]
    dt_h = to_heads(dt_raw[0], nctx)

    handed = shifted(previous[0], "section", 1)
    stream = jnp.where(lax.axis_index("section") == 0, fresh, handed)
    x_h = to_heads(stream, nctx)

    halo = -(-MOST_DOC // tok_rows)
    kv_row = jnp.concatenate([keys[0], values[0]], axis=1)
    kv_win = jnp.concatenate([shifted(kv_row, "ctx", by) for by in range(halo, 0, -1)] + [kv_row], axis=0)
    kv_win, x_h = lax.optimization_barrier((kv_win, x_h))
    all_ids = doc_ids[0]
    lead = halo * tok_rows
    padded_ids = jnp.concatenate([jnp.full((lead,), -1, all_ids.dtype), all_ids])
    ids_k = lax.dynamic_slice_in_dim(padded_ids, me * tok_rows, lead + tok_rows)
    ids_q = lax.dynamic_slice_in_dim(all_ids, me * tok_rows, tok_rows)

    bias_h = lax.dynamic_slice_in_dim(dt_bias[0], me * heads_dev, heads_dev)
    alog_h = lax.dynamic_slice_in_dim(a_log[0], me * heads_dev, heads_dev)
    skip_h = lax.dynamic_slice_in_dim(skip_d[0], me * heads_dev, heads_dev)
    gain_h = lax.dynamic_slice_in_dim(norm_gain[0], me * part, part)

    mixer_out, sq_part = mixer_heads(x_h, dt_h, bias_h, alog_h, b_g, c_g, skip_h, all_ids)
    attended = attend_rows(queries[0], kv_win, ids_q.reshape(tok_rows, 1), ids_k.reshape(1, lead + tok_rows))
    sq_all = lax.all_to_all(
        jnp.broadcast_to(sq_part[:, 0][None], (nctx, total)), "ctx", split_axis=0, concat_axis=0, tiled=True
    )
    mean_sq = (jnp.sum(sq_all, axis=0) / width)[:, None]
    inv_rms = lax.rsqrt(mean_sq + norm_eps)
    mixed = (
        x_h.astype(jnp.float32) + mixer_out * inv_rms * gain_h.astype(jnp.float32)[None, :]
    ).astype(jnp.bfloat16)
    mixed_rows = to_rows(mixed, nctx)
    return (mixed_rows.astype(jnp.float32) + attended.astype(jnp.float32)).astype(jnp.bfloat16)[None]


def solution(mesh):
    in_specs = (
        P("section", "ctx", None),
        P("ctx", None),
        P("section", "ctx", None),
        P("section", None),
        P("section", None),
        P("section", "ctx", None),
        P("section", "ctx", None),
        P("section", None),
        P("section", None),
        P("section", "ctx", None),
        P("section", "ctx", None),
        P("section", "ctx", None),
        P("section", None),
    )
    out_specs = P("section", "ctx", None)
    return jax.shard_map(body, mesh=mesh, in_specs=in_specs, out_specs=out_specs, check_vma=False)
```

```python
import math

import jax
import jax.numpy as jnp
from jax import lax
from jax.experimental import pallas as pl
from jax.experimental.pallas import tpu as pltpu
from jax.sharding import PartitionSpec as P

HEAD_A = 128
STATE = 128
GROUPS = 8
BLOCK = 128
MOST_DOC = 512
Q_BLOCK = 256


norm_eps = 1e-05


def shifted(value, axis, by):
    peers = lax.axis_size(axis)
    pairs = [(i, i + by) for i in range(peers) if 0 <= i + by < peers]
    return lax.ppermute(value, axis, pairs)


def to_heads(row, chunks):
    tok_rows = row.shape[0]
    width = row.shape[1] // chunks
    lead = row.reshape(tok_rows, chunks, width).transpose(1, 0, 2)
    moved = lax.all_to_all(lead, "ctx", split_axis=0, concat_axis=0, tiled=True)
    return moved.reshape(tok_rows * chunks, width)


def to_rows(block, chunks):
    total, width = block.shape
    tok_rows = total // chunks
    moved = lax.all_to_all(block.reshape(chunks, tok_rows, width), "ctx", split_axis=0, concat_axis=0, tiled=True)
    return moved.transpose(1, 0, 2).reshape(tok_rows, chunks * width)


def mixer_heads(x_h, dt_h, bias_h, alog_h, b_g, c_g, skip_h, all_ids, interpret=False):
    total, x_width = x_h.shape
    heads = dt_h.shape[1]
    head_dim = x_width // heads
    nblk = total // BLOCK
    step = jax.nn.softplus(dt_h + bias_h[None, :])
    log_rate = -step * jnp.exp(alog_h)[None, :]
    log_cum = log_rate.reshape(nblk, BLOCK, heads)
    reach = 1
    while reach < BLOCK:
        log_cum = log_cum + jnp.pad(log_cum[:, :-reach], ((0, 0), (reach, 0), (0, 0)))
        reach *= 2
    st = step.reshape(nblk, BLOCK, heads)
    ids = all_ids.reshape(nblk, BLOCK)
    last_id = ids[:, -1]
    prev_last = jnp.concatenate([jnp.full((1,), -1, ids.dtype), last_id[:-1]])
    edge_valid = (ids == prev_last[:, None]).astype(jnp.float32)
    carry_scale = jnp.exp(log_cum) * edge_valid[:, :, None]
    end_scale = (
        jnp.exp(log_cum[:, -1:, :] - log_cum) * st * (ids == last_id[:, None]).astype(jnp.float32)[:, :, None]
    )
    edge_match = (ids[:, 0] == prev_last).astype(jnp.float32)
    block_gain = jnp.exp(log_cum[:, -1, :]) * (ids[:, 0] == last_id).astype(jnp.float32)[:, None]
    block_gain = block_gain * edge_match[:, None]
    gain_rows = jnp.broadcast_to(block_gain[:, :, None], (nblk, heads, head_dim))
    lc_rows = log_cum.transpose(0, 2, 1)
    end_rows = end_scale.transpose(0, 2, 1)
    b_t = b_g.T
    st_rows = st.transpose(0, 2, 1)

    sub = 2 if nblk % 2 == 0 else 1
    span = sub * BLOCK

    def kernel(x_ref, b_ref, c_ref, lcc_ref, lcr_ref, str_ref, csc_ref, esc_ref, gain_ref,
               idc_ref, idr_ref, skip_ref, o_ref, sq_ref, carry_ref):
        @pl.when(pl.program_id(0) == 0)
        def _():
            carry_ref[...] = jnp.zeros(carry_ref.shape, carry_ref.dtype)

        rows_at = lax.broadcasted_iota(jnp.int32, (BLOCK, BLOCK), 0)
        cols_at = lax.broadcasted_iota(jnp.int32, (BLOCK, BLOCK), 1)
        for s in range(sub):
            rows = slice(s * BLOCK, (s + 1) * BLOCK)
            b_t_blk = b_ref[:, rows]
            c_blk = c_ref[rows, :]
            inner_cb = jnp.dot(c_blk, b_t_blk, preferred_element_type=jnp.float32)
            same_doc = (idc_ref[rows, :] == idr_ref[s]) & (rows_at >= cols_at)
            b_t_f32 = b_t_blk.astype(jnp.float32)
            sq = jnp.zeros((BLOCK, 1), jnp.float32)
            for h in range(heads):
                cols = slice(h * head_dim, (h + 1) * head_dim)
                lc_c = lcc_ref[s, :, h:h + 1]
                lc_r = lcr_ref[s, h:h + 1, :]
                decay = jnp.where(same_doc, jnp.exp(lc_c - lc_r), 0.0)
                intra_w = (decay * inner_cb * str_ref[s, h:h + 1, :]).astype(jnp.bfloat16)
                xh = x_ref[rows, cols]
                local = jnp.dot(intra_w, xh, preferred_element_type=jnp.float32)
                state_bf = carry_ref[h].astype(jnp.bfloat16)
                carried = jnp.dot(c_blk, state_bf, preferred_element_type=jnp.float32)
                carried = carried * csc_ref[s, :, h:h + 1]
                out = local + carried + skip_ref[h] * xh.astype(jnp.float32)
                o_ref[rows, cols] = out
                sq = sq + jnp.sum(out * out, axis=1, keepdims=True)
                end_w_t = (esc_ref[s, h:h + 1, :] * b_t_f32).astype(jnp.bfloat16)
                block_state = jnp.dot(end_w_t, xh, preferred_element_type=jnp.float32)
                carry_ref[h] = gain_ref[s, h:h + 1, :] * carry_ref[h] + block_state
            sq_ref[rows, :] = sq

    per_block = lambda shape: pl.BlockSpec((sub,) + shape, lambda i: (i, 0, 0))
    return pl.pallas_call(
        kernel,
        grid=(nblk // sub,),
        in_specs=[
            pl.BlockSpec((span, x_width), lambda i: (i, 0)),
            pl.BlockSpec((STATE, span), lambda i: (0, i)),
            pl.BlockSpec((span, STATE), lambda i: (i, 0)),
            per_block((BLOCK, heads)),
            per_block((heads, BLOCK)),
            per_block((heads, BLOCK)),
            per_block((BLOCK, heads)),
            per_block((heads, BLOCK)),
            per_block((heads, head_dim)),
            pl.BlockSpec((span, 1), lambda i: (i, 0)),
            per_block((1, BLOCK)),
            pl.BlockSpec(memory_space=pltpu.SMEM),
        ],
        out_specs=[
            pl.BlockSpec((span, x_width), lambda i: (i, 0)),
            pl.BlockSpec((span, 1), lambda i: (i, 0)),
        ],
        out_shape=[
            jax.ShapeDtypeStruct((total, x_width), jnp.float32),
            jax.ShapeDtypeStruct((total, 1), jnp.float32),
        ],
        scratch_shapes=[pltpu.VMEM((heads, STATE, head_dim), jnp.float32)],
        compiler_params=pltpu.CompilerParams(dimension_semantics=("arbitrary",)),
        interpret=interpret,
    )(
        x_h, b_t, c_g, log_cum, lc_rows, st_rows, carry_scale, end_rows, gain_rows,
        all_ids.reshape(total, 1), ids.reshape(nblk, 1, BLOCK), skip_h,
    )


def attend_rows(q_row, kv_win, ids_q, ids_k, interpret=False):
    tok_rows, q_width = q_row.shape
    window = kv_win.shape[0]
    kv_heads = kv_win.shape[1] // (2 * HEAD_A)
    group = q_width // HEAD_A // kv_heads
    lead = window - tok_rows
    inv_sqrt = 1.0 / math.sqrt(HEAD_A)

    def kernel(q_ref, k_ref, v_ref, iq_ref, ik_ref, o_ref):
        q_at = lead + lax.broadcasted_iota(jnp.int32, (tok_rows, window), 0)
        k_at = lax.broadcasted_iota(jnp.int32, (tok_rows, window), 1)
        allowed = (iq_ref[...] == ik_ref[...]) & (q_at >= k_at)
        kb = k_ref[...]
        vb = v_ref[...]
        for g in range(group):
            cols = slice(g * HEAD_A, (g + 1) * HEAD_A)
            logits = lax.dot_general(
                q_ref[:, cols], kb, (((1,), (1,)), ((), ())), preferred_element_type=jnp.float32
            ) * inv_sqrt
            logits = jnp.where(allowed, logits, -jnp.inf)
            row_max = jnp.max(logits, axis=1, keepdims=True)
            exp_terms = jnp.exp(logits - row_max)
            probs = (exp_terms / jnp.sum(exp_terms, axis=1, keepdims=True)).astype(jnp.bfloat16)
            o_ref[:, cols] = jnp.dot(probs, vb, preferred_element_type=jnp.float32).astype(o_ref.dtype)

    return pl.pallas_call(
        kernel,
        grid=(kv_heads,),
        in_specs=[
            pl.BlockSpec((tok_rows, group * HEAD_A), lambda i: (0, i)),
            pl.BlockSpec((window, HEAD_A), lambda i: (0, i)),
            pl.BlockSpec((window, HEAD_A), lambda i: (0, kv_heads + i)),
            pl.BlockSpec((tok_rows, 1), lambda i: (0, 0)),
            pl.BlockSpec((1, window), lambda i: (0, 0)),
        ],
        out_specs=pl.BlockSpec((tok_rows, group * HEAD_A), lambda i: (0, i)),
        out_shape=jax.ShapeDtypeStruct((tok_rows, q_width), jnp.bfloat16),
        interpret=interpret,
    )(q_row, kv_win, kv_win, ids_q, ids_k)


def body(
    previous,
    fresh,
    dt_raw,
    dt_bias,
    a_log,
    b_in,
    c_in,
    skip_d,
    norm_gain,
    queries,
    keys,
    values,
    doc_ids,
):
    tok_rows, width = fresh.shape
    nctx = lax.axis_size("ctx")
    me = lax.axis_index("ctx")
    total = tok_rows * nctx
    part = width // nctx
    mamba_heads = dt_raw.shape[2]
    heads_dev = mamba_heads // nctx
    head_dim = width // mamba_heads
    kv_heads = keys.shape[2] // HEAD_A
    qpd = part // HEAD_A

    rep = nctx // kv_heads
    bc = jnp.stack(
        [b_in[0].reshape(tok_rows, GROUPS, STATE), c_in[0].reshape(tok_rows, GROUPS, STATE)], axis=2
    )
    bc_h = to_heads(jnp.repeat(bc, rep, axis=1).reshape(tok_rows, nctx * 2 * STATE), nctx)
    b_g, c_g = bc_h[:, :STATE], bc_h[:, STATE:]
    dt_h = to_heads(dt_raw[0], nctx)

    handed = shifted(previous[0], "section", 1)
    stream = jnp.where(lax.axis_index("section") == 0, fresh, handed)
    x_h = to_heads(stream, nctx)

    halo = -(-MOST_DOC // tok_rows)
    kv_row = jnp.concatenate([keys[0], values[0]], axis=1)
    kv_win = jnp.concatenate([shifted(kv_row, "ctx", by) for by in range(halo, 0, -1)] + [kv_row], axis=0)
    kv_win, x_h = lax.optimization_barrier((kv_win, x_h))
    all_ids = doc_ids[0]
    lead = halo * tok_rows
    padded_ids = jnp.concatenate([jnp.full((lead,), -1, all_ids.dtype), all_ids])
    ids_k = lax.dynamic_slice_in_dim(padded_ids, me * tok_rows, lead + tok_rows)
    ids_q = lax.dynamic_slice_in_dim(all_ids, me * tok_rows, tok_rows)

    bias_h = lax.dynamic_slice_in_dim(dt_bias[0], me * heads_dev, heads_dev)
    alog_h = lax.dynamic_slice_in_dim(a_log[0], me * heads_dev, heads_dev)
    skip_h = lax.dynamic_slice_in_dim(skip_d[0], me * heads_dev, heads_dev)
    gain_h = lax.dynamic_slice_in_dim(norm_gain[0], me * part, part)

    mixer_out, sq_part = mixer_heads(x_h, dt_h, bias_h, alog_h, b_g, c_g, skip_h, all_ids)
    attended = attend_rows(queries[0], kv_win, ids_q.reshape(tok_rows, 1), ids_k.reshape(1, lead + tok_rows))
    sq_all = lax.all_to_all(
        jnp.broadcast_to(sq_part[:, 0][None], (nctx, total)), "ctx", split_axis=0, concat_axis=0, tiled=True
    )
    mean_sq = (jnp.sum(sq_all, axis=0) / width)[:, None]
    inv_rms = lax.rsqrt(mean_sq + norm_eps)
    mixed = (
        x_h.astype(jnp.float32) + mixer_out * inv_rms * gain_h.astype(jnp.float32)[None, :]
    ).astype(jnp.bfloat16)
    mixed_rows = to_rows(mixed, nctx)
    return (mixed_rows.astype(jnp.float32) + attended.astype(jnp.float32)).astype(jnp.bfloat16)[None]


def solution(mesh):
    in_specs = (
        P("section", "ctx", None),
        P("ctx", None),
        P("section", "ctx", None),
        P("section", None),
        P("section", None),
        P("section", "ctx", None),
        P("section", "ctx", None),
        P("section", None),
        P("section", None),
        P("section", "ctx", None),
        P("section", "ctx", None),
        P("section", "ctx", None),
        P("section", None),
    )
    out_specs = P("section", "ctx", None)
    return jax.shard_map(body, mesh=mesh, in_specs=in_specs, out_specs=out_specs, check_vma=False)
```

```python
import math

import jax
import jax.numpy as jnp
from jax import lax
from jax.experimental import pallas as pl
from jax.experimental.pallas import tpu as pltpu
from jax.sharding import PartitionSpec as P

HEAD_A = 128
STATE = 128
GROUPS = 8
BLOCK = 128
MOST_DOC = 512
Q_BLOCK = 256


norm_eps = 1e-05


def shifted(value, axis, by):
    peers = lax.axis_size(axis)
    pairs = [(i, i + by) for i in range(peers) if 0 <= i + by < peers]
    return lax.ppermute(value, axis, pairs)


def to_heads(row, chunks):
    tok_rows = row.shape[0]
    width = row.shape[1] // chunks
    lead = row.reshape(tok_rows, chunks, width).transpose(1, 0, 2)
    moved = lax.all_to_all(lead, "ctx", split_axis=0, concat_axis=0, tiled=True)
    return moved.reshape(tok_rows * chunks, width)


def to_rows(block, chunks):
    total, width = block.shape
    tok_rows = total // chunks
    moved = lax.all_to_all(block.reshape(chunks, tok_rows, width), "ctx", split_axis=0, concat_axis=0, tiled=True)
    return moved.transpose(1, 0, 2).reshape(tok_rows, chunks * width)


def mixer_heads(x_h, dt_h, bias_h, alog_h, b_g, c_g, skip_h, all_ids, interpret=False):
    total, x_width = x_h.shape
    heads = dt_h.shape[1]
    head_dim = x_width // heads
    nblk = total // BLOCK
    step = jax.nn.softplus(dt_h + bias_h[None, :])
    log_rate = -step * jnp.exp(alog_h)[None, :]
    log_cum = log_rate.reshape(nblk, BLOCK, heads)
    reach = 1
    while reach < BLOCK:
        log_cum = log_cum + jnp.pad(log_cum[:, :-reach], ((0, 0), (reach, 0), (0, 0)))
        reach *= 2
    st = step.reshape(nblk, BLOCK, heads)
    ids = all_ids.reshape(nblk, BLOCK)
    last_id = ids[:, -1]
    prev_last = jnp.concatenate([jnp.full((1,), -1, ids.dtype), last_id[:-1]])
    edge_valid = (ids == prev_last[:, None]).astype(jnp.float32)
    carry_scale = jnp.exp(log_cum) * edge_valid[:, :, None]
    end_scale = (
        jnp.exp(log_cum[:, -1:, :] - log_cum) * st * (ids == last_id[:, None]).astype(jnp.float32)[:, :, None]
    )
    edge_match = (ids[:, 0] == prev_last).astype(jnp.float32)
    block_gain = jnp.exp(log_cum[:, -1, :]) * (ids[:, 0] == last_id).astype(jnp.float32)[:, None]
    block_gain = block_gain * edge_match[:, None]
    gain_rows = jnp.broadcast_to(block_gain[:, :, None], (nblk, heads, head_dim))
    lc_rows = log_cum.transpose(0, 2, 1)
    end_rows = end_scale.transpose(0, 2, 1)
    b_t = b_g.T
    st_rows = st.transpose(0, 2, 1)

    def kernel(x_ref, b_ref, c_ref, lcc_ref, lcr_ref, str_ref, csc_ref, esc_ref, gain_ref,
               idc_ref, idr_ref, skip_ref, o_ref, sq_ref, carry_ref):
        @pl.when(pl.program_id(0) == 0)
        def _():
            carry_ref[...] = jnp.zeros(carry_ref.shape, carry_ref.dtype)

        b_t_blk = b_ref[...]
        c_blk = c_ref[...]
        inner_cb = jnp.dot(c_blk, b_t_blk, preferred_element_type=jnp.float32)
        rows_at = lax.broadcasted_iota(jnp.int32, (BLOCK, BLOCK), 0)
        cols_at = lax.broadcasted_iota(jnp.int32, (BLOCK, BLOCK), 1)
        same_doc = (idc_ref[...] == idr_ref[0]) & (rows_at >= cols_at)
        b_t_f32 = b_t_blk.astype(jnp.float32)
        sq = jnp.zeros((BLOCK, 1), jnp.float32)
        for h in range(heads):
            cols = slice(h * head_dim, (h + 1) * head_dim)
            lc_c = lcc_ref[0, :, h:h + 1]
            lc_r = lcr_ref[0, h:h + 1, :]
            decay = jnp.where(same_doc, jnp.exp(lc_c - lc_r), 0.0)
            intra_w = (decay * inner_cb * str_ref[0, h:h + 1, :]).astype(jnp.bfloat16)
            xh = x_ref[:, cols]
            local = jnp.dot(intra_w, xh, preferred_element_type=jnp.float32)
            state_bf = carry_ref[h].astype(jnp.bfloat16)
            carried = jnp.dot(c_blk, state_bf, preferred_element_type=jnp.float32)
            carried = carried * csc_ref[0, :, h:h + 1]
            out = local + carried + skip_ref[h] * xh.astype(jnp.float32)
            o_ref[:, cols] = out
            sq = sq + jnp.sum(out * out, axis=1, keepdims=True)
            end_w_t = (esc_ref[0, h:h + 1, :] * b_t_f32).astype(jnp.bfloat16)
            block_state = jnp.dot(end_w_t, xh, preferred_element_type=jnp.float32)
            carry_ref[h] = gain_ref[0, h:h + 1, :] * carry_ref[h] + block_state
        sq_ref[...] = sq

    per_block = lambda shape: pl.BlockSpec((1,) + shape, lambda i: (i, 0, 0))
    return pl.pallas_call(
        kernel,
        grid=(nblk,),
        in_specs=[
            pl.BlockSpec((BLOCK, x_width), lambda i: (i, 0)),
            pl.BlockSpec((STATE, BLOCK), lambda i: (0, i)),
            pl.BlockSpec((BLOCK, STATE), lambda i: (i, 0)),
            per_block((BLOCK, heads)),
            per_block((heads, BLOCK)),
            per_block((heads, BLOCK)),
            per_block((BLOCK, heads)),
            per_block((heads, BLOCK)),
            per_block((heads, head_dim)),
            pl.BlockSpec((BLOCK, 1), lambda i: (i, 0)),
            per_block((1, BLOCK)),
            pl.BlockSpec(memory_space=pltpu.SMEM),
        ],
        out_specs=[
            pl.BlockSpec((BLOCK, x_width), lambda i: (i, 0)),
            pl.BlockSpec((BLOCK, 1), lambda i: (i, 0)),
        ],
        out_shape=[
            jax.ShapeDtypeStruct((total, x_width), jnp.float32),
            jax.ShapeDtypeStruct((total, 1), jnp.float32),
        ],
        scratch_shapes=[pltpu.VMEM((heads, STATE, head_dim), jnp.float32)],
        compiler_params=pltpu.CompilerParams(dimension_semantics=("arbitrary",)),
        interpret=interpret,
    )(
        x_h, b_t, c_g, log_cum, lc_rows, st_rows, carry_scale, end_rows, gain_rows,
        all_ids.reshape(total, 1), ids.reshape(nblk, 1, BLOCK), skip_h,
    )


def attend_rows(q_row, kv_win, ids_q, ids_k, first, count, interpret=False):
    tok_rows, q_width = q_row.shape
    window = kv_win.shape[0]
    kv_heads = kv_win.shape[1] // (2 * HEAD_A)
    group = q_width // HEAD_A // kv_heads
    lead = window - tok_rows
    inv_sqrt = 1.0 / math.sqrt(HEAD_A)

    def kernel(q_ref, k_ref, v_ref, iq_ref, ik_ref, o_ref):
        q_at = lead + lax.broadcasted_iota(jnp.int32, (tok_rows, window), 0)
        k_at = lax.broadcasted_iota(jnp.int32, (tok_rows, window), 1)
        allowed = (iq_ref[...] == ik_ref[...]) & (q_at >= k_at)
        kb = k_ref[...]
        vb = v_ref[...]
        for g in range(group):
            cols = slice(g * HEAD_A, (g + 1) * HEAD_A)
            logits = lax.dot_general(
                q_ref[:, cols], kb, (((1,), (1,)), ((), ())), preferred_element_type=jnp.float32
            ) * inv_sqrt
            logits = jnp.where(allowed, logits, -jnp.inf)
            row_max = jnp.max(logits, axis=1, keepdims=True)
            exp_terms = jnp.exp(logits - row_max)
            probs = (exp_terms / jnp.sum(exp_terms, axis=1, keepdims=True)).astype(jnp.bfloat16)
            o_ref[:, cols] = jnp.dot(probs, vb, preferred_element_type=jnp.float32).astype(o_ref.dtype)

    return pl.pallas_call(
        kernel,
        grid=(count,),
        in_specs=[
            pl.BlockSpec((tok_rows, group * HEAD_A), lambda i: (0, first + i)),
            pl.BlockSpec((window, HEAD_A), lambda i: (0, first + i)),
            pl.BlockSpec((window, HEAD_A), lambda i: (0, kv_heads + first + i)),
            pl.BlockSpec((tok_rows, 1), lambda i: (0, 0)),
            pl.BlockSpec((1, window), lambda i: (0, 0)),
        ],
        out_specs=pl.BlockSpec((tok_rows, group * HEAD_A), lambda i: (0, i)),
        out_shape=jax.ShapeDtypeStruct((tok_rows, count * group * HEAD_A), jnp.bfloat16),
        interpret=interpret,
    )(q_row, kv_win, kv_win, ids_q, ids_k)


def body(
    previous,
    fresh,
    dt_raw,
    dt_bias,
    a_log,
    b_in,
    c_in,
    skip_d,
    norm_gain,
    queries,
    keys,
    values,
    doc_ids,
):
    tok_rows, width = fresh.shape
    nctx = lax.axis_size("ctx")
    me = lax.axis_index("ctx")
    total = tok_rows * nctx
    part = width // nctx
    mamba_heads = dt_raw.shape[2]
    heads_dev = mamba_heads // nctx
    head_dim = width // mamba_heads
    kv_heads = keys.shape[2] // HEAD_A
    qpd = part // HEAD_A

    rep = nctx // kv_heads
    bc = jnp.stack(
        [b_in[0].reshape(tok_rows, GROUPS, STATE), c_in[0].reshape(tok_rows, GROUPS, STATE)], axis=2
    )
    bc_h = to_heads(jnp.repeat(bc, rep, axis=1).reshape(tok_rows, nctx * 2 * STATE), nctx)
    b_g, c_g = bc_h[:, :STATE], bc_h[:, STATE:]
    dt_h = to_heads(dt_raw[0], nctx)

    handed = shifted(previous[0], "section", 1)
    stream = jnp.where(lax.axis_index("section") == 0, fresh, handed)
    x_h = to_heads(stream, nctx)

    halo = -(-MOST_DOC // tok_rows)
    kv_row = jnp.concatenate([keys[0], values[0]], axis=1)
    kv_win = jnp.concatenate([shifted(kv_row, "ctx", by) for by in range(halo, 0, -1)] + [kv_row], axis=0)
    all_ids = doc_ids[0]
    lead = halo * tok_rows
    padded_ids = jnp.concatenate([jnp.full((lead,), -1, all_ids.dtype), all_ids])
    ids_k = lax.dynamic_slice_in_dim(padded_ids, me * tok_rows, lead + tok_rows)
    ids_q = lax.dynamic_slice_in_dim(all_ids, me * tok_rows, tok_rows)

    bias_h = lax.dynamic_slice_in_dim(dt_bias[0], me * heads_dev, heads_dev)
    alog_h = lax.dynamic_slice_in_dim(a_log[0], me * heads_dev, heads_dev)
    skip_h = lax.dynamic_slice_in_dim(skip_d[0], me * heads_dev, heads_dev)
    gain_h = lax.dynamic_slice_in_dim(norm_gain[0], me * part, part)

    mixer_out, sq_part = mixer_heads(x_h, dt_h, bias_h, alog_h, b_g, c_g, skip_h, all_ids)
    half = kv_heads // 2
    ids_q2, ids_k2 = ids_q.reshape(tok_rows, 1), ids_k.reshape(1, lead + tok_rows)
    att_a = attend_rows(queries[0], kv_win, ids_q2, ids_k2, 0, half)
    att_a, x_h = lax.optimization_barrier((att_a, x_h))
    sq_all = lax.all_to_all(
        jnp.broadcast_to(sq_part[:, 0][None], (nctx, total)), "ctx", split_axis=0, concat_axis=0, tiled=True
    )
    mean_sq = (jnp.sum(sq_all, axis=0) / width)[:, None]
    inv_rms = lax.rsqrt(mean_sq + norm_eps)
    mixed = (
        x_h.astype(jnp.float32) + mixer_out * inv_rms * gain_h.astype(jnp.float32)[None, :]
    ).astype(jnp.bfloat16)
    mixed_rows = to_rows(mixed, nctx)
    att_b = attend_rows(queries[0], kv_win, ids_q2, ids_k2, half, kv_heads - half)
    attended = jnp.concatenate([att_a, att_b], axis=1)
    return (mixed_rows.astype(jnp.float32) + attended.astype(jnp.float32)).astype(jnp.bfloat16)[None]


def solution(mesh):
    in_specs = (
        P("section", "ctx", None),
        P("ctx", None),
        P("section", "ctx", None),
        P("section", None),
        P("section", None),
        P("section", "ctx", None),
        P("section", "ctx", None),
        P("section", None),
        P("section", None),
        P("section", "ctx", None),
        P("section", "ctx", None),
        P("section", "ctx", None),
        P("section", None),
    )
    out_specs = P("section", "ctx", None)
    return jax.shard_map(body, mesh=mesh, in_specs=in_specs, out_specs=out_specs, check_vma=False)
```

```python
import math

import jax
import jax.numpy as jnp
from jax import lax
from jax.experimental import pallas as pl
from jax.experimental.pallas import tpu as pltpu
from jax.sharding import PartitionSpec as P

HEAD_A = 128
STATE = 128
GROUPS = 8
BLOCK = 128
MOST_DOC = 512
Q_BLOCK = 256


norm_eps = 1e-05


def shifted(value, axis, by):
    peers = lax.axis_size(axis)
    pairs = [(i, i + by) for i in range(peers) if 0 <= i + by < peers]
    return lax.ppermute(value, axis, pairs)


def to_heads(row, chunks):
    tok_rows = row.shape[0]
    width = row.shape[1] // chunks
    lead = row.reshape(tok_rows, chunks, width).transpose(1, 0, 2)
    moved = lax.all_to_all(lead, "ctx", split_axis=0, concat_axis=0, tiled=True)
    return moved.reshape(tok_rows * chunks, width)


def to_rows(block, chunks):
    total, width = block.shape
    tok_rows = total // chunks
    moved = lax.all_to_all(block.reshape(chunks, tok_rows, width), "ctx", split_axis=0, concat_axis=0, tiled=True)
    return moved.transpose(1, 0, 2).reshape(tok_rows, chunks * width)


def mixer_heads(x_h, dt_h, bias_h, alog_h, b_g, c_g, skip_h, all_ids, interpret=False):
    total, x_width = x_h.shape
    heads = dt_h.shape[1]
    head_dim = x_width // heads
    nblk = total // BLOCK
    step = jax.nn.softplus(dt_h + bias_h[None, :])
    log_rate = -step * jnp.exp(alog_h)[None, :]
    log_cum = log_rate.reshape(nblk, BLOCK, heads)
    reach = 1
    while reach < BLOCK:
        log_cum = log_cum + jnp.pad(log_cum[:, :-reach], ((0, 0), (reach, 0), (0, 0)))
        reach *= 2
    st = step.reshape(nblk, BLOCK, heads)
    ids = all_ids.reshape(nblk, BLOCK)
    last_id = ids[:, -1]
    prev_last = jnp.concatenate([jnp.full((1,), -1, ids.dtype), last_id[:-1]])
    edge_valid = (ids == prev_last[:, None]).astype(jnp.float32)
    carry_scale = jnp.exp(log_cum) * edge_valid[:, :, None]
    end_scale = (
        jnp.exp(log_cum[:, -1:, :] - log_cum) * st * (ids == last_id[:, None]).astype(jnp.float32)[:, :, None]
    )
    edge_match = (ids[:, 0] == prev_last).astype(jnp.float32)
    block_gain = jnp.exp(log_cum[:, -1, :]) * (ids[:, 0] == last_id).astype(jnp.float32)[:, None]
    block_gain = block_gain * edge_match[:, None]
    gain_rows = jnp.broadcast_to(block_gain[:, :, None], (nblk, heads, head_dim))
    lc_rows = log_cum.transpose(0, 2, 1)
    end_rows = end_scale.transpose(0, 2, 1)
    b_t = b_g.T
    st_rows = st.transpose(0, 2, 1)

    def kernel(x_ref, b_ref, c_ref, lcc_ref, lcr_ref, str_ref, csc_ref, esc_ref, gain_ref,
               idc_ref, idr_ref, skip_ref, o_ref, sq_ref, carry_ref):
        @pl.when(pl.program_id(0) == 0)
        def _():
            carry_ref[...] = jnp.zeros(carry_ref.shape, carry_ref.dtype)

        b_t_blk = b_ref[...]
        c_blk = c_ref[...]
        inner_cb = jnp.dot(c_blk, b_t_blk, preferred_element_type=jnp.float32)
        rows_at = lax.broadcasted_iota(jnp.int32, (BLOCK, BLOCK), 0)
        cols_at = lax.broadcasted_iota(jnp.int32, (BLOCK, BLOCK), 1)
        same_doc = (idc_ref[...] == idr_ref[0]) & (rows_at >= cols_at)
        b_t_f32 = b_t_blk.astype(jnp.float32)
        sq = jnp.zeros((BLOCK, 1), jnp.float32)
        for h in range(heads):
            cols = slice(h * head_dim, (h + 1) * head_dim)
            lc_c = lcc_ref[0, :, h:h + 1]
            lc_r = lcr_ref[0, h:h + 1, :]
            decay = jnp.where(same_doc, jnp.exp(lc_c - lc_r), 0.0)
            intra_w = (decay * inner_cb * str_ref[0, h:h + 1, :]).astype(jnp.bfloat16)
            xh = x_ref[:, cols]
            local = jnp.dot(intra_w, xh, preferred_element_type=jnp.float32)
            state_bf = carry_ref[h].astype(jnp.bfloat16)
            carried = jnp.dot(c_blk, state_bf, preferred_element_type=jnp.float32)
            carried = carried * csc_ref[0, :, h:h + 1]
            out = local + carried + skip_ref[h] * xh.astype(jnp.float32)
            o_ref[:, cols] = out
            sq = sq + jnp.sum(out * out, axis=1, keepdims=True)
            end_w_t = (esc_ref[0, h:h + 1, :] * b_t_f32).astype(jnp.bfloat16)
            block_state = jnp.dot(end_w_t, xh, preferred_element_type=jnp.float32)
            carry_ref[h] = gain_ref[0, h:h + 1, :] * carry_ref[h] + block_state
        sq_ref[...] = sq

    per_block = lambda shape: pl.BlockSpec((1,) + shape, lambda i: (i, 0, 0))
    return pl.pallas_call(
        kernel,
        grid=(nblk,),
        in_specs=[
            pl.BlockSpec((BLOCK, x_width), lambda i: (i, 0)),
            pl.BlockSpec((STATE, BLOCK), lambda i: (0, i)),
            pl.BlockSpec((BLOCK, STATE), lambda i: (i, 0)),
            per_block((BLOCK, heads)),
            per_block((heads, BLOCK)),
            per_block((heads, BLOCK)),
            per_block((BLOCK, heads)),
            per_block((heads, BLOCK)),
            per_block((heads, head_dim)),
            pl.BlockSpec((BLOCK, 1), lambda i: (i, 0)),
            per_block((1, BLOCK)),
            pl.BlockSpec(memory_space=pltpu.SMEM),
        ],
        out_specs=[
            pl.BlockSpec((BLOCK, x_width), lambda i: (i, 0)),
            pl.BlockSpec((BLOCK, 1), lambda i: (i, 0)),
        ],
        out_shape=[
            jax.ShapeDtypeStruct((total, x_width), jnp.float32),
            jax.ShapeDtypeStruct((total, 1), jnp.float32),
        ],
        scratch_shapes=[pltpu.VMEM((heads, STATE, head_dim), jnp.float32)],
        compiler_params=pltpu.CompilerParams(dimension_semantics=("arbitrary",)),
        interpret=interpret,
    )(
        x_h, b_t, c_g, log_cum, lc_rows, st_rows, carry_scale, end_rows, gain_rows,
        all_ids.reshape(total, 1), ids.reshape(nblk, 1, BLOCK), skip_h,
    )


def attend_rows(q_row, kv_win, ids_q, ids_k, interpret=False):
    tok_rows, q_width = q_row.shape
    window = kv_win.shape[0]
    kv_heads = kv_win.shape[1] // (2 * HEAD_A)
    group = q_width // HEAD_A // kv_heads
    lead = window - tok_rows
    inv_sqrt = 1.0 / math.sqrt(HEAD_A)

    def kernel(q_ref, k_ref, v_ref, iq_ref, ik_ref, o_ref):
        q_at = lead + lax.broadcasted_iota(jnp.int32, (tok_rows, window), 0)
        k_at = lax.broadcasted_iota(jnp.int32, (tok_rows, window), 1)
        allowed = (iq_ref[...] == ik_ref[...]) & (q_at >= k_at)
        kb = k_ref[...]
        vb = v_ref[...]
        for g in range(group):
            cols = slice(g * HEAD_A, (g + 1) * HEAD_A)
            logits = lax.dot_general(
                q_ref[:, cols], kb, (((1,), (1,)), ((), ())), preferred_element_type=jnp.float32
            ) * inv_sqrt
            logits = jnp.where(allowed, logits, -jnp.inf)
            row_max = jnp.max(logits, axis=1, keepdims=True)
            exp_terms = jnp.exp(logits - row_max)
            probs = (exp_terms / jnp.sum(exp_terms, axis=1, keepdims=True)).astype(jnp.bfloat16)
            o_ref[:, cols] = jnp.dot(probs, vb, preferred_element_type=jnp.float32).astype(o_ref.dtype)

    return pl.pallas_call(
        kernel,
        grid=(kv_heads,),
        in_specs=[
            pl.BlockSpec((tok_rows, group * HEAD_A), lambda i: (0, i)),
            pl.BlockSpec((window, HEAD_A), lambda i: (0, i)),
            pl.BlockSpec((window, HEAD_A), lambda i: (0, kv_heads + i)),
            pl.BlockSpec((tok_rows, 1), lambda i: (0, 0)),
            pl.BlockSpec((1, window), lambda i: (0, 0)),
        ],
        out_specs=pl.BlockSpec((tok_rows, group * HEAD_A), lambda i: (0, i)),
        out_shape=jax.ShapeDtypeStruct((tok_rows, q_width), jnp.bfloat16),
        interpret=interpret,
    )(q_row, kv_win, kv_win, ids_q, ids_k)


def body(
    previous,
    fresh,
    dt_raw,
    dt_bias,
    a_log,
    b_in,
    c_in,
    skip_d,
    norm_gain,
    queries,
    keys,
    values,
    doc_ids,
):
    tok_rows, width = fresh.shape
    nctx = lax.axis_size("ctx")
    me = lax.axis_index("ctx")
    total = tok_rows * nctx
    part = width // nctx
    mamba_heads = dt_raw.shape[2]
    heads_dev = mamba_heads // nctx
    head_dim = width // mamba_heads
    kv_heads = keys.shape[2] // HEAD_A
    qpd = part // HEAD_A

    rep = nctx // kv_heads
    bc = jnp.stack(
        [b_in[0].reshape(tok_rows, GROUPS, STATE), c_in[0].reshape(tok_rows, GROUPS, STATE)], axis=2
    )
    bc_rows = jnp.repeat(bc, rep, axis=1).reshape(tok_rows, nctx, 2 * STATE).astype(jnp.float32)
    dt_rows = dt_raw[0].reshape(tok_rows, nctx, heads_dev)
    side = to_heads(jnp.concatenate([bc_rows, dt_rows], axis=2).reshape(tok_rows, -1), nctx)
    b_g = side[:, :STATE].astype(jnp.bfloat16)
    c_g = side[:, STATE:2 * STATE].astype(jnp.bfloat16)
    dt_h = side[:, 2 * STATE:]

    handed = shifted(previous[0], "section", 1)
    stream = jnp.where(lax.axis_index("section") == 0, fresh, handed)
    x_h = to_heads(stream, nctx)

    halo = -(-MOST_DOC // tok_rows)
    kv_row = jnp.concatenate([keys[0], values[0]], axis=1)
    kv_win = jnp.concatenate([shifted(kv_row, "ctx", by) for by in range(halo, 0, -1)] + [kv_row], axis=0)
    kv_win, x_h = lax.optimization_barrier((kv_win, x_h))
    all_ids = doc_ids[0]
    lead = halo * tok_rows
    padded_ids = jnp.concatenate([jnp.full((lead,), -1, all_ids.dtype), all_ids])
    ids_k = lax.dynamic_slice_in_dim(padded_ids, me * tok_rows, lead + tok_rows)
    ids_q = lax.dynamic_slice_in_dim(all_ids, me * tok_rows, tok_rows)

    bias_h = lax.dynamic_slice_in_dim(dt_bias[0], me * heads_dev, heads_dev)
    alog_h = lax.dynamic_slice_in_dim(a_log[0], me * heads_dev, heads_dev)
    skip_h = lax.dynamic_slice_in_dim(skip_d[0], me * heads_dev, heads_dev)
    gain_h = lax.dynamic_slice_in_dim(norm_gain[0], me * part, part)

    mixer_out, sq_part = mixer_heads(x_h, dt_h, bias_h, alog_h, b_g, c_g, skip_h, all_ids)
    attended = attend_rows(queries[0], kv_win, ids_q.reshape(tok_rows, 1), ids_k.reshape(1, lead + tok_rows))
    sq_all = lax.all_to_all(
        jnp.broadcast_to(sq_part[:, 0][None], (nctx, total)), "ctx", split_axis=0, concat_axis=0, tiled=True
    )
    mean_sq = (jnp.sum(sq_all, axis=0) / width)[:, None]
    inv_rms = lax.rsqrt(mean_sq + norm_eps)
    mixed = (
        x_h.astype(jnp.float32) + mixer_out * inv_rms * gain_h.astype(jnp.float32)[None, :]
    ).astype(jnp.bfloat16)
    mixed_rows = to_rows(mixed, nctx)
    return (mixed_rows.astype(jnp.float32) + attended.astype(jnp.float32)).astype(jnp.bfloat16)[None]


def solution(mesh):
    in_specs = (
        P("section", "ctx", None),
        P("ctx", None),
        P("section", "ctx", None),
        P("section", None),
        P("section", None),
        P("section", "ctx", None),
        P("section", "ctx", None),
        P("section", None),
        P("section", None),
        P("section", "ctx", None),
        P("section", "ctx", None),
        P("section", "ctx", None),
        P("section", None),
    )
    out_specs = P("section", "ctx", None)
    return jax.shard_map(body, mesh=mesh, in_specs=in_specs, out_specs=out_specs, check_vma=False)
```

```python
import math

import jax
import jax.numpy as jnp
from jax import lax
from jax.experimental import pallas as pl
from jax.experimental.pallas import tpu as pltpu
from jax.sharding import PartitionSpec as P

HEAD_A = 128
STATE = 128
GROUPS = 8
BLOCK = 128
MOST_DOC = 512
Q_BLOCK = 256


norm_eps = 1e-05


def shifted(value, axis, by):
    peers = lax.axis_size(axis)
    pairs = [(i, i + by) for i in range(peers) if 0 <= i + by < peers]
    return lax.ppermute(value, axis, pairs)


def to_heads(row, chunks):
    tok_rows = row.shape[0]
    width = row.shape[1] // chunks
    lead = row.reshape(tok_rows, chunks, width).transpose(1, 0, 2)
    moved = lax.all_to_all(lead, "ctx", split_axis=0, concat_axis=0, tiled=True)
    return moved.reshape(tok_rows * chunks, width)


def to_rows(block, chunks):
    total, width = block.shape
    tok_rows = total // chunks
    moved = lax.all_to_all(block.reshape(chunks, tok_rows, width), "ctx", split_axis=0, concat_axis=0, tiled=True)
    return moved.transpose(1, 0, 2).reshape(tok_rows, chunks * width)


def mixer_heads(x_h, dt_h, bias_h, alog_h, b_g, c_g, skip_h, all_ids, interpret=False):
    total, x_width = x_h.shape
    heads = dt_h.shape[1]
    head_dim = x_width // heads
    nblk = total // BLOCK
    step = jax.nn.softplus(dt_h + bias_h[None, :])
    log_rate = -step * jnp.exp(alog_h)[None, :]
    log_cum = log_rate.reshape(nblk, BLOCK, heads)
    reach = 1
    while reach < BLOCK:
        log_cum = log_cum + jnp.pad(log_cum[:, :-reach], ((0, 0), (reach, 0), (0, 0)))
        reach *= 2
    st = step.reshape(nblk, BLOCK, heads)
    ids = all_ids.reshape(nblk, BLOCK)
    last_id = ids[:, -1]
    prev_last = jnp.concatenate([jnp.full((1,), -1, ids.dtype), last_id[:-1]])
    edge_valid = (ids == prev_last[:, None]).astype(jnp.float32)
    carry_scale = jnp.exp(log_cum) * edge_valid[:, :, None]
    end_scale = (
        jnp.exp(log_cum[:, -1:, :] - log_cum) * st * (ids == last_id[:, None]).astype(jnp.float32)[:, :, None]
    )
    edge_match = (ids[:, 0] == prev_last).astype(jnp.float32)
    block_gain = jnp.exp(log_cum[:, -1, :]) * (ids[:, 0] == last_id).astype(jnp.float32)[:, None]
    block_gain = block_gain * edge_match[:, None]
    gain_rows = jnp.broadcast_to(block_gain[:, :, None], (nblk, heads, head_dim))
    lc_rows = log_cum.transpose(0, 2, 1)
    end_rows = end_scale.transpose(0, 2, 1)
    b_t = b_g.T
    st_rows = st.transpose(0, 2, 1)

    def kernel(x_ref, b_ref, c_ref, lcc_ref, lcr_ref, str_ref, csc_ref, esc_ref, gain_ref,
               idc_ref, idr_ref, skip_ref, o_ref, sq_ref, carry_ref):
        @pl.when(pl.program_id(0) == 0)
        def _():
            carry_ref[...] = jnp.zeros(carry_ref.shape, carry_ref.dtype)

        b_t_blk = b_ref[...]
        c_blk = c_ref[...]
        inner_cb = jnp.dot(c_blk, b_t_blk, preferred_element_type=jnp.float32)
        rows_at = lax.broadcasted_iota(jnp.int32, (BLOCK, BLOCK), 0)
        cols_at = lax.broadcasted_iota(jnp.int32, (BLOCK, BLOCK), 1)
        same_doc = (idc_ref[...] == idr_ref[0]) & (rows_at >= cols_at)
        b_t_f32 = b_t_blk.astype(jnp.float32)
        sq = jnp.zeros((BLOCK, 1), jnp.float32)
        for h in range(heads):
            cols = slice(h * head_dim, (h + 1) * head_dim)
            lc_c = lcc_ref[0, :, h:h + 1]
            lc_r = lcr_ref[0, h:h + 1, :]
            decay = jnp.where(same_doc, jnp.exp(lc_c - lc_r), 0.0)
            intra_w = (decay * inner_cb * str_ref[0, h:h + 1, :]).astype(jnp.bfloat16)
            xh = x_ref[:, cols]
            local = jnp.dot(intra_w, xh, preferred_element_type=jnp.float32)
            state_bf = carry_ref[h].astype(jnp.bfloat16)
            carried = jnp.dot(c_blk, state_bf, preferred_element_type=jnp.float32)
            carried = carried * csc_ref[0, :, h:h + 1]
            out = local + carried + skip_ref[h] * xh.astype(jnp.float32)
            o_ref[:, cols] = out
            sq = sq + jnp.sum(out * out, axis=1, keepdims=True)
            end_w_t = (esc_ref[0, h:h + 1, :] * b_t_f32).astype(jnp.bfloat16)
            block_state = jnp.dot(end_w_t, xh, preferred_element_type=jnp.float32)
            carry_ref[h] = gain_ref[0, h:h + 1, :] * carry_ref[h] + block_state
        sq_ref[...] = sq

    per_block = lambda shape: pl.BlockSpec((1,) + shape, lambda i: (i, 0, 0))
    return pl.pallas_call(
        kernel,
        grid=(nblk,),
        in_specs=[
            pl.BlockSpec((BLOCK, x_width), lambda i: (i, 0)),
            pl.BlockSpec((STATE, BLOCK), lambda i: (0, i)),
            pl.BlockSpec((BLOCK, STATE), lambda i: (i, 0)),
            per_block((BLOCK, heads)),
            per_block((heads, BLOCK)),
            per_block((heads, BLOCK)),
            per_block((BLOCK, heads)),
            per_block((heads, BLOCK)),
            per_block((heads, head_dim)),
            pl.BlockSpec((BLOCK, 1), lambda i: (i, 0)),
            per_block((1, BLOCK)),
            pl.BlockSpec(memory_space=pltpu.SMEM),
        ],
        out_specs=[
            pl.BlockSpec((BLOCK, x_width), lambda i: (i, 0)),
            pl.BlockSpec((BLOCK, 1), lambda i: (i, 0)),
        ],
        out_shape=[
            jax.ShapeDtypeStruct((total, x_width), jnp.float32),
            jax.ShapeDtypeStruct((total, 1), jnp.float32),
        ],
        scratch_shapes=[pltpu.VMEM((heads, STATE, head_dim), jnp.float32)],
        compiler_params=pltpu.CompilerParams(dimension_semantics=("arbitrary",)),
        interpret=interpret,
    )(
        x_h, b_t, c_g, log_cum, lc_rows, st_rows, carry_scale, end_rows, gain_rows,
        all_ids.reshape(total, 1), ids.reshape(nblk, 1, BLOCK), skip_h,
    )


def attend_rows(q_row, kv_win, ids_q, ids_k, interpret=False):
    tok_rows, q_width = q_row.shape
    window = kv_win.shape[0]
    kv_heads = kv_win.shape[1] // (2 * HEAD_A)
    group = q_width // HEAD_A // kv_heads
    lead = window - tok_rows
    pair = 2 if kv_heads % 2 == 0 else 1
    inv_sqrt = 1.0 / math.sqrt(HEAD_A)

    def kernel(q_ref, k_ref, v_ref, iq_ref, ik_ref, o_ref):
        q_at = lead + lax.broadcasted_iota(jnp.int32, (tok_rows, window), 0)
        k_at = lax.broadcasted_iota(jnp.int32, (tok_rows, window), 1)
        allowed = (iq_ref[...] == ik_ref[...]) & (q_at >= k_at)
        for g in range(pair * group):
            kv_cols = slice((g // group) * HEAD_A, (g // group + 1) * HEAD_A)
            kb = k_ref[:, kv_cols]
            vb = v_ref[:, kv_cols]
            cols = slice(g * HEAD_A, (g + 1) * HEAD_A)
            logits = lax.dot_general(
                q_ref[:, cols], kb, (((1,), (1,)), ((), ())), preferred_element_type=jnp.float32
            ) * inv_sqrt
            logits = jnp.where(allowed, logits, -jnp.inf)
            row_max = jnp.max(logits, axis=1, keepdims=True)
            exp_terms = jnp.exp(logits - row_max)
            probs = (exp_terms / jnp.sum(exp_terms, axis=1, keepdims=True)).astype(jnp.bfloat16)
            o_ref[:, cols] = jnp.dot(probs, vb, preferred_element_type=jnp.float32).astype(o_ref.dtype)

    return pl.pallas_call(
        kernel,
        grid=(kv_heads // pair,),
        in_specs=[
            pl.BlockSpec((tok_rows, pair * group * HEAD_A), lambda i: (0, i)),
            pl.BlockSpec((window, pair * HEAD_A), lambda i: (0, i)),
            pl.BlockSpec((window, pair * HEAD_A), lambda i: (0, kv_heads // pair + i)),
            pl.BlockSpec((tok_rows, 1), lambda i: (0, 0)),
            pl.BlockSpec((1, window), lambda i: (0, 0)),
        ],
        out_specs=pl.BlockSpec((tok_rows, pair * group * HEAD_A), lambda i: (0, i)),
        out_shape=jax.ShapeDtypeStruct((tok_rows, q_width), jnp.bfloat16),
        interpret=interpret,
    )(q_row, kv_win, kv_win, ids_q, ids_k)


def body(
    previous,
    fresh,
    dt_raw,
    dt_bias,
    a_log,
    b_in,
    c_in,
    skip_d,
    norm_gain,
    queries,
    keys,
    values,
    doc_ids,
):
    tok_rows, width = fresh.shape
    nctx = lax.axis_size("ctx")
    me = lax.axis_index("ctx")
    total = tok_rows * nctx
    part = width // nctx
    mamba_heads = dt_raw.shape[2]
    heads_dev = mamba_heads // nctx
    head_dim = width // mamba_heads
    kv_heads = keys.shape[2] // HEAD_A
    qpd = part // HEAD_A

    rep = nctx // kv_heads
    bc = jnp.stack(
        [b_in[0].reshape(tok_rows, GROUPS, STATE), c_in[0].reshape(tok_rows, GROUPS, STATE)], axis=2
    )
    bc_h = to_heads(jnp.repeat(bc, rep, axis=1).reshape(tok_rows, nctx * 2 * STATE), nctx)
    b_g, c_g = bc_h[:, :STATE], bc_h[:, STATE:]
    dt_h = to_heads(dt_raw[0], nctx)

    handed = shifted(previous[0], "section", 1)
    stream = jnp.where(lax.axis_index("section") == 0, fresh, handed)
    x_h = to_heads(stream, nctx)

    halo = -(-MOST_DOC // tok_rows)
    kv_row = jnp.concatenate([keys[0], values[0]], axis=1)
    kv_win = jnp.concatenate([shifted(kv_row, "ctx", by) for by in range(halo, 0, -1)] + [kv_row], axis=0)
    kv_win, x_h = lax.optimization_barrier((kv_win, x_h))
    all_ids = doc_ids[0]
    lead = halo * tok_rows
    padded_ids = jnp.concatenate([jnp.full((lead,), -1, all_ids.dtype), all_ids])
    ids_k = lax.dynamic_slice_in_dim(padded_ids, me * tok_rows, lead + tok_rows)
    ids_q = lax.dynamic_slice_in_dim(all_ids, me * tok_rows, tok_rows)

    bias_h = lax.dynamic_slice_in_dim(dt_bias[0], me * heads_dev, heads_dev)
    alog_h = lax.dynamic_slice_in_dim(a_log[0], me * heads_dev, heads_dev)
    skip_h = lax.dynamic_slice_in_dim(skip_d[0], me * heads_dev, heads_dev)
    gain_h = lax.dynamic_slice_in_dim(norm_gain[0], me * part, part)

    mixer_out, sq_part = mixer_heads(x_h, dt_h, bias_h, alog_h, b_g, c_g, skip_h, all_ids)
    attended = attend_rows(queries[0], kv_win, ids_q.reshape(tok_rows, 1), ids_k.reshape(1, lead + tok_rows))
    sq_all = lax.all_to_all(
        jnp.broadcast_to(sq_part[:, 0][None], (nctx, total)), "ctx", split_axis=0, concat_axis=0, tiled=True
    )
    mean_sq = (jnp.sum(sq_all, axis=0) / width)[:, None]
    inv_rms = lax.rsqrt(mean_sq + norm_eps)
    mixed = (
        x_h.astype(jnp.float32) + mixer_out * inv_rms * gain_h.astype(jnp.float32)[None, :]
    ).astype(jnp.bfloat16)
    mixed_rows = to_rows(mixed, nctx)
    return (mixed_rows.astype(jnp.float32) + attended.astype(jnp.float32)).astype(jnp.bfloat16)[None]


def solution(mesh):
    in_specs = (
        P("section", "ctx", None),
        P("ctx", None),
        P("section", "ctx", None),
        P("section", None),
        P("section", None),
        P("section", "ctx", None),
        P("section", "ctx", None),
        P("section", None),
        P("section", None),
        P("section", "ctx", None),
        P("section", "ctx", None),
        P("section", "ctx", None),
        P("section", None),
    )
    out_specs = P("section", "ctx", None)
    return jax.shard_map(body, mesh=mesh, in_specs=in_specs, out_specs=out_specs, check_vma=False)
```

```python
import math

import jax
import jax.numpy as jnp
from jax import lax
from jax.experimental import pallas as pl
from jax.experimental.pallas import tpu as pltpu
from jax.sharding import PartitionSpec as P

HEAD_A = 128
STATE = 128
GROUPS = 8
BLOCK = 128
MOST_DOC = 512
Q_BLOCK = 256


norm_eps = 1e-05


def shifted(value, axis, by):
    peers = lax.axis_size(axis)
    pairs = [(i, i + by) for i in range(peers) if 0 <= i + by < peers]
    return lax.ppermute(value, axis, pairs)


def to_heads(row, chunks):
    tok_rows = row.shape[0]
    width = row.shape[1] // chunks
    lead = row.reshape(tok_rows, chunks, width).transpose(1, 0, 2)
    moved = lax.all_to_all(lead, "ctx", split_axis=0, concat_axis=0, tiled=True)
    return moved.reshape(tok_rows * chunks, width)


def to_rows(block, chunks):
    total, width = block.shape
    tok_rows = total // chunks
    moved = lax.all_to_all(block.reshape(chunks, tok_rows, width), "ctx", split_axis=0, concat_axis=0, tiled=True)
    return moved.transpose(1, 0, 2).reshape(tok_rows, chunks * width)


def mixer_heads(x_h, dt_h, bias_h, alog_h, b_g, c_g, skip_h, all_ids, interpret=False):
    total, x_width = x_h.shape
    heads = dt_h.shape[1]
    head_dim = x_width // heads
    nblk = total // BLOCK
    step = jax.nn.softplus(dt_h + bias_h[None, :])
    log_rate = -step * jnp.exp(alog_h)[None, :]
    log_cum = log_rate.reshape(nblk, BLOCK, heads)
    reach = 1
    while reach < BLOCK:
        log_cum = log_cum + jnp.pad(log_cum[:, :-reach], ((0, 0), (reach, 0), (0, 0)))
        reach *= 2
    st = step.reshape(nblk, BLOCK, heads)
    ids = all_ids.reshape(nblk, BLOCK)
    last_id = ids[:, -1]
    prev_last = jnp.concatenate([jnp.full((1,), -1, ids.dtype), last_id[:-1]])
    edge_valid = (ids == prev_last[:, None]).astype(jnp.float32)
    carry_scale = jnp.exp(log_cum) * edge_valid[:, :, None]
    end_scale = (
        jnp.exp(log_cum[:, -1:, :] - log_cum) * st * (ids == last_id[:, None]).astype(jnp.float32)[:, :, None]
    )
    edge_match = (ids[:, 0] == prev_last).astype(jnp.float32)
    block_gain = jnp.exp(log_cum[:, -1, :]) * (ids[:, 0] == last_id).astype(jnp.float32)[:, None]
    block_gain = block_gain * edge_match[:, None]
    gain_rows = jnp.broadcast_to(block_gain[:, :, None], (nblk, heads, head_dim))
    lc_rows = log_cum.transpose(0, 2, 1)
    end_rows = end_scale.transpose(0, 2, 1)
    b_t = b_g.T
    st_rows = st.transpose(0, 2, 1)

    def kernel(x_ref, b_ref, c_ref, lcc_ref, lcr_ref, str_ref, csc_ref, esc_ref, gain_ref,
               idc_ref, idr_ref, skip_ref, o_ref, sq_ref, carry_ref):
        @pl.when(pl.program_id(0) == 0)
        def _():
            carry_ref[...] = jnp.zeros(carry_ref.shape, carry_ref.dtype)

        b_t_blk = b_ref[...]
        c_blk = c_ref[...]
        inner_cb = jnp.dot(c_blk, b_t_blk, preferred_element_type=jnp.float32)
        rows_at = lax.broadcasted_iota(jnp.int32, (BLOCK, BLOCK), 0)
        cols_at = lax.broadcasted_iota(jnp.int32, (BLOCK, BLOCK), 1)
        same_doc = (idc_ref[...] == idr_ref[0]) & (rows_at >= cols_at)
        b_t_f32 = b_t_blk.astype(jnp.float32)
        sq = jnp.zeros((BLOCK, head_dim), jnp.float32)
        for h in range(heads):
            cols = slice(h * head_dim, (h + 1) * head_dim)
            lc_c = lcc_ref[0, :, h:h + 1]
            lc_r = lcr_ref[0, h:h + 1, :]
            decay = jnp.where(same_doc, jnp.exp(lc_c - lc_r), 0.0)
            intra_w = (decay * inner_cb * str_ref[0, h:h + 1, :]).astype(jnp.bfloat16)
            xh = x_ref[:, cols]
            local = jnp.dot(intra_w, xh, preferred_element_type=jnp.float32)
            state_bf = carry_ref[h].astype(jnp.bfloat16)
            carried = jnp.dot(c_blk, state_bf, preferred_element_type=jnp.float32)
            carried = carried * csc_ref[0, :, h:h + 1]
            out = local + carried + skip_ref[h] * xh.astype(jnp.float32)
            o_ref[:, cols] = out
            sq = sq + out * out
            end_w_t = (esc_ref[0, h:h + 1, :] * b_t_f32).astype(jnp.bfloat16)
            block_state = jnp.dot(end_w_t, xh, preferred_element_type=jnp.float32)
            carry_ref[h] = gain_ref[0, h:h + 1, :] * carry_ref[h] + block_state
        sq_ref[...] = jnp.sum(sq, axis=1, keepdims=True)

    per_block = lambda shape: pl.BlockSpec((1,) + shape, lambda i: (i, 0, 0))
    return pl.pallas_call(
        kernel,
        grid=(nblk,),
        in_specs=[
            pl.BlockSpec((BLOCK, x_width), lambda i: (i, 0)),
            pl.BlockSpec((STATE, BLOCK), lambda i: (0, i)),
            pl.BlockSpec((BLOCK, STATE), lambda i: (i, 0)),
            per_block((BLOCK, heads)),
            per_block((heads, BLOCK)),
            per_block((heads, BLOCK)),
            per_block((BLOCK, heads)),
            per_block((heads, BLOCK)),
            per_block((heads, head_dim)),
            pl.BlockSpec((BLOCK, 1), lambda i: (i, 0)),
            per_block((1, BLOCK)),
            pl.BlockSpec(memory_space=pltpu.SMEM),
        ],
        out_specs=[
            pl.BlockSpec((BLOCK, x_width), lambda i: (i, 0)),
            pl.BlockSpec((BLOCK, 1), lambda i: (i, 0)),
        ],
        out_shape=[
            jax.ShapeDtypeStruct((total, x_width), jnp.float32),
            jax.ShapeDtypeStruct((total, 1), jnp.float32),
        ],
        scratch_shapes=[pltpu.VMEM((heads, STATE, head_dim), jnp.float32)],
        compiler_params=pltpu.CompilerParams(dimension_semantics=("arbitrary",)),
        interpret=interpret,
    )(
        x_h, b_t, c_g, log_cum, lc_rows, st_rows, carry_scale, end_rows, gain_rows,
        all_ids.reshape(total, 1), ids.reshape(nblk, 1, BLOCK), skip_h,
    )


def attend_rows(q_row, kv_win, ids_q, ids_k, interpret=False):
    tok_rows, q_width = q_row.shape
    window = kv_win.shape[0]
    kv_heads = kv_win.shape[1] // (2 * HEAD_A)
    group = q_width // HEAD_A // kv_heads
    lead = window - tok_rows
    pair = 2 if kv_heads % 2 == 0 else 1
    inv_sqrt = 1.0 / math.sqrt(HEAD_A)

    def kernel(q_ref, k_ref, v_ref, iq_ref, ik_ref, o_ref):
        q_at = lead + lax.broadcasted_iota(jnp.int32, (tok_rows, window), 0)
        k_at = lax.broadcasted_iota(jnp.int32, (tok_rows, window), 1)
        allowed = (iq_ref[...] == ik_ref[...]) & (q_at >= k_at)
        for g in range(pair * group):
            kv_cols = slice((g // group) * HEAD_A, (g // group + 1) * HEAD_A)
            kb = k_ref[:, kv_cols]
            vb = v_ref[:, kv_cols]
            cols = slice(g * HEAD_A, (g + 1) * HEAD_A)
            logits = lax.dot_general(
                q_ref[:, cols], kb, (((1,), (1,)), ((), ())), preferred_element_type=jnp.float32
            ) * inv_sqrt
            logits = jnp.where(allowed, logits, -jnp.inf)
            row_max = jnp.max(logits, axis=1, keepdims=True)
            exp_terms = jnp.exp(logits - row_max)
            probs = (exp_terms / jnp.sum(exp_terms, axis=1, keepdims=True)).astype(jnp.bfloat16)
            o_ref[:, cols] = jnp.dot(probs, vb, preferred_element_type=jnp.float32).astype(o_ref.dtype)

    return pl.pallas_call(
        kernel,
        grid=(kv_heads // pair,),
        in_specs=[
            pl.BlockSpec((tok_rows, pair * group * HEAD_A), lambda i: (0, i)),
            pl.BlockSpec((window, pair * HEAD_A), lambda i: (0, i)),
            pl.BlockSpec((window, pair * HEAD_A), lambda i: (0, kv_heads // pair + i)),
            pl.BlockSpec((tok_rows, 1), lambda i: (0, 0)),
            pl.BlockSpec((1, window), lambda i: (0, 0)),
        ],
        out_specs=pl.BlockSpec((tok_rows, pair * group * HEAD_A), lambda i: (0, i)),
        out_shape=jax.ShapeDtypeStruct((tok_rows, q_width), jnp.bfloat16),
        interpret=interpret,
    )(q_row, kv_win, kv_win, ids_q, ids_k)


def body(
    previous,
    fresh,
    dt_raw,
    dt_bias,
    a_log,
    b_in,
    c_in,
    skip_d,
    norm_gain,
    queries,
    keys,
    values,
    doc_ids,
):
    tok_rows, width = fresh.shape
    nctx = lax.axis_size("ctx")
    me = lax.axis_index("ctx")
    total = tok_rows * nctx
    part = width // nctx
    mamba_heads = dt_raw.shape[2]
    heads_dev = mamba_heads // nctx
    head_dim = width // mamba_heads
    kv_heads = keys.shape[2] // HEAD_A
    qpd = part // HEAD_A

    rep = nctx // kv_heads
    bc = jnp.stack(
        [b_in[0].reshape(tok_rows, GROUPS, STATE), c_in[0].reshape(tok_rows, GROUPS, STATE)], axis=2
    )
    bc_h = to_heads(jnp.repeat(bc, rep, axis=1).reshape(tok_rows, nctx * 2 * STATE), nctx)
    b_g, c_g = bc_h[:, :STATE], bc_h[:, STATE:]
    dt_h = to_heads(dt_raw[0], nctx)

    handed = shifted(previous[0], "section", 1)
    stream = jnp.where(lax.axis_index("section") == 0, fresh, handed)
    x_h = to_heads(stream, nctx)

    halo = -(-MOST_DOC // tok_rows)
    kv_row = jnp.concatenate([keys[0], values[0]], axis=1)
    kv_win = jnp.concatenate([shifted(kv_row, "ctx", by) for by in range(halo, 0, -1)] + [kv_row], axis=0)
    kv_win, x_h = lax.optimization_barrier((kv_win, x_h))
    all_ids = doc_ids[0]
    lead = halo * tok_rows
    padded_ids = jnp.concatenate([jnp.full((lead,), -1, all_ids.dtype), all_ids])
    ids_k = lax.dynamic_slice_in_dim(padded_ids, me * tok_rows, lead + tok_rows)
    ids_q = lax.dynamic_slice_in_dim(all_ids, me * tok_rows, tok_rows)

    bias_h = lax.dynamic_slice_in_dim(dt_bias[0], me * heads_dev, heads_dev)
    alog_h = lax.dynamic_slice_in_dim(a_log[0], me * heads_dev, heads_dev)
    skip_h = lax.dynamic_slice_in_dim(skip_d[0], me * heads_dev, heads_dev)
    gain_h = lax.dynamic_slice_in_dim(norm_gain[0], me * part, part)

    mixer_out, sq_part = mixer_heads(x_h, dt_h, bias_h, alog_h, b_g, c_g, skip_h, all_ids)
    attended = attend_rows(queries[0], kv_win, ids_q.reshape(tok_rows, 1), ids_k.reshape(1, lead + tok_rows))
    sq_all = lax.all_to_all(
        jnp.broadcast_to(sq_part[:, 0][None], (nctx, total)), "ctx", split_axis=0, concat_axis=0, tiled=True
    )
    mean_sq = (jnp.sum(sq_all, axis=0) / width)[:, None]
    inv_rms = lax.rsqrt(mean_sq + norm_eps)
    mixed = (
        x_h.astype(jnp.float32) + mixer_out * inv_rms * gain_h.astype(jnp.float32)[None, :]
    ).astype(jnp.bfloat16)
    mixed_rows = to_rows(mixed, nctx)
    return (mixed_rows.astype(jnp.float32) + attended.astype(jnp.float32)).astype(jnp.bfloat16)[None]


def solution(mesh):
    in_specs = (
        P("section", "ctx", None),
        P("ctx", None),
        P("section", "ctx", None),
        P("section", None),
        P("section", None),
        P("section", "ctx", None),
        P("section", "ctx", None),
        P("section", None),
        P("section", None),
        P("section", "ctx", None),
        P("section", "ctx", None),
        P("section", "ctx", None),
        P("section", None),
    )
    out_specs = P("section", "ctx", None)
    return jax.shard_map(body, mesh=mesh, in_specs=in_specs, out_specs=out_specs, check_vma=False)
```

```python
import math

import jax
import jax.numpy as jnp
from jax import lax
from jax.experimental import pallas as pl
from jax.experimental.pallas import tpu as pltpu
from jax.sharding import PartitionSpec as P

HEAD_A = 128
STATE = 128
GROUPS = 8
BLOCK = 128
MOST_DOC = 512
Q_BLOCK = 256


norm_eps = 1e-05


def shifted(value, axis, by):
    peers = lax.axis_size(axis)
    pairs = [(i, i + by) for i in range(peers) if 0 <= i + by < peers]
    return lax.ppermute(value, axis, pairs)


def to_heads(row, chunks):
    tok_rows = row.shape[0]
    width = row.shape[1] // chunks
    lead = row.reshape(tok_rows, chunks, width).transpose(1, 0, 2)
    moved = lax.all_to_all(lead, "ctx", split_axis=0, concat_axis=0, tiled=True)
    return moved.reshape(tok_rows * chunks, width)


def to_rows(block, chunks):
    total, width = block.shape
    tok_rows = total // chunks
    moved = lax.all_to_all(block.reshape(chunks, tok_rows, width), "ctx", split_axis=0, concat_axis=0, tiled=True)
    return moved.transpose(1, 0, 2).reshape(tok_rows, chunks * width)


def mixer_heads(x_h, dt_h, bias_h, alog_h, b_g, c_g, skip_h, all_ids, interpret=False):
    total, x_width = x_h.shape
    heads = dt_h.shape[1]
    head_dim = x_width // heads
    nblk = total // BLOCK
    step = jax.nn.softplus(dt_h + bias_h[None, :])
    log_rate = -step * jnp.exp(alog_h)[None, :]
    log_cum = log_rate.reshape(nblk, BLOCK, heads)
    reach = 1
    while reach < BLOCK:
        log_cum = log_cum + jnp.pad(log_cum[:, :-reach], ((0, 0), (reach, 0), (0, 0)))
        reach *= 2
    st = step.reshape(nblk, BLOCK, heads)
    ids = all_ids.reshape(nblk, BLOCK)
    last_id = ids[:, -1]
    prev_last = jnp.concatenate([jnp.full((1,), -1, ids.dtype), last_id[:-1]])
    edge_valid = (ids == prev_last[:, None]).astype(jnp.float32)
    carry_scale = jnp.exp(log_cum) * edge_valid[:, :, None]
    end_scale = (
        jnp.exp(log_cum[:, -1:, :] - log_cum) * st * (ids == last_id[:, None]).astype(jnp.float32)[:, :, None]
    )
    edge_match = (ids[:, 0] == prev_last).astype(jnp.float32)
    block_gain = jnp.exp(log_cum[:, -1, :]) * (ids[:, 0] == last_id).astype(jnp.float32)[:, None]
    block_gain = block_gain * edge_match[:, None]
    gain_rows = jnp.broadcast_to(block_gain[:, :, None], (nblk, heads, head_dim))
    lc_rows = log_cum.transpose(0, 2, 1)
    end_rows = end_scale.transpose(0, 2, 1)
    b_t = b_g.T
    st_rows = st.transpose(0, 2, 1)

    def kernel(x_ref, b_ref, c_ref, lcc_ref, lcr_ref, str_ref, csc_ref, esc_ref, gain_ref,
               idc_ref, idr_ref, skip_ref, o_ref, sq_ref, carry_ref):
        @pl.when(pl.program_id(0) == 0)
        def _():
            carry_ref[...] = jnp.zeros(carry_ref.shape, carry_ref.dtype)

        b_t_blk = b_ref[...]
        c_blk = c_ref[...]
        inner_cb = jnp.dot(c_blk, b_t_blk, preferred_element_type=jnp.float32)
        rows_at = lax.broadcasted_iota(jnp.int32, (BLOCK, BLOCK), 0)
        cols_at = lax.broadcasted_iota(jnp.int32, (BLOCK, BLOCK), 1)
        same_doc = (idc_ref[...] == idr_ref[0]) & (rows_at >= cols_at)
        b_t_f32 = b_t_blk.astype(jnp.float32)
        sq = jnp.zeros((BLOCK, head_dim), jnp.float32)
        for h in range(heads):
            cols = slice(h * head_dim, (h + 1) * head_dim)
            lc_c = lcc_ref[0, :, h:h + 1]
            lc_r = lcr_ref[0, h:h + 1, :]
            decay = jnp.where(same_doc, jnp.exp(lc_c - lc_r), 0.0)
            intra_w = (decay * inner_cb * str_ref[0, h:h + 1, :]).astype(jnp.bfloat16)
            xh = x_ref[:, cols]
            local = jnp.dot(intra_w, xh, preferred_element_type=jnp.float32)
            state_bf = carry_ref[h].astype(jnp.bfloat16)
            carried = jnp.dot(c_blk, state_bf, preferred_element_type=jnp.float32)
            carried = carried * csc_ref[0, :, h:h + 1]
            out = local + carried + skip_ref[h] * xh.astype(jnp.float32)
            o_ref[:, cols] = out
            sq = sq + out * out
            end_w_t = (esc_ref[0, h:h + 1, :] * b_t_f32).astype(jnp.bfloat16)
            block_state = jnp.dot(end_w_t, xh, preferred_element_type=jnp.float32)
            carry_ref[h] = gain_ref[0, h:h + 1, :] * carry_ref[h] + block_state
        sq_ref[...] = jnp.sum(sq, axis=1, keepdims=True)

    per_block = lambda shape: pl.BlockSpec((1,) + shape, lambda i: (i, 0, 0))
    return pl.pallas_call(
        kernel,
        grid=(nblk,),
        in_specs=[
            pl.BlockSpec((BLOCK, x_width), lambda i: (i, 0)),
            pl.BlockSpec((STATE, BLOCK), lambda i: (0, i)),
            pl.BlockSpec((BLOCK, STATE), lambda i: (i, 0)),
            per_block((BLOCK, heads)),
            per_block((heads, BLOCK)),
            per_block((heads, BLOCK)),
            per_block((BLOCK, heads)),
            per_block((heads, BLOCK)),
            per_block((heads, head_dim)),
            pl.BlockSpec((BLOCK, 1), lambda i: (i, 0)),
            per_block((1, BLOCK)),
            pl.BlockSpec(memory_space=pltpu.SMEM),
        ],
        out_specs=[
            pl.BlockSpec((BLOCK, x_width), lambda i: (i, 0)),
            pl.BlockSpec((BLOCK, 1), lambda i: (i, 0)),
        ],
        out_shape=[
            jax.ShapeDtypeStruct((total, x_width), jnp.float32),
            jax.ShapeDtypeStruct((total, 1), jnp.float32),
        ],
        scratch_shapes=[pltpu.VMEM((heads, STATE, head_dim), jnp.float32)],
        compiler_params=pltpu.CompilerParams(dimension_semantics=("arbitrary",)),
        interpret=interpret,
    )(
        x_h, b_t, c_g, log_cum, lc_rows, st_rows, carry_scale, end_rows, gain_rows,
        all_ids.reshape(total, 1), ids.reshape(nblk, 1, BLOCK), skip_h,
    )


def attend_rows(q_row, kv_win, ids_q, ids_k, interpret=False):
    tok_rows, q_width = q_row.shape
    window = kv_win.shape[0]
    kv_heads = kv_win.shape[1] // (2 * HEAD_A)
    group = q_width // HEAD_A // kv_heads
    lead = window - tok_rows
    pair = 4 if kv_heads % 4 == 0 else 1
    inv_sqrt = 1.0 / math.sqrt(HEAD_A)

    def kernel(q_ref, k_ref, v_ref, iq_ref, ik_ref, o_ref):
        q_at = lead + lax.broadcasted_iota(jnp.int32, (tok_rows, window), 0)
        k_at = lax.broadcasted_iota(jnp.int32, (tok_rows, window), 1)
        allowed = (iq_ref[...] == ik_ref[...]) & (q_at >= k_at)
        for g in range(pair * group):
            kv_cols = slice((g // group) * HEAD_A, (g // group + 1) * HEAD_A)
            kb = k_ref[:, kv_cols]
            vb = v_ref[:, kv_cols]
            cols = slice(g * HEAD_A, (g + 1) * HEAD_A)
            logits = lax.dot_general(
                q_ref[:, cols], kb, (((1,), (1,)), ((), ())), preferred_element_type=jnp.float32
            ) * inv_sqrt
            logits = jnp.where(allowed, logits, -jnp.inf)
            row_max = jnp.max(logits, axis=1, keepdims=True)
            exp_terms = jnp.exp(logits - row_max)
            probs = (exp_terms / jnp.sum(exp_terms, axis=1, keepdims=True)).astype(jnp.bfloat16)
            o_ref[:, cols] = jnp.dot(probs, vb, preferred_element_type=jnp.float32).astype(o_ref.dtype)

    return pl.pallas_call(
        kernel,
        grid=(kv_heads // pair,),
        in_specs=[
            pl.BlockSpec((tok_rows, pair * group * HEAD_A), lambda i: (0, i)),
            pl.BlockSpec((window, pair * HEAD_A), lambda i: (0, i)),
            pl.BlockSpec((window, pair * HEAD_A), lambda i: (0, kv_heads // pair + i)),
            pl.BlockSpec((tok_rows, 1), lambda i: (0, 0)),
            pl.BlockSpec((1, window), lambda i: (0, 0)),
        ],
        out_specs=pl.BlockSpec((tok_rows, pair * group * HEAD_A), lambda i: (0, i)),
        out_shape=jax.ShapeDtypeStruct((tok_rows, q_width), jnp.bfloat16),
        interpret=interpret,
    )(q_row, kv_win, kv_win, ids_q, ids_k)


def body(
    previous,
    fresh,
    dt_raw,
    dt_bias,
    a_log,
    b_in,
    c_in,
    skip_d,
    norm_gain,
    queries,
    keys,
    values,
    doc_ids,
):
    tok_rows, width = fresh.shape
    nctx = lax.axis_size("ctx")
    me = lax.axis_index("ctx")
    total = tok_rows * nctx
    part = width // nctx
    mamba_heads = dt_raw.shape[2]
    heads_dev = mamba_heads // nctx
    head_dim = width // mamba_heads
    kv_heads = keys.shape[2] // HEAD_A
    qpd = part // HEAD_A

    rep = nctx // kv_heads
    bc = jnp.stack(
        [b_in[0].reshape(tok_rows, GROUPS, STATE), c_in[0].reshape(tok_rows, GROUPS, STATE)], axis=2
    )
    bc_h = to_heads(jnp.repeat(bc, rep, axis=1).reshape(tok_rows, nctx * 2 * STATE), nctx)
    b_g, c_g = bc_h[:, :STATE], bc_h[:, STATE:]
    dt_h = to_heads(dt_raw[0], nctx)

    handed = shifted(previous[0], "section", 1)
    stream = jnp.where(lax.axis_index("section") == 0, fresh, handed)
    x_h = to_heads(stream, nctx)

    halo = -(-MOST_DOC // tok_rows)
    kv_row = jnp.concatenate([keys[0], values[0]], axis=1)
    kv_win = jnp.concatenate([shifted(kv_row, "ctx", by) for by in range(halo, 0, -1)] + [kv_row], axis=0)
    kv_win, x_h = lax.optimization_barrier((kv_win, x_h))
    all_ids = doc_ids[0]
    lead = halo * tok_rows
    padded_ids = jnp.concatenate([jnp.full((lead,), -1, all_ids.dtype), all_ids])
    ids_k = lax.dynamic_slice_in_dim(padded_ids, me * tok_rows, lead + tok_rows)
    ids_q = lax.dynamic_slice_in_dim(all_ids, me * tok_rows, tok_rows)

    bias_h = lax.dynamic_slice_in_dim(dt_bias[0], me * heads_dev, heads_dev)
    alog_h = lax.dynamic_slice_in_dim(a_log[0], me * heads_dev, heads_dev)
    skip_h = lax.dynamic_slice_in_dim(skip_d[0], me * heads_dev, heads_dev)
    gain_h = lax.dynamic_slice_in_dim(norm_gain[0], me * part, part)

    mixer_out, sq_part = mixer_heads(x_h, dt_h, bias_h, alog_h, b_g, c_g, skip_h, all_ids)
    attended = attend_rows(queries[0], kv_win, ids_q.reshape(tok_rows, 1), ids_k.reshape(1, lead + tok_rows))
    sq_all = lax.all_to_all(
        jnp.broadcast_to(sq_part[:, 0][None], (nctx, total)), "ctx", split_axis=0, concat_axis=0, tiled=True
    )
    mean_sq = (jnp.sum(sq_all, axis=0) / width)[:, None]
    inv_rms = lax.rsqrt(mean_sq + norm_eps)
    mixed = (
        x_h.astype(jnp.float32) + mixer_out * inv_rms * gain_h.astype(jnp.float32)[None, :]
    ).astype(jnp.bfloat16)
    mixed_rows = to_rows(mixed, nctx)
    return (mixed_rows.astype(jnp.float32) + attended.astype(jnp.float32)).astype(jnp.bfloat16)[None]


def solution(mesh):
    in_specs = (
        P("section", "ctx", None),
        P("ctx", None),
        P("section", "ctx", None),
        P("section", None),
        P("section", None),
        P("section", "ctx", None),
        P("section", "ctx", None),
        P("section", None),
        P("section", None),
        P("section", "ctx", None),
        P("section", "ctx", None),
        P("section", "ctx", None),
        P("section", None),
    )
    out_specs = P("section", "ctx", None)
    return jax.shard_map(body, mesh=mesh, in_specs=in_specs, out_specs=out_specs, check_vma=False)
```

```python
import math

import jax
import jax.numpy as jnp
from jax import lax
from jax.experimental import pallas as pl
from jax.experimental.pallas import tpu as pltpu
from jax.sharding import PartitionSpec as P

HEAD_A = 128
STATE = 128
GROUPS = 8
BLOCK = 128
MOST_DOC = 512
Q_BLOCK = 256


norm_eps = 1e-05


def shifted(value, axis, by):
    peers = lax.axis_size(axis)
    pairs = [(i, i + by) for i in range(peers) if 0 <= i + by < peers]
    return lax.ppermute(value, axis, pairs)


def to_heads(row, chunks):
    tok_rows = row.shape[0]
    width = row.shape[1] // chunks
    lead = row.reshape(tok_rows, chunks, width).transpose(1, 0, 2)
    moved = lax.all_to_all(lead, "ctx", split_axis=0, concat_axis=0, tiled=True)
    return moved.reshape(tok_rows * chunks, width)


def to_rows(block, chunks):
    total, width = block.shape
    tok_rows = total // chunks
    moved = lax.all_to_all(block.reshape(chunks, tok_rows, width), "ctx", split_axis=0, concat_axis=0, tiled=True)
    return moved.transpose(1, 0, 2).reshape(tok_rows, chunks * width)


def mixer_heads(x_h, dt_h, bias_h, alog_h, b_g, c_g, skip_h, all_ids, interpret=False):
    total, x_width = x_h.shape
    heads = dt_h.shape[1]
    head_dim = x_width // heads
    nblk = total // BLOCK
    step = jax.nn.softplus(dt_h + bias_h[None, :])
    log_rate = -step * jnp.exp(alog_h)[None, :]
    log_cum = log_rate.reshape(nblk, BLOCK, heads)
    reach = 1
    while reach < BLOCK:
        log_cum = log_cum + jnp.pad(log_cum[:, :-reach], ((0, 0), (reach, 0), (0, 0)))
        reach *= 2
    st = step.reshape(nblk, BLOCK, heads)
    ids = all_ids.reshape(nblk, BLOCK)
    last_id = ids[:, -1]
    prev_last = jnp.concatenate([jnp.full((1,), -1, ids.dtype), last_id[:-1]])
    edge_valid = (ids == prev_last[:, None]).astype(jnp.float32)
    carry_scale = jnp.exp(log_cum) * edge_valid[:, :, None]
    end_scale = (
        jnp.exp(log_cum[:, -1:, :] - log_cum) * st * (ids == last_id[:, None]).astype(jnp.float32)[:, :, None]
    )
    edge_match = (ids[:, 0] == prev_last).astype(jnp.float32)
    block_gain = jnp.exp(log_cum[:, -1, :]) * (ids[:, 0] == last_id).astype(jnp.float32)[:, None]
    block_gain = block_gain * edge_match[:, None]
    gain_rows = jnp.broadcast_to(block_gain[:, :, None], (nblk, heads, head_dim))
    lc_rows = log_cum.transpose(0, 2, 1)
    end_rows = end_scale.transpose(0, 2, 1)
    b_t = b_g.T
    st_rows = st.transpose(0, 2, 1)

    def kernel(x_ref, b_ref, c_ref, lcc_ref, lcr_ref, str_ref, csc_ref, esc_ref, gain_ref,
               idc_ref, idr_ref, skip_ref, o_ref, sq_ref, carry_ref):
        @pl.when(pl.program_id(0) == 0)
        def _():
            carry_ref[...] = jnp.zeros(carry_ref.shape, carry_ref.dtype)

        b_t_blk = b_ref[...]
        c_blk = c_ref[...]
        inner_cb = jnp.dot(c_blk, b_t_blk, preferred_element_type=jnp.float32)
        rows_at = lax.broadcasted_iota(jnp.int32, (BLOCK, BLOCK), 0)
        cols_at = lax.broadcasted_iota(jnp.int32, (BLOCK, BLOCK), 1)
        same_doc = (idc_ref[...] == idr_ref[0]) & (rows_at >= cols_at)
        b_t_f32 = b_t_blk.astype(jnp.float32)
        sq = jnp.zeros((BLOCK, head_dim), jnp.float32)
        for h in range(heads):
            cols = slice(h * head_dim, (h + 1) * head_dim)
            lc_c = lcc_ref[0, h]
            lc_r = lcr_ref[0, h:h + 1, :]
            decay = jnp.where(same_doc, jnp.exp(lc_c - lc_r), 0.0)
            intra_w = (decay * inner_cb * str_ref[0, h:h + 1, :]).astype(jnp.bfloat16)
            xh = x_ref[:, cols]
            local = jnp.dot(intra_w, xh, preferred_element_type=jnp.float32)
            state_bf = carry_ref[h].astype(jnp.bfloat16)
            carried = jnp.dot(c_blk, state_bf, preferred_element_type=jnp.float32)
            carried = carried * csc_ref[0, :, h:h + 1]
            out = local + carried + skip_ref[h] * xh.astype(jnp.float32)
            o_ref[:, cols] = out
            sq = sq + out * out
            end_w_t = (esc_ref[0, h:h + 1, :] * b_t_f32).astype(jnp.bfloat16)
            block_state = jnp.dot(end_w_t, xh, preferred_element_type=jnp.float32)
            carry_ref[h] = gain_ref[0, h:h + 1, :] * carry_ref[h] + block_state
        sq_ref[...] = jnp.sum(sq, axis=1, keepdims=True)

    per_block = lambda shape: pl.BlockSpec((1,) + shape, lambda i: (i, 0, 0))
    return pl.pallas_call(
        kernel,
        grid=(nblk,),
        in_specs=[
            pl.BlockSpec((BLOCK, x_width), lambda i: (i, 0)),
            pl.BlockSpec((STATE, BLOCK), lambda i: (0, i)),
            pl.BlockSpec((BLOCK, STATE), lambda i: (i, 0)),
            pl.BlockSpec((1, heads, BLOCK, BLOCK), lambda i: (i, 0, 0, 0)),
            per_block((heads, BLOCK)),
            per_block((heads, BLOCK)),
            per_block((BLOCK, heads)),
            per_block((heads, BLOCK)),
            per_block((heads, head_dim)),
            pl.BlockSpec((BLOCK, 1), lambda i: (i, 0)),
            per_block((1, BLOCK)),
            pl.BlockSpec(memory_space=pltpu.SMEM),
        ],
        out_specs=[
            pl.BlockSpec((BLOCK, x_width), lambda i: (i, 0)),
            pl.BlockSpec((BLOCK, 1), lambda i: (i, 0)),
        ],
        out_shape=[
            jax.ShapeDtypeStruct((total, x_width), jnp.float32),
            jax.ShapeDtypeStruct((total, 1), jnp.float32),
        ],
        scratch_shapes=[pltpu.VMEM((heads, STATE, head_dim), jnp.float32)],
        compiler_params=pltpu.CompilerParams(dimension_semantics=("arbitrary",)),
        interpret=interpret,
    )(
        x_h, b_t, c_g, jnp.broadcast_to(lc_rows[:, :, :, None], (nblk, heads, BLOCK, BLOCK)), lc_rows, st_rows, carry_scale, end_rows, gain_rows,
        all_ids.reshape(total, 1), ids.reshape(nblk, 1, BLOCK), skip_h,
    )


def attend_rows(q_row, kv_win, ids_q, ids_k, interpret=False):
    tok_rows, q_width = q_row.shape
    window = kv_win.shape[0]
    kv_heads = kv_win.shape[1] // (2 * HEAD_A)
    group = q_width // HEAD_A // kv_heads
    lead = window - tok_rows
    pair = 2 if kv_heads % 2 == 0 else 1
    inv_sqrt = 1.0 / math.sqrt(HEAD_A)

    def kernel(q_ref, k_ref, v_ref, iq_ref, ik_ref, o_ref):
        q_at = lead + lax.broadcasted_iota(jnp.int32, (tok_rows, window), 0)
        k_at = lax.broadcasted_iota(jnp.int32, (tok_rows, window), 1)
        allowed = (iq_ref[...] == ik_ref[...]) & (q_at >= k_at)
        for g in range(pair * group):
            kv_cols = slice((g // group) * HEAD_A, (g // group + 1) * HEAD_A)
            kb = k_ref[:, kv_cols]
            vb = v_ref[:, kv_cols]
            cols = slice(g * HEAD_A, (g + 1) * HEAD_A)
            logits = lax.dot_general(
                q_ref[:, cols], kb, (((1,), (1,)), ((), ())), preferred_element_type=jnp.float32
            ) * inv_sqrt
            logits = jnp.where(allowed, logits, -jnp.inf)
            row_max = jnp.max(logits, axis=1, keepdims=True)
            exp_terms = jnp.exp(logits - row_max)
            probs = (exp_terms / jnp.sum(exp_terms, axis=1, keepdims=True)).astype(jnp.bfloat16)
            o_ref[:, cols] = jnp.dot(probs, vb, preferred_element_type=jnp.float32).astype(o_ref.dtype)

    return pl.pallas_call(
        kernel,
        grid=(kv_heads // pair,),
        in_specs=[
            pl.BlockSpec((tok_rows, pair * group * HEAD_A), lambda i: (0, i)),
            pl.BlockSpec((window, pair * HEAD_A), lambda i: (0, i)),
            pl.BlockSpec((window, pair * HEAD_A), lambda i: (0, kv_heads // pair + i)),
            pl.BlockSpec((tok_rows, 1), lambda i: (0, 0)),
            pl.BlockSpec((1, window), lambda i: (0, 0)),
        ],
        out_specs=pl.BlockSpec((tok_rows, pair * group * HEAD_A), lambda i: (0, i)),
        out_shape=jax.ShapeDtypeStruct((tok_rows, q_width), jnp.bfloat16),
        interpret=interpret,
    )(q_row, kv_win, kv_win, ids_q, ids_k)


def body(
    previous,
    fresh,
    dt_raw,
    dt_bias,
    a_log,
    b_in,
    c_in,
    skip_d,
    norm_gain,
    queries,
    keys,
    values,
    doc_ids,
):
    tok_rows, width = fresh.shape
    nctx = lax.axis_size("ctx")
    me = lax.axis_index("ctx")
    total = tok_rows * nctx
    part = width // nctx
    mamba_heads = dt_raw.shape[2]
    heads_dev = mamba_heads // nctx
    head_dim = width // mamba_heads
    kv_heads = keys.shape[2] // HEAD_A
    qpd = part // HEAD_A

    rep = nctx // kv_heads
    bc = jnp.stack(
        [b_in[0].reshape(tok_rows, GROUPS, STATE), c_in[0].reshape(tok_rows, GROUPS, STATE)], axis=2
    )
    bc_h = to_heads(jnp.repeat(bc, rep, axis=1).reshape(tok_rows, nctx * 2 * STATE), nctx)
    b_g, c_g = bc_h[:, :STATE], bc_h[:, STATE:]
    dt_h = to_heads(dt_raw[0], nctx)

    handed = shifted(previous[0], "section", 1)
    stream = jnp.where(lax.axis_index("section") == 0, fresh, handed)
    x_h = to_heads(stream, nctx)

    halo = -(-MOST_DOC // tok_rows)
    kv_row = jnp.concatenate([keys[0], values[0]], axis=1)
    kv_win = jnp.concatenate([shifted(kv_row, "ctx", by) for by in range(halo, 0, -1)] + [kv_row], axis=0)
    kv_win, x_h = lax.optimization_barrier((kv_win, x_h))
    all_ids = doc_ids[0]
    lead = halo * tok_rows
    padded_ids = jnp.concatenate([jnp.full((lead,), -1, all_ids.dtype), all_ids])
    ids_k = lax.dynamic_slice_in_dim(padded_ids, me * tok_rows, lead + tok_rows)
    ids_q = lax.dynamic_slice_in_dim(all_ids, me * tok_rows, tok_rows)

    bias_h = lax.dynamic_slice_in_dim(dt_bias[0], me * heads_dev, heads_dev)
    alog_h = lax.dynamic_slice_in_dim(a_log[0], me * heads_dev, heads_dev)
    skip_h = lax.dynamic_slice_in_dim(skip_d[0], me * heads_dev, heads_dev)
    gain_h = lax.dynamic_slice_in_dim(norm_gain[0], me * part, part)

    mixer_out, sq_part = mixer_heads(x_h, dt_h, bias_h, alog_h, b_g, c_g, skip_h, all_ids)
    attended = attend_rows(queries[0], kv_win, ids_q.reshape(tok_rows, 1), ids_k.reshape(1, lead + tok_rows))
    sq_all = lax.all_to_all(
        jnp.broadcast_to(sq_part[:, 0][None], (nctx, total)), "ctx", split_axis=0, concat_axis=0, tiled=True
    )
    mean_sq = (jnp.sum(sq_all, axis=0) / width)[:, None]
    inv_rms = lax.rsqrt(mean_sq + norm_eps)
    mixed = (
        x_h.astype(jnp.float32) + mixer_out * inv_rms * gain_h.astype(jnp.float32)[None, :]
    ).astype(jnp.bfloat16)
    mixed_rows = to_rows(mixed, nctx)
    return (mixed_rows.astype(jnp.float32) + attended.astype(jnp.float32)).astype(jnp.bfloat16)[None]


def solution(mesh):
    in_specs = (
        P("section", "ctx", None),
        P("ctx", None),
        P("section", "ctx", None),
        P("section", None),
        P("section", None),
        P("section", "ctx", None),
        P("section", "ctx", None),
        P("section", None),
        P("section", None),
        P("section", "ctx", None),
        P("section", "ctx", None),
        P("section", "ctx", None),
        P("section", None),
    )
    out_specs = P("section", "ctx", None)
    return jax.shard_map(body, mesh=mesh, in_specs=in_specs, out_specs=out_specs, check_vma=False)
```
